32 devices in a mesh: groups: 2 (over x), seq: 16 (over z, y, core).
Axes of the slice: x: 2, y: 2, z: 4, core: 2. Of those that a mesh axis runs over, the one named last changes fastest.
Arguments:
- query: bfloat16 [4096, 2048], P(('groups', 'seq')), parts along dimension 0, may hold values from -8 to 8
- keys: bfloat16 [4096, 2048], P(('groups', 'seq')), parts along dimension 0, may hold values from -8 to 8
- values: bfloat16 [4096, 2048], P(('groups', 'seq')), parts along dimension 0, may hold values from -6 to 6
- grad_out: bfloat16 [4096, 2048], P(('groups', 'seq')), parts along dimension 0, may hold values from -6 to 6
- global_blocks: int32 [4], P('groups'), parts along dimension 0, may hold values from 0 to 15
- random_blocks: int32 [32, 3], P('groups'), parts along dimension 0, may hold values from 0 to 15
Outputs:
- attended: bfloat16 [4096, 2048], P(('groups', 'seq')), parts along dimension 0
- grad_query: bfloat16 [4096, 2048], P(('groups', 'seq')), parts along dimension 0
- grad_keys: bfloat16 [4096, 2048], P(('groups', 'seq')), parts along dimension 0
- grad_values: bfloat16 [4096, 2048], P(('groups', 'seq')), parts along dimension 0
The draws below stay inside these ranges and needn't reach their ends.
There are 2 independent parts, one for each index of `groups`. The reference program is written for one: setup_inputs(seed, part) draws one part's arguments, and reference() takes and returns one part's arrays. A program takes and returns all parts, laid end to end along the dimension named above; each array names one. Nothing has to cross between parts.
All inputs are finite; a program needn't handle non-finite values.
Results may differ from the reference program's by a relative error of at most 0.022.
Values may be sent and summed in bfloat16 or wider, within the bound.
No kernel may reach another device: no remote copies, remote signals or barrier semaphores. Data moves between devices by JAX's collectives and lax.ppermute only.
A program may use at most 192 MiB of HBM per device.

```python
import math
import jax
import jax.numpy as jnp
import numpy as np
from jax import lax

H = 16
HD = 128
BLK = 128
G = 2
R = 3
NB = 16
TOKENS = 2048
C = 2048


def paired(key):
    width = H * HD
    first = jax.random.normal(jax.random.fold_in(key, 101), (TOKENS, width), jnp.float32)
    second = jax.random.normal(jax.random.fold_in(key, 202), (TOKENS, width), jnp.float32)
    return (jnp.clip(first, -6.0, 6.0), jnp.clip(second, -6.0, 6.0))


def draw_query(key, part):
    return paired(key)[0].astype(jnp.bfloat16)


def draw_keys(key, part):
    return paired(key)[1].astype(jnp.bfloat16)


def with_ends(entries, key, low, high):
    spot = [jax.random.randint(jax.random.fold_in(key, axis), (), 0, length) for axis, length in enumerate(entries.shape)]
    longest = entries.shape.index(max(entries.shape))
    neighbour = spot[:longest] + [(spot[longest] + 1) % entries.shape[longest]] + spot[longest + 1:]
    return entries.at[tuple(spot)].set(low).at[tuple(neighbour)].set(high)


def block_scale(stream_key, shape, cuts, smallest, largest):
    loudness, own = 1.0, jax.random.fold_in(stream_key, 6)
    for axis_at, blocks in cuts:
        steps = jnp.exp(jax.random.uniform(jax.random.fold_in(own, axis_at), (blocks,), jnp.float32, smallest / len(cuts), largest / len(cuts)))
        loudness = loudness * jnp.repeat(steps, shape[axis_at] // blocks).reshape([-1 if axis == axis_at else 1 for axis in range(len(shape))])
    return loudness


def rank_bounds(count, lean):
    portions = [(1 << 20) // math.isqrt(grade ** lean) + 1 for grade in range(1, count + 1)]
    spread = 1 + sum(portions) // (1 << 30)
    return np.cumsum(np.array([max(1, weight // spread) for weight in portions]))


def ranked_ids(own_key, shape, count, slope):
    grid = rank_bounds(count, slope)
    pick = jax.random.randint(jax.random.fold_in(own_key, 1), shape, 0, int(grid[count - 1]))
    standing = jnp.searchsorted(jnp.asarray(grid, jnp.int32), pick, side="right")
    return jax.random.permutation(jax.random.fold_in(own_key, 2), count)[standing].astype(jnp.int32)


def bell_draw(rng, dims, deviation, most, cuts=(), kind=jnp.bfloat16):
    result = jax.random.normal(rng, dims, jnp.float32) * deviation
    if len(cuts) > 0:
        result = block_scale(rng, dims, cuts, -0.22, 0.18) * result
    return jnp.clip(result, min=-most, max=most).astype(kind)


def setup_inputs(seed: int = 0, part: int = 0) -> dict:
    splits = jax.random.split(jax.random.key(seed), 7)
    part_splits = jax.random.split(jax.random.fold_in(splits[6], part), 7)
    query = draw_query(jax.random.fold_in(jax.random.fold_in(splits[6], part), 71), part)
    keys = draw_keys(jax.random.fold_in(jax.random.fold_in(splits[6], part), 71), part)
    values = bell_draw(part_splits[2], (TOKENS, C), 1.0, 6.0, ((0, 16),))
    grad_out = bell_draw(part_splits[3], (TOKENS, C), 1.0, 6.0, ((0, 16),))
    global_blocks = jax.random.randint(part_splits[4], (G,), 0, NB).astype(jnp.int32)
    random_blocks = with_ends(ranked_ids(part_splits[5], (NB, R), NB, 1), jax.random.fold_in(part_splits[5], 3), 0, NB - 1).astype(jnp.int32)
    return dict(query=query, keys=keys, values=values, grad_out=grad_out, global_blocks=global_blocks, random_blocks=random_blocks)


def attend_block(query_blk, grad_blk, key_tiles, value_tiles):
    row_count = query_blk.shape[0]
    keys_total = key_tiles.shape[0]
    scaling = HD ** -0.5
    query_heads = query_blk.astype(jnp.float32).reshape(row_count, H, HD)
    key_heads = key_tiles.astype(jnp.float32).reshape(keys_total, H, HD)
    value_heads = value_tiles.astype(jnp.float32).reshape(keys_total, H, HD)
    grad_heads = grad_blk.astype(jnp.float32).reshape(row_count, H, HD)
    scores = jnp.einsum("qhd,khd->hqk", query_heads, key_heads) * scaling
    probability = jax.nn.softmax(scores, axis=-1)
    weights = probability.astype(jnp.bfloat16)
    weights_wide = weights.astype(jnp.float32)
    attended = jnp.einsum("hqk,khd->qhd", weights_wide, value_heads).astype(jnp.bfloat16)
    deltas = jnp.sum(grad_heads * attended.astype(jnp.float32), axis=-1)
    grad_prob = jnp.einsum("qhd,khd->hqk", grad_heads, value_heads)
    grad_score = (probability * (grad_prob - jnp.transpose(deltas)[:, :, None])).astype(jnp.bfloat16)
    score_wide = grad_score.astype(jnp.float32)
    grad_query = (jnp.einsum("hqk,khd->qhd", score_wide, key_heads) * scaling).astype(jnp.bfloat16)
    grad_keys = jnp.einsum("hqk,qhd->khd", score_wide, query_heads) * scaling
    grad_values = jnp.einsum("hqk,qhd->khd", weights_wide, grad_heads)
    width = H * HD
    return (attended.reshape(row_count, width), grad_query.reshape(row_count, width),
            grad_keys.reshape(keys_total, width), grad_values.reshape(keys_total, width))


def reference(query, keys, values, grad_out, global_blocks, random_blocks):
    width = H * HD
    total_blocks = TOKENS // BLK
    query_blocks = query.reshape(total_blocks, BLK, width)
    key_blocks = keys.reshape(total_blocks, BLK, width)
    value_blocks = values.reshape(total_blocks, BLK, width)
    grad_blocks = grad_out.reshape(total_blocks, BLK, width)

    def visit(carry, block):
        acc_keys, acc_values = carry
        window = jnp.stack([block, (block - 1) % total_blocks, (block + 1) % total_blocks]).astype(jnp.int32)
        listed = jnp.concatenate([window, global_blocks.astype(jnp.int32), random_blocks[block].astype(jnp.int32)])
        tile_keys = key_blocks[listed].reshape(-1, width)
        tile_values = value_blocks[listed].reshape(-1, width)
        attended, grad_query, part_keys, part_values = attend_block(query_blocks[block], grad_blocks[block], tile_keys, tile_values)
        acc_keys = acc_keys.at[listed].add(part_keys.reshape(-1, BLK, width))
        acc_values = acc_values.at[listed].add(part_values.reshape(-1, BLK, width))
        return (acc_keys, acc_values), (attended, grad_query)

    zeros = jnp.zeros((total_blocks, BLK, width), jnp.float32)
    (acc_keys, acc_values), (attended, grad_query) = lax.scan(visit, (zeros, zeros), jnp.arange(total_blocks, dtype=jnp.int32))
    return (attended.reshape(TOKENS, width), grad_query.reshape(TOKENS, width),
            acc_keys.astype(jnp.bfloat16).reshape(TOKENS, width), acc_values.astype(jnp.bfloat16).reshape(TOKENS, width))
```

```python
import jax
import jax.numpy as jnp
from jax import lax
from jax.experimental import pallas as pl
from jax.experimental.pallas import tpu as pltpu
from jax.sharding import PartitionSpec as P

HD = 128
BLK = 128
G = 2


def attend_block(operands):
    query_blk, grad_blk, key_tiles, value_tiles = operands
    row_count, width = query_blk.shape
    keys_total = key_tiles.shape[0]
    head_size = HD
    head_count = width // head_size
    scaling = HD ** (-0.5)
    last_dims = (((1,), (1,)), ((), ()))
    first_dims = (((0,), (0,)), ((), ()))

    def one_head(head, carry):
        out_attended, out_gquery, out_gkeys, out_gvalues = carry
        start = head * head_size
        query_head = lax.dynamic_slice_in_dim(query_blk, start, head_size, 1)
        grad_head = lax.dynamic_slice_in_dim(grad_blk, start, head_size, 1)
        key_head = lax.dynamic_slice_in_dim(key_tiles, start, head_size, 1)
        value_head = lax.dynamic_slice_in_dim(value_tiles, start, head_size, 1)
        scores = (
            lax.dot_general(query_head, key_head, last_dims, preferred_element_type=jnp.float32)
            * scaling
        )
        probability = jax.nn.softmax(scores, axis=-1)
        weights = probability.astype(jnp.bfloat16)
        attended_head = jnp.dot(weights, value_head, preferred_element_type=jnp.float32).astype(
            jnp.bfloat16
        )
        deltas = jnp.sum(grad_head.astype(jnp.float32) * attended_head.astype(jnp.float32), axis=-1)
        grad_prob = lax.dot_general(
            grad_head, value_head, last_dims, preferred_element_type=jnp.float32
        )
        grad_score = (probability * (grad_prob - deltas[:, None])).astype(jnp.bfloat16)
        gquery_head = (
            jnp.dot(grad_score, key_head, preferred_element_type=jnp.float32) * scaling
        ).astype(jnp.bfloat16)
        gkeys_head = (
            lax.dot_general(grad_score, query_head, first_dims, preferred_element_type=jnp.float32)
            * scaling
        )
        gvalues_head = lax.dot_general(
            weights, grad_head, first_dims, preferred_element_type=jnp.float32
        )
        out_attended = lax.dynamic_update_slice_in_dim(out_attended, attended_head, start, 1)
        out_gquery = lax.dynamic_update_slice_in_dim(out_gquery, gquery_head, start, 1)
        out_gkeys = lax.dynamic_update_slice_in_dim(out_gkeys, gkeys_head, start, 1)
        out_gvalues = lax.dynamic_update_slice_in_dim(out_gvalues, gvalues_head, start, 1)
        return (out_attended, out_gquery, out_gkeys, out_gvalues)

    initial = (
        jnp.zeros((row_count, width), jnp.bfloat16),
        jnp.zeros((row_count, width), jnp.bfloat16),
        jnp.zeros((keys_total, width), jnp.float32),
        jnp.zeros((keys_total, width), jnp.float32),
    )
    return lax.fori_loop(0, head_count, one_head, initial)


def fetch_table(device_ids, block_count, total_blocks, global_blocks, random_blocks):
    owned_blocks = (
        device_ids[:, None] * block_count + jnp.arange(block_count, dtype=jnp.int32)[None, :]
    )
    pieces = []
    pieces.append(((owned_blocks - 1) % total_blocks)[:, :, None])
    pieces.append(((owned_blocks + 1) % total_blocks)[:, :, None])
    pieces.append(
        jnp.broadcast_to(
            global_blocks[None, None, :], owned_blocks.shape + (global_blocks.shape[0],)
        )
    )
    pieces.append(random_blocks[owned_blocks])
    return jnp.concatenate(pieces, axis=2).reshape(device_ids.shape[0], -1)


def shards_exchange(query, keys, values, grad_out, global_blocks, random_blocks):
    devices = lax.axis_size("seq")
    tok_rows, width = query.shape
    per_device = tok_rows // BLK
    total_blocks = per_device * devices
    row_share = BLK // devices
    key_blocks = keys.reshape(per_device, BLK, width)
    value_blocks = values.reshape(per_device, BLK, width)
    row_keys, row_values = (
        lax.all_to_all(
            keys.reshape(per_device, devices, row_share, width),
            "seq",
            split_axis=1,
            concat_axis=0,
            tiled=True,
        ),
        lax.all_to_all(
            values.reshape(per_device, devices, row_share, width),
            "seq",
            split_axis=1,
            concat_axis=0,
            tiled=True,
        ),
    )
    row_keys = row_keys.reshape(total_blocks, row_share, width)
    row_values = row_values.reshape(total_blocks, row_share, width)
    fetch_lists = fetch_table(
        jnp.arange(devices, dtype=jnp.int32), per_device, total_blocks, global_blocks, random_blocks
    )
    fetched = fetch_lists.shape[1]
    got_keys, got_values = (
        lax.all_to_all(row_keys[fetch_lists], "seq", split_axis=0, concat_axis=2, tiled=True),
        lax.all_to_all(row_values[fetch_lists], "seq", split_axis=0, concat_axis=2, tiled=True),
    )
    offset = 0
    window_keys = got_keys[:, 0:2]
    window_values = got_values[:, 0:2]
    offset = 2
    global_keys = got_keys[:, offset : offset + G]
    global_values = got_values[:, offset : offset + G]
    offset = offset + G
    random_keys = got_keys[:, offset:]
    random_values = got_values[:, offset:]
    tile_keys = jnp.concatenate(
        [key_blocks[:, None], window_keys, global_keys, random_keys], axis=1
    ).reshape(per_device, -1, width)
    tile_values = jnp.concatenate(
        [value_blocks[:, None], window_values, global_values, random_values], axis=1
    ).reshape(per_device, -1, width)
    attended, grad_query, tile_gkeys, tile_gvalues = lax.map(
        attend_block,
        (
            query.reshape(per_device, BLK, width),
            grad_out.reshape(per_device, BLK, width),
            tile_keys,
            tile_values,
        ),
    )
    tile_gkeys = tile_gkeys.reshape(per_device, -1, BLK, width)
    tile_gvalues = tile_gvalues.reshape(per_device, -1, BLK, width)
    window_gkeys = tile_gkeys[:, 1:3]
    window_gvalues = tile_gvalues[:, 1:3]
    global_gkeys = tile_gkeys[:, 3 : 3 + G]
    global_gvalues = tile_gvalues[:, 3 : 3 + G]
    back_keys = []
    back_values = []
    back_keys.append(window_gkeys)
    back_values.append(window_gvalues)
    back_keys.append(global_gkeys)
    back_values.append(global_gvalues)
    back_keys.append(tile_gkeys[:, 3 + G :])
    back_values.append(tile_gvalues[:, 3 + G :])
    back_keys = jnp.concatenate(back_keys, axis=1).reshape(1, fetched, devices, row_share, width)
    back_values = jnp.concatenate(back_values, axis=1).reshape(
        1, fetched, devices, row_share, width
    )
    recv_keys, recv_values = (
        lax.all_to_all(back_keys, "seq", split_axis=2, concat_axis=0, tiled=True),
        lax.all_to_all(back_values, "seq", split_axis=2, concat_axis=0, tiled=True),
    )
    flat_index = fetch_lists.reshape(-1)
    table_keys = (
        jnp.zeros((total_blocks, row_share, width), jnp.float32)
        .at[flat_index]
        .add(recv_keys.reshape(devices * fetched, row_share, width))
    )
    table_values = (
        jnp.zeros((total_blocks, row_share, width), jnp.float32)
        .at[flat_index]
        .add(recv_values.reshape(devices * fetched, row_share, width))
    )
    home_keys, home_values = (
        lax.all_to_all(
            table_keys.reshape(total_blocks, 1, row_share, width),
            "seq",
            split_axis=0,
            concat_axis=1,
            tiled=True,
        ),
        lax.all_to_all(
            table_values.reshape(total_blocks, 1, row_share, width),
            "seq",
            split_axis=0,
            concat_axis=1,
            tiled=True,
        ),
    )
    grad_key_blocks = tile_gkeys[:, 0] + home_keys.reshape(per_device, BLK, width)
    grad_value_blocks = tile_gvalues[:, 0] + home_values.reshape(per_device, BLK, width)
    return (
        attended.reshape(tok_rows, width),
        grad_query.reshape(tok_rows, width),
        grad_key_blocks.astype(jnp.bfloat16).reshape(tok_rows, width),
        grad_value_blocks.astype(jnp.bfloat16).reshape(tok_rows, width),
    )

SLOTS = 3 + G + 3


def _send(v, pairs):
    return lax.ppermute(v.astype(jnp.bfloat16), "seq", pairs).astype(v.dtype)


def gather_blocks(x, n):
    line_len = n // 4
    z = lax.axis_index("seq") // 4
    ups, downs = [], []
    up, down = x, x
    for k in range(1, line_len):
        up = _send(
            up, [(4 * z0 + r, 4 * (z0 + 1) + r) for z0 in range(k - 1, line_len - 1) for r in range(4)]
        )
        down = _send(
            down, [(4 * z0 + r, 4 * (z0 - 1) + r) for z0 in range(1, line_len - k + 1) for r in range(4)]
        )
        ups.append(up)
        downs.append(down)
    rel = jnp.stack(ups[::-1] + [x] + downs)
    line = lax.dynamic_slice_in_dim(rel, line_len - 1 - z, line_len, axis=0)
    other = _send(line, [(i, i ^ 2) for i in range(n)])
    pair = jnp.stack([line, other])
    sibling = _send(pair, [(i, i ^ 1) for i in range(n)])
    return jnp.stack([pair, sibling])


def _attend_kernel(pos_ref, q_ref, g_ref, *refs):
    k_refs = refs[:SLOTS]
    v_refs = refs[SLOTS : 2 * SLOTS]
    att_ref, gq_ref, dk_ref, dv_ref = refs[2 * SLOTS :]
    scale = HD ** (-0.5)
    nt = (((1,), (1,)), ((), ()))
    q = q_ref[...]
    g = g_ref[...]
    k_all = jnp.concatenate([r[...] for r in k_refs], axis=0)
    v_all = jnp.concatenate([r[...] for r in v_refs], axis=0)
    s = lax.dot_general(q, k_all, nt, preferred_element_type=jnp.float32) * scale
    e = jnp.exp(s - jnp.max(s, axis=-1, keepdims=True))
    p = e / jnp.sum(e, axis=-1, keepdims=True)
    w = p.astype(jnp.bfloat16)
    att = jnp.dot(w, v_all, preferred_element_type=jnp.float32).astype(jnp.bfloat16)
    att_ref[...] = att
    delta = jnp.sum(g.astype(jnp.float32) * att.astype(jnp.float32), axis=-1, keepdims=True)
    gp = lax.dot_general(g, v_all, nt, preferred_element_type=jnp.float32)
    gs32 = p * (gp - delta)
    gs = gs32.astype(jnp.bfloat16)
    gq_ref[...] = (jnp.dot(gs, k_all, preferred_element_type=jnp.float32) * scale).astype(
        jnp.bfloat16
    )
    gk = jnp.dot(gs32.T.astype(jnp.bfloat16), q, preferred_element_type=jnp.float32) * scale
    gv = jnp.dot(p.T.astype(jnp.bfloat16), g, preferred_element_type=jnp.float32)
    dk_ref[...] = jnp.zeros(dk_ref.shape, jnp.float32)
    dv_ref[...] = jnp.zeros(dv_ref.shape, jnp.float32)
    rows = q.shape[0]
    for j in range(SLOTS):
        at = pos_ref[j]
        dk_ref[at] = dk_ref[at] + gk[j * rows : (j + 1) * rows]
        dv_ref[at] = dv_ref[at] + gv[j * rows : (j + 1) * rows]


def attend_local(pos, query, grad_out, keys_local, values_local):
    rows, width = query.shape
    held = keys_local.shape[0]
    heads = width // HD
    head_spec = pl.BlockSpec((rows, HD), lambda h, pos: (0, h))
    slot_specs = [
        pl.BlockSpec((None, rows, HD), lambda h, pos, j=j: (pos[j], 0, h)) for j in range(SLOTS)
    ]
    part_spec = pl.BlockSpec((held, rows, HD), lambda h, pos: (0, 0, h))
    flops = 12 * rows * SLOTS * rows * HD * heads
    moved = 2 * SLOTS * rows * width * 2 + 4 * rows * width * 2 + 2 * held * rows * width * 4
    call = pl.pallas_call(
        _attend_kernel,
        out_shape=(
            jax.ShapeDtypeStruct((rows, width), jnp.bfloat16),
            jax.ShapeDtypeStruct((rows, width), jnp.bfloat16),
            jax.ShapeDtypeStruct((held, rows, width), jnp.float32),
            jax.ShapeDtypeStruct((held, rows, width), jnp.float32),
        ),
        grid_spec=pltpu.PrefetchScalarGridSpec(
            num_scalar_prefetch=1,
            grid=(heads,),
            in_specs=[head_spec, head_spec] + slot_specs + slot_specs,
            out_specs=(head_spec, head_spec, part_spec, part_spec),
        ),
        compiler_params=pltpu.CompilerParams(dimension_semantics=("arbitrary",)),
        cost_estimate=pl.CostEstimate(
            flops=flops, transcendentals=rows * SLOTS * rows * heads, bytes_accessed=moved
        ),
    )
    return call(
        pos, query, grad_out, *([keys_local] * SLOTS), *([values_local] * SLOTS)
    )


def shards_gather(query, keys, values, grad_out, global_blocks, random_blocks):
    n = lax.axis_size("seq")
    rows, width = query.shape
    line_len = n // 4
    idx = lax.axis_index("seq")
    listed = jnp.concatenate(
        [
            jnp.stack([idx, (idx - 1) % n, (idx + 1) % n]).astype(jnp.int32),
            global_blocks.astype(jnp.int32),
            random_blocks[idx].astype(jnp.int32),
        ]
    )
    listed = jnp.clip(listed, 0, n - 1)
    core = idx % 2
    ypos = (idx // 2) % 2
    pos = (((listed % 2) ^ core) * 2 + (((listed // 2) % 2) ^ ypos)) * line_len + listed // 4
    keys_local = gather_blocks(keys, n).reshape(n, rows, width)
    values_local = gather_blocks(values, n).reshape(n, rows, width)
    attended, grad_query, part_keys, part_values = attend_local(
        pos, query, grad_out, keys_local, values_local
    )
    scatter = jax.linear_transpose(
        lambda t: gather_blocks(t, n), jax.ShapeDtypeStruct((rows, width), jnp.float32)
    )
    (grad_keys,) = scatter(part_keys.reshape(2, 2, line_len, rows, width))
    (grad_values,) = scatter(part_values.reshape(2, 2, line_len, rows, width))
    return (
        attended,
        grad_query,
        grad_keys.astype(jnp.bfloat16),
        grad_values.astype(jnp.bfloat16),
    )


def shards(query, keys, values, grad_out, global_blocks, random_blocks):
    n = lax.axis_size("seq")
    if query.shape[0] == BLK and n % 4 == 0 and n <= 32:
        return shards_gather(query, keys, values, grad_out, global_blocks, random_blocks)
    return shards_exchange(query, keys, values, grad_out, global_blocks, random_blocks)


def solution(mesh):
    placed = (
        P(("groups", "seq"), None),
        P(("groups", "seq"), None),
        P(("groups", "seq"), None),
        P(("groups", "seq"), None),
        P("groups"),
        P("groups", None),
    )
    return jax.shard_map(
        shards,
        mesh=mesh,
        in_specs=placed,
        out_specs=(
            P(("groups", "seq"), None),
            P(("groups", "seq"), None),
            P(("groups", "seq"), None),
            P(("groups", "seq"), None),
        ),
        check_vma=False,
    )
```

```python
import jax
import jax.numpy as jnp
from jax import lax
from jax.experimental import pallas as pl
from jax.experimental.pallas import tpu as pltpu
from jax.sharding import PartitionSpec as P

HD = 128
BLK = 128
G = 2


def attend_block(operands):
    query_blk, grad_blk, key_tiles, value_tiles = operands
    row_count, width = query_blk.shape
    keys_total = key_tiles.shape[0]
    head_size = HD
    head_count = width // head_size
    scaling = HD ** (-0.5)
    last_dims = (((1,), (1,)), ((), ()))
    first_dims = (((0,), (0,)), ((), ()))

    def one_head(head, carry):
        out_attended, out_gquery, out_gkeys, out_gvalues = carry
        start = head * head_size
        query_head = lax.dynamic_slice_in_dim(query_blk, start, head_size, 1)
        grad_head = lax.dynamic_slice_in_dim(grad_blk, start, head_size, 1)
        key_head = lax.dynamic_slice_in_dim(key_tiles, start, head_size, 1)
        value_head = lax.dynamic_slice_in_dim(value_tiles, start, head_size, 1)
        scores = (
            lax.dot_general(query_head, key_head, last_dims, preferred_element_type=jnp.float32)
            * scaling
        )
        probability = jax.nn.softmax(scores, axis=-1)
        weights = probability.astype(jnp.bfloat16)
        attended_head = jnp.dot(weights, value_head, preferred_element_type=jnp.float32).astype(
            jnp.bfloat16
        )
        deltas = jnp.sum(grad_head.astype(jnp.float32) * attended_head.astype(jnp.float32), axis=-1)
        grad_prob = lax.dot_general(
            grad_head, value_head, last_dims, preferred_element_type=jnp.float32
        )
        grad_score = (probability * (grad_prob - deltas[:, None])).astype(jnp.bfloat16)
        gquery_head = (
            jnp.dot(grad_score, key_head, preferred_element_type=jnp.float32) * scaling
        ).astype(jnp.bfloat16)
        gkeys_head = (
            lax.dot_general(grad_score, query_head, first_dims, preferred_element_type=jnp.float32)
            * scaling
        )
        gvalues_head = lax.dot_general(
            weights, grad_head, first_dims, preferred_element_type=jnp.float32
        )
        out_attended = lax.dynamic_update_slice_in_dim(out_attended, attended_head, start, 1)
        out_gquery = lax.dynamic_update_slice_in_dim(out_gquery, gquery_head, start, 1)
        out_gkeys = lax.dynamic_update_slice_in_dim(out_gkeys, gkeys_head, start, 1)
        out_gvalues = lax.dynamic_update_slice_in_dim(out_gvalues, gvalues_head, start, 1)
        return (out_attended, out_gquery, out_gkeys, out_gvalues)

    initial = (
        jnp.zeros((row_count, width), jnp.bfloat16),
        jnp.zeros((row_count, width), jnp.bfloat16),
        jnp.zeros((keys_total, width), jnp.float32),
        jnp.zeros((keys_total, width), jnp.float32),
    )
    return lax.fori_loop(0, head_count, one_head, initial)


def fetch_table(device_ids, block_count, total_blocks, global_blocks, random_blocks):
    owned_blocks = (
        device_ids[:, None] * block_count + jnp.arange(block_count, dtype=jnp.int32)[None, :]
    )
    pieces = []
    pieces.append(((owned_blocks - 1) % total_blocks)[:, :, None])
    pieces.append(((owned_blocks + 1) % total_blocks)[:, :, None])
    pieces.append(
        jnp.broadcast_to(
            global_blocks[None, None, :], owned_blocks.shape + (global_blocks.shape[0],)
        )
    )
    pieces.append(random_blocks[owned_blocks])
    return jnp.concatenate(pieces, axis=2).reshape(device_ids.shape[0], -1)


def shards_exchange(query, keys, values, grad_out, global_blocks, random_blocks):
    devices = lax.axis_size("seq")
    tok_rows, width = query.shape
    per_device = tok_rows // BLK
    total_blocks = per_device * devices
    row_share = BLK // devices
    key_blocks = keys.reshape(per_device, BLK, width)
    value_blocks = values.reshape(per_device, BLK, width)
    row_keys, row_values = (
        lax.all_to_all(
            keys.reshape(per_device, devices, row_share, width),
            "seq",
            split_axis=1,
            concat_axis=0,
            tiled=True,
        ),
        lax.all_to_all(
            values.reshape(per_device, devices, row_share, width),
            "seq",
            split_axis=1,
            concat_axis=0,
            tiled=True,
        ),
    )
    row_keys = row_keys.reshape(total_blocks, row_share, width)
    row_values = row_values.reshape(total_blocks, row_share, width)
    fetch_lists = fetch_table(
        jnp.arange(devices, dtype=jnp.int32), per_device, total_blocks, global_blocks, random_blocks
    )
    fetched = fetch_lists.shape[1]
    got_keys, got_values = (
        lax.all_to_all(row_keys[fetch_lists], "seq", split_axis=0, concat_axis=2, tiled=True),
        lax.all_to_all(row_values[fetch_lists], "seq", split_axis=0, concat_axis=2, tiled=True),
    )
    offset = 0
    window_keys = got_keys[:, 0:2]
    window_values = got_values[:, 0:2]
    offset = 2
    global_keys = got_keys[:, offset : offset + G]
    global_values = got_values[:, offset : offset + G]
    offset = offset + G
    random_keys = got_keys[:, offset:]
    random_values = got_values[:, offset:]
    tile_keys = jnp.concatenate(
        [key_blocks[:, None], window_keys, global_keys, random_keys], axis=1
    ).reshape(per_device, -1, width)
    tile_values = jnp.concatenate(
        [value_blocks[:, None], window_values, global_values, random_values], axis=1
    ).reshape(per_device, -1, width)
    attended, grad_query, tile_gkeys, tile_gvalues = lax.map(
        attend_block,
        (
            query.reshape(per_device, BLK, width),
            grad_out.reshape(per_device, BLK, width),
            tile_keys,
            tile_values,
        ),
    )
    tile_gkeys = tile_gkeys.reshape(per_device, -1, BLK, width)
    tile_gvalues = tile_gvalues.reshape(per_device, -1, BLK, width)
    window_gkeys = tile_gkeys[:, 1:3]
    window_gvalues = tile_gvalues[:, 1:3]
    global_gkeys = tile_gkeys[:, 3 : 3 + G]
    global_gvalues = tile_gvalues[:, 3 : 3 + G]
    back_keys = []
    back_values = []
    back_keys.append(window_gkeys)
    back_values.append(window_gvalues)
    back_keys.append(global_gkeys)
    back_values.append(global_gvalues)
    back_keys.append(tile_gkeys[:, 3 + G :])
    back_values.append(tile_gvalues[:, 3 + G :])
    back_keys = jnp.concatenate(back_keys, axis=1).reshape(1, fetched, devices, row_share, width)
    back_values = jnp.concatenate(back_values, axis=1).reshape(
        1, fetched, devices, row_share, width
    )
    recv_keys, recv_values = (
        lax.all_to_all(back_keys, "seq", split_axis=2, concat_axis=0, tiled=True),
        lax.all_to_all(back_values, "seq", split_axis=2, concat_axis=0, tiled=True),
    )
    flat_index = fetch_lists.reshape(-1)
    table_keys = (
        jnp.zeros((total_blocks, row_share, width), jnp.float32)
        .at[flat_index]
        .add(recv_keys.reshape(devices * fetched, row_share, width))
    )
    table_values = (
        jnp.zeros((total_blocks, row_share, width), jnp.float32)
        .at[flat_index]
        .add(recv_values.reshape(devices * fetched, row_share, width))
    )
    home_keys, home_values = (
        lax.all_to_all(
            table_keys.reshape(total_blocks, 1, row_share, width),
            "seq",
            split_axis=0,
            concat_axis=1,
            tiled=True,
        ),
        lax.all_to_all(
            table_values.reshape(total_blocks, 1, row_share, width),
            "seq",
            split_axis=0,
            concat_axis=1,
            tiled=True,
        ),
    )
    grad_key_blocks = tile_gkeys[:, 0] + home_keys.reshape(per_device, BLK, width)
    grad_value_blocks = tile_gvalues[:, 0] + home_values.reshape(per_device, BLK, width)
    return (
        attended.reshape(tok_rows, width),
        grad_query.reshape(tok_rows, width),
        grad_key_blocks.astype(jnp.bfloat16).reshape(tok_rows, width),
        grad_value_blocks.astype(jnp.bfloat16).reshape(tok_rows, width),
    )

SLOTS = 3 + G + 3


def _send(v, pairs):
    return lax.ppermute(v.astype(jnp.bfloat16), "seq", pairs).astype(v.dtype)


def _line_shifts(x, n):
    line_len = n // 4
    z = lax.axis_index("seq") // 4
    got = {0: x}
    for d in range(1, line_len):
        for sign in (1, -1):
            step = sign * d
            pairs = [
                (4 * z0 + r, 4 * (z0 + step) + r)
                for z0 in range(line_len)
                if 0 <= z0 + step < line_len
                for r in range(4)
            ]
            got[-step] = _send(x, pairs)
    rel = jnp.stack([got[m] for m in range(-(line_len - 1), line_len)])
    return lax.dynamic_slice_in_dim(rel, line_len - 1 - z, line_len, axis=0)


def _gather_z_first(x, n):
    line = _line_shifts(x, n)
    other = _send(line, [(i, i ^ 2) for i in range(n)])
    pair = jnp.stack([line, other])
    sibling = _send(pair, [(i, i ^ 1) for i in range(n)])
    return jnp.stack([pair, sibling])


def _gather_y_first(x, n):
    other = _send(x, [(i, i ^ 2) for i in range(n)])
    line = _line_shifts(jnp.stack([x, other]), n)
    pair = jnp.moveaxis(line, 1, 0)
    sibling = _send(pair, [(i, i ^ 1) for i in range(n)])
    return jnp.stack([pair, sibling])


Y_FIRST_HEADS = 3


def gather_blocks(x, n):
    split = x.shape[-1] - Y_FIRST_HEADS * HD
    return jnp.concatenate(
        [_gather_z_first(x[:, :split], n), _gather_y_first(x[:, split:], n)], axis=-1
    )


def _attend_kernel(pos_ref, q_ref, g_ref, *refs):
    k_refs = refs[:SLOTS]
    v_refs = refs[SLOTS : 2 * SLOTS]
    att_ref, gq_ref, dk_ref, dv_ref = refs[2 * SLOTS :]
    scale = HD ** (-0.5)
    nt = (((1,), (1,)), ((), ()))
    q = q_ref[...]
    g = g_ref[...]
    k_all = jnp.concatenate([r[...] for r in k_refs], axis=0)
    v_all = jnp.concatenate([r[...] for r in v_refs], axis=0)
    s = lax.dot_general(q, k_all, nt, preferred_element_type=jnp.float32) * scale
    e = jnp.exp(s - jnp.max(s, axis=-1, keepdims=True))
    p = e / jnp.sum(e, axis=-1, keepdims=True)
    w = p.astype(jnp.bfloat16)
    att = jnp.dot(w, v_all, preferred_element_type=jnp.float32).astype(jnp.bfloat16)
    att_ref[...] = att
    delta = jnp.sum(g.astype(jnp.float32) * att.astype(jnp.float32), axis=-1, keepdims=True)
    gp = lax.dot_general(g, v_all, nt, preferred_element_type=jnp.float32)
    gs32 = p * (gp - delta)
    gs = gs32.astype(jnp.bfloat16)
    gq_ref[...] = (jnp.dot(gs, k_all, preferred_element_type=jnp.float32) * scale).astype(
        jnp.bfloat16
    )
    gk = jnp.dot(gs32.T.astype(jnp.bfloat16), q, preferred_element_type=jnp.float32) * scale
    gv = jnp.dot(p.T.astype(jnp.bfloat16), g, preferred_element_type=jnp.float32)
    dk_ref[...] = jnp.zeros(dk_ref.shape, jnp.float32)
    dv_ref[...] = jnp.zeros(dv_ref.shape, jnp.float32)
    rows = q.shape[0]
    for j in range(SLOTS):
        at = pos_ref[j]
        dk_ref[at] = dk_ref[at] + gk[j * rows : (j + 1) * rows]
        dv_ref[at] = dv_ref[at] + gv[j * rows : (j + 1) * rows]


def attend_local(pos, query, grad_out, keys_local, values_local):
    rows, width = query.shape
    held = keys_local.shape[0]
    heads = width // HD
    head_spec = pl.BlockSpec((rows, HD), lambda h, pos: (0, h))
    slot_specs = [
        pl.BlockSpec((None, rows, HD), lambda h, pos, j=j: (pos[j], 0, h)) for j in range(SLOTS)
    ]
    part_spec = pl.BlockSpec((held, rows, HD), lambda h, pos: (0, 0, h))
    flops = 12 * rows * SLOTS * rows * HD * heads
    moved = 2 * SLOTS * rows * width * 2 + 4 * rows * width * 2 + 2 * held * rows * width * 4
    call = pl.pallas_call(
        _attend_kernel,
        out_shape=(
            jax.ShapeDtypeStruct((rows, width), jnp.bfloat16),
            jax.ShapeDtypeStruct((rows, width), jnp.bfloat16),
            jax.ShapeDtypeStruct((held, rows, width), jnp.float32),
            jax.ShapeDtypeStruct((held, rows, width), jnp.float32),
        ),
        grid_spec=pltpu.PrefetchScalarGridSpec(
            num_scalar_prefetch=1,
            grid=(heads,),
            in_specs=[head_spec, head_spec] + slot_specs + slot_specs,
            out_specs=(head_spec, head_spec, part_spec, part_spec),
        ),
        compiler_params=pltpu.CompilerParams(dimension_semantics=("arbitrary",)),
        cost_estimate=pl.CostEstimate(
            flops=flops, transcendentals=rows * SLOTS * rows * heads, bytes_accessed=moved
        ),
    )
    return call(
        pos, query, grad_out, *([keys_local] * SLOTS), *([values_local] * SLOTS)
    )


def shards_gather(query, keys, values, grad_out, global_blocks, random_blocks):
    n = lax.axis_size("seq")
    rows, width = query.shape
    line_len = n // 4
    idx = lax.axis_index("seq")
    listed = jnp.concatenate(
        [
            jnp.stack([idx, (idx - 1) % n, (idx + 1) % n]).astype(jnp.int32),
            global_blocks.astype(jnp.int32),
            random_blocks[idx].astype(jnp.int32),
        ]
    )
    listed = jnp.clip(listed, 0, n - 1)
    core = idx % 2
    ypos = (idx // 2) % 2
    pos = (((listed % 2) ^ core) * 2 + (((listed // 2) % 2) ^ ypos)) * line_len + listed // 4
    keys_local = gather_blocks(keys, n).reshape(n, rows, width)
    values_local = gather_blocks(values, n).reshape(n, rows, width)
    attended, grad_query, part_keys, part_values = attend_local(
        pos, query, grad_out, keys_local, values_local
    )
    scatter = jax.linear_transpose(
        lambda t: gather_blocks(t, n), jax.ShapeDtypeStruct((rows, width), jnp.float32)
    )
    (grad_keys,) = scatter(part_keys.reshape(2, 2, line_len, rows, width))
    (grad_values,) = scatter(part_values.reshape(2, 2, line_len, rows, width))
    return (
        attended,
        grad_query,
        grad_keys.astype(jnp.bfloat16),
        grad_values.astype(jnp.bfloat16),
    )


def shards(query, keys, values, grad_out, global_blocks, random_blocks):
    n = lax.axis_size("seq")
    if query.shape[0] == BLK and n % 4 == 0 and n <= 32:
        return shards_gather(query, keys, values, grad_out, global_blocks, random_blocks)
    return shards_exchange(query, keys, values, grad_out, global_blocks, random_blocks)


def solution(mesh):
    placed = (
        P(("groups", "seq"), None),
        P(("groups", "seq"), None),
        P(("groups", "seq"), None),
        P(("groups", "seq"), None),
        P("groups"),
        P("groups", None),
    )
    return jax.shard_map(
        shards,
        mesh=mesh,
        in_specs=placed,
        out_specs=(
            P(("groups", "seq"), None),
            P(("groups", "seq"), None),
            P(("groups", "seq"), None),
            P(("groups", "seq"), None),
        ),
        check_vma=False,
    )
```

```python
import jax
import jax.numpy as jnp
from jax import lax
from jax.experimental import pallas as pl
from jax.experimental.pallas import tpu as pltpu
from jax.sharding import PartitionSpec as P

HD = 128
BLK = 128
G = 2


def attend_block(operands):
    query_blk, grad_blk, key_tiles, value_tiles = operands
    row_count, width = query_blk.shape
    keys_total = key_tiles.shape[0]
    head_size = HD
    head_count = width // head_size
    scaling = HD ** (-0.5)
    last_dims = (((1,), (1,)), ((), ()))
    first_dims = (((0,), (0,)), ((), ()))

    def one_head(head, carry):
        out_attended, out_gquery, out_gkeys, out_gvalues = carry
        start = head * head_size
        query_head = lax.dynamic_slice_in_dim(query_blk, start, head_size, 1)
        grad_head = lax.dynamic_slice_in_dim(grad_blk, start, head_size, 1)
        key_head = lax.dynamic_slice_in_dim(key_tiles, start, head_size, 1)
        value_head = lax.dynamic_slice_in_dim(value_tiles, start, head_size, 1)
        scores = (
            lax.dot_general(query_head, key_head, last_dims, preferred_element_type=jnp.float32)
            * scaling
        )
        probability = jax.nn.softmax(scores, axis=-1)
        weights = probability.astype(jnp.bfloat16)
        attended_head = jnp.dot(weights, value_head, preferred_element_type=jnp.float32).astype(
            jnp.bfloat16
        )
        deltas = jnp.sum(grad_head.astype(jnp.float32) * attended_head.astype(jnp.float32), axis=-1)
        grad_prob = lax.dot_general(
            grad_head, value_head, last_dims, preferred_element_type=jnp.float32
        )
        grad_score = (probability * (grad_prob - deltas[:, None])).astype(jnp.bfloat16)
        gquery_head = (
            jnp.dot(grad_score, key_head, preferred_element_type=jnp.float32) * scaling
        ).astype(jnp.bfloat16)
        gkeys_head = (
            lax.dot_general(grad_score, query_head, first_dims, preferred_element_type=jnp.float32)
            * scaling
        )
        gvalues_head = lax.dot_general(
            weights, grad_head, first_dims, preferred_element_type=jnp.float32
        )
        out_attended = lax.dynamic_update_slice_in_dim(out_attended, attended_head, start, 1)
        out_gquery = lax.dynamic_update_slice_in_dim(out_gquery, gquery_head, start, 1)
        out_gkeys = lax.dynamic_update_slice_in_dim(out_gkeys, gkeys_head, start, 1)
        out_gvalues = lax.dynamic_update_slice_in_dim(out_gvalues, gvalues_head, start, 1)
        return (out_attended, out_gquery, out_gkeys, out_gvalues)

    initial = (
        jnp.zeros((row_count, width), jnp.bfloat16),
        jnp.zeros((row_count, width), jnp.bfloat16),
        jnp.zeros((keys_total, width), jnp.float32),
        jnp.zeros((keys_total, width), jnp.float32),
    )
    return lax.fori_loop(0, head_count, one_head, initial)


def fetch_table(device_ids, block_count, total_blocks, global_blocks, random_blocks):
    owned_blocks = (
        device_ids[:, None] * block_count + jnp.arange(block_count, dtype=jnp.int32)[None, :]
    )
    pieces = []
    pieces.append(((owned_blocks - 1) % total_blocks)[:, :, None])
    pieces.append(((owned_blocks + 1) % total_blocks)[:, :, None])
    pieces.append(
        jnp.broadcast_to(
            global_blocks[None, None, :], owned_blocks.shape + (global_blocks.shape[0],)
        )
    )
    pieces.append(random_blocks[owned_blocks])
    return jnp.concatenate(pieces, axis=2).reshape(device_ids.shape[0], -1)


def shards_exchange(query, keys, values, grad_out, global_blocks, random_blocks):
    devices = lax.axis_size("seq")
    tok_rows, width = query.shape
    per_device = tok_rows // BLK
    total_blocks = per_device * devices
    row_share = BLK // devices
    key_blocks = keys.reshape(per_device, BLK, width)
    value_blocks = values.reshape(per_device, BLK, width)
    row_keys, row_values = (
        lax.all_to_all(
            keys.reshape(per_device, devices, row_share, width),
            "seq",
            split_axis=1,
            concat_axis=0,
            tiled=True,
        ),
        lax.all_to_all(
            values.reshape(per_device, devices, row_share, width),
            "seq",
            split_axis=1,
            concat_axis=0,
            tiled=True,
        ),
    )
    row_keys = row_keys.reshape(total_blocks, row_share, width)
    row_values = row_values.reshape(total_blocks, row_share, width)
    fetch_lists = fetch_table(
        jnp.arange(devices, dtype=jnp.int32), per_device, total_blocks, global_blocks, random_blocks
    )
    fetched = fetch_lists.shape[1]
    got_keys, got_values = (
        lax.all_to_all(row_keys[fetch_lists], "seq", split_axis=0, concat_axis=2, tiled=True),
        lax.all_to_all(row_values[fetch_lists], "seq", split_axis=0, concat_axis=2, tiled=True),
    )
    offset = 0
    window_keys = got_keys[:, 0:2]
    window_values = got_values[:, 0:2]
    offset = 2
    global_keys = got_keys[:, offset : offset + G]
    global_values = got_values[:, offset : offset + G]
    offset = offset + G
    random_keys = got_keys[:, offset:]
    random_values = got_values[:, offset:]
    tile_keys = jnp.concatenate(
        [key_blocks[:, None], window_keys, global_keys, random_keys], axis=1
    ).reshape(per_device, -1, width)
    tile_values = jnp.concatenate(
        [value_blocks[:, None], window_values, global_values, random_values], axis=1
    ).reshape(per_device, -1, width)
    attended, grad_query, tile_gkeys, tile_gvalues = lax.map(
        attend_block,
        (
            query.reshape(per_device, BLK, width),
            grad_out.reshape(per_device, BLK, width),
            tile_keys,
            tile_values,
        ),
    )
    tile_gkeys = tile_gkeys.reshape(per_device, -1, BLK, width)
    tile_gvalues = tile_gvalues.reshape(per_device, -1, BLK, width)
    window_gkeys = tile_gkeys[:, 1:3]
    window_gvalues = tile_gvalues[:, 1:3]
    global_gkeys = tile_gkeys[:, 3 : 3 + G]
    global_gvalues = tile_gvalues[:, 3 : 3 + G]
    back_keys = []
    back_values = []
    back_keys.append(window_gkeys)
    back_values.append(window_gvalues)
    back_keys.append(global_gkeys)
    back_values.append(global_gvalues)
    back_keys.append(tile_gkeys[:, 3 + G :])
    back_values.append(tile_gvalues[:, 3 + G :])
    back_keys = jnp.concatenate(back_keys, axis=1).reshape(1, fetched, devices, row_share, width)
    back_values = jnp.concatenate(back_values, axis=1).reshape(
        1, fetched, devices, row_share, width
    )
    recv_keys, recv_values = (
        lax.all_to_all(back_keys, "seq", split_axis=2, concat_axis=0, tiled=True),
        lax.all_to_all(back_values, "seq", split_axis=2, concat_axis=0, tiled=True),
    )
    flat_index = fetch_lists.reshape(-1)
    table_keys = (
        jnp.zeros((total_blocks, row_share, width), jnp.float32)
        .at[flat_index]
        .add(recv_keys.reshape(devices * fetched, row_share, width))
    )
    table_values = (
        jnp.zeros((total_blocks, row_share, width), jnp.float32)
        .at[flat_index]
        .add(recv_values.reshape(devices * fetched, row_share, width))
    )
    home_keys, home_values = (
        lax.all_to_all(
            table_keys.reshape(total_blocks, 1, row_share, width),
            "seq",
            split_axis=0,
            concat_axis=1,
            tiled=True,
        ),
        lax.all_to_all(
            table_values.reshape(total_blocks, 1, row_share, width),
            "seq",
            split_axis=0,
            concat_axis=1,
            tiled=True,
        ),
    )
    grad_key_blocks = tile_gkeys[:, 0] + home_keys.reshape(per_device, BLK, width)
    grad_value_blocks = tile_gvalues[:, 0] + home_values.reshape(per_device, BLK, width)
    return (
        attended.reshape(tok_rows, width),
        grad_query.reshape(tok_rows, width),
        grad_key_blocks.astype(jnp.bfloat16).reshape(tok_rows, width),
        grad_value_blocks.astype(jnp.bfloat16).reshape(tok_rows, width),
    )

SLOTS = 3 + G + 3


def _send(v, pairs):
    return lax.ppermute(v.astype(jnp.bfloat16), "seq", pairs).astype(v.dtype)


def gather_blocks(x, n):
    line_len = n // 4
    z = lax.axis_index("seq") // 4
    ups, downs = [], []
    up, down = x, x
    for k in range(1, line_len):
        up = _send(
            up, [(4 * z0 + r, 4 * (z0 + 1) + r) for z0 in range(k - 1, line_len - 1) for r in range(4)]
        )
        down = _send(
            down, [(4 * z0 + r, 4 * (z0 - 1) + r) for z0 in range(1, line_len - k + 1) for r in range(4)]
        )
        ups.append(up)
        downs.append(down)
    rel = jnp.stack(ups[::-1] + [x] + downs)
    line = lax.dynamic_slice_in_dim(rel, line_len - 1 - z, line_len, axis=0)
    other = _send(line, [(i, i ^ 2) for i in range(n)])
    pair = jnp.stack([line, other])
    sibling = _send(pair, [(i, i ^ 1) for i in range(n)])
    return jnp.stack([pair, sibling])


def _attend_kernel(pos_ref, q_ref, g_ref, *refs):
    k_refs = refs[:SLOTS]
    v_refs = refs[SLOTS : 2 * SLOTS]
    att_ref, gq_ref, dk_ref, dv_ref = refs[2 * SLOTS :]
    scale = HD ** (-0.5)
    nt = (((1,), (1,)), ((), ()))
    q = q_ref[...]
    g = g_ref[...]
    k_all = jnp.concatenate([r[...] for r in k_refs], axis=0)
    v_all = jnp.concatenate([r[...] for r in v_refs], axis=0)
    s = lax.dot_general(q, k_all, nt, preferred_element_type=jnp.float32) * scale
    e = jnp.exp(s - jnp.max(s, axis=-1, keepdims=True))
    p = e / jnp.sum(e, axis=-1, keepdims=True)
    w = p.astype(jnp.bfloat16)
    att = jnp.dot(w, v_all, preferred_element_type=jnp.float32).astype(jnp.bfloat16)
    att_ref[...] = att
    delta = jnp.sum(g.astype(jnp.float32) * att.astype(jnp.float32), axis=-1, keepdims=True)
    gp = lax.dot_general(g, v_all, nt, preferred_element_type=jnp.float32)
    gs32 = p * (gp - delta)
    gs = gs32.astype(jnp.bfloat16)
    gq_ref[...] = (jnp.dot(gs, k_all, preferred_element_type=jnp.float32) * scale).astype(
        jnp.bfloat16
    )
    gk = jnp.dot(gs32.T.astype(jnp.bfloat16), q, preferred_element_type=jnp.float32) * scale
    gv = jnp.dot(p.T.astype(jnp.bfloat16), g, preferred_element_type=jnp.float32)
    dk_ref[...] = jnp.zeros(dk_ref.shape, jnp.float32)
    dv_ref[...] = jnp.zeros(dv_ref.shape, jnp.float32)
    rows = q.shape[0]
    for j in range(SLOTS):
        at = pos_ref[j]
        dk_ref[at] = dk_ref[at] + gk[j * rows : (j + 1) * rows]
        dv_ref[at] = dv_ref[at] + gv[j * rows : (j + 1) * rows]


def attend_local(pos, query, grad_out, keys_local, values_local):
    rows, width = query.shape
    held = keys_local.shape[0]
    heads = width // HD
    head_spec = pl.BlockSpec((rows, HD), lambda h, pos: (0, h))
    slot_specs = [
        pl.BlockSpec((None, rows, HD), lambda h, pos, j=j: (pos[j], 0, h)) for j in range(SLOTS)
    ]
    part_spec = pl.BlockSpec((held, rows, HD), lambda h, pos: (0, 0, h))
    flops = 12 * rows * SLOTS * rows * HD * heads
    moved = 2 * SLOTS * rows * width * 2 + 4 * rows * width * 2 + 2 * held * rows * width * 4
    call = pl.pallas_call(
        _attend_kernel,
        out_shape=(
            jax.ShapeDtypeStruct((rows, width), jnp.bfloat16),
            jax.ShapeDtypeStruct((rows, width), jnp.bfloat16),
            jax.ShapeDtypeStruct((held, rows, width), jnp.float32),
            jax.ShapeDtypeStruct((held, rows, width), jnp.float32),
        ),
        grid_spec=pltpu.PrefetchScalarGridSpec(
            num_scalar_prefetch=1,
            grid=(heads,),
            in_specs=[head_spec, head_spec] + slot_specs + slot_specs,
            out_specs=(head_spec, head_spec, part_spec, part_spec),
        ),
        compiler_params=pltpu.CompilerParams(dimension_semantics=("arbitrary",)),
        cost_estimate=pl.CostEstimate(
            flops=flops, transcendentals=rows * SLOTS * rows * heads, bytes_accessed=moved
        ),
    )
    return call(
        pos, query, grad_out, *([keys_local] * SLOTS), *([values_local] * SLOTS)
    )


STREAMS = 2


def _stream(pos, query, grad_out, keys, values):
    n = lax.axis_size("seq")
    rows, width = query.shape
    line_len = n // 4
    keys_local = gather_blocks(keys, n).reshape(n, rows, width)
    values_local = gather_blocks(values, n).reshape(n, rows, width)
    attended, grad_query, part_keys, part_values = attend_local(
        pos, query, grad_out, keys_local, values_local
    )
    scatter = jax.linear_transpose(
        lambda t: gather_blocks(t, n), jax.ShapeDtypeStruct((rows, width), jnp.float32)
    )
    (grad_keys,) = scatter(part_keys.reshape(2, 2, line_len, rows, width))
    (grad_values,) = scatter(part_values.reshape(2, 2, line_len, rows, width))
    return attended, grad_query, grad_keys.astype(jnp.bfloat16), grad_values.astype(jnp.bfloat16)


def shards_gather(query, keys, values, grad_out, global_blocks, random_blocks):
    n = lax.axis_size("seq")
    rows, width = query.shape
    line_len = n // 4
    idx = lax.axis_index("seq")
    listed = jnp.concatenate(
        [
            jnp.stack([idx, (idx - 1) % n, (idx + 1) % n]).astype(jnp.int32),
            global_blocks.astype(jnp.int32),
            random_blocks[idx].astype(jnp.int32),
        ]
    )
    listed = jnp.clip(listed, 0, n - 1)
    core = idx % 2
    ypos = (idx // 2) % 2
    pos = (((listed % 2) ^ core) * 2 + (((listed // 2) % 2) ^ ypos)) * line_len + listed // 4
    cut = width // STREAMS
    outs = []
    for s in range(STREAMS):
        cols = slice(s * cut, (s + 1) * cut)
        with jax.named_scope(f"stream{s}"):
            outs.append(
                _stream(pos, query[:, cols], grad_out[:, cols], keys[:, cols], values[:, cols])
            )
    return tuple(jnp.concatenate(parts, axis=1) for parts in zip(*outs))


def shards(query, keys, values, grad_out, global_blocks, random_blocks):
    n = lax.axis_size("seq")
    if query.shape[0] == BLK and n % 4 == 0 and n <= 32:
        return shards_gather(query, keys, values, grad_out, global_blocks, random_blocks)
    return shards_exchange(query, keys, values, grad_out, global_blocks, random_blocks)


def solution(mesh):
    placed = (
        P(("groups", "seq"), None),
        P(("groups", "seq"), None),
        P(("groups", "seq"), None),
        P(("groups", "seq"), None),
        P("groups"),
        P("groups", None),
    )
    return jax.shard_map(
        shards,
        mesh=mesh,
        in_specs=placed,
        out_specs=(
            P(("groups", "seq"), None),
            P(("groups", "seq"), None),
            P(("groups", "seq"), None),
            P(("groups", "seq"), None),
        ),
        check_vma=False,
    )
```

```python
import jax
import jax.numpy as jnp
from jax import lax
from jax.experimental import pallas as pl
from jax.experimental.pallas import tpu as pltpu
from jax.sharding import PartitionSpec as P

HD = 128
BLK = 128
G = 2


def attend_block(operands):
    query_blk, grad_blk, key_tiles, value_tiles = operands
    row_count, width = query_blk.shape
    keys_total = key_tiles.shape[0]
    head_size = HD
    head_count = width // head_size
    scaling = HD ** (-0.5)
    last_dims = (((1,), (1,)), ((), ()))
    first_dims = (((0,), (0,)), ((), ()))

    def one_head(head, carry):
        out_attended, out_gquery, out_gkeys, out_gvalues = carry
        start = head * head_size
        query_head = lax.dynamic_slice_in_dim(query_blk, start, head_size, 1)
        grad_head = lax.dynamic_slice_in_dim(grad_blk, start, head_size, 1)
        key_head = lax.dynamic_slice_in_dim(key_tiles, start, head_size, 1)
        value_head = lax.dynamic_slice_in_dim(value_tiles, start, head_size, 1)
        scores = (
            lax.dot_general(query_head, key_head, last_dims, preferred_element_type=jnp.float32)
            * scaling
        )
        probability = jax.nn.softmax(scores, axis=-1)
        weights = probability.astype(jnp.bfloat16)
        attended_head = jnp.dot(weights, value_head, preferred_element_type=jnp.float32).astype(
            jnp.bfloat16
        )
        deltas = jnp.sum(grad_head.astype(jnp.float32) * attended_head.astype(jnp.float32), axis=-1)
        grad_prob = lax.dot_general(
            grad_head, value_head, last_dims, preferred_element_type=jnp.float32
        )
        grad_score = (probability * (grad_prob - deltas[:, None])).astype(jnp.bfloat16)
        gquery_head = (
            jnp.dot(grad_score, key_head, preferred_element_type=jnp.float32) * scaling
        ).astype(jnp.bfloat16)
        gkeys_head = (
            lax.dot_general(grad_score, query_head, first_dims, preferred_element_type=jnp.float32)
            * scaling
        )
        gvalues_head = lax.dot_general(
            weights, grad_head, first_dims, preferred_element_type=jnp.float32
        )
        out_attended = lax.dynamic_update_slice_in_dim(out_attended, attended_head, start, 1)
        out_gquery = lax.dynamic_update_slice_in_dim(out_gquery, gquery_head, start, 1)
        out_gkeys = lax.dynamic_update_slice_in_dim(out_gkeys, gkeys_head, start, 1)
        out_gvalues = lax.dynamic_update_slice_in_dim(out_gvalues, gvalues_head, start, 1)
        return (out_attended, out_gquery, out_gkeys, out_gvalues)

    initial = (
        jnp.zeros((row_count, width), jnp.bfloat16),
        jnp.zeros((row_count, width), jnp.bfloat16),
        jnp.zeros((keys_total, width), jnp.float32),
        jnp.zeros((keys_total, width), jnp.float32),
    )
    return lax.fori_loop(0, head_count, one_head, initial)


def fetch_table(device_ids, block_count, total_blocks, global_blocks, random_blocks):
    owned_blocks = (
        device_ids[:, None] * block_count + jnp.arange(block_count, dtype=jnp.int32)[None, :]
    )
    pieces = []
    pieces.append(((owned_blocks - 1) % total_blocks)[:, :, None])
    pieces.append(((owned_blocks + 1) % total_blocks)[:, :, None])
    pieces.append(
        jnp.broadcast_to(
            global_blocks[None, None, :], owned_blocks.shape + (global_blocks.shape[0],)
        )
    )
    pieces.append(random_blocks[owned_blocks])
    return jnp.concatenate(pieces, axis=2).reshape(device_ids.shape[0], -1)


def shards_exchange(query, keys, values, grad_out, global_blocks, random_blocks):
    devices = lax.axis_size("seq")
    tok_rows, width = query.shape
    per_device = tok_rows // BLK
    total_blocks = per_device * devices
    row_share = BLK // devices
    key_blocks = keys.reshape(per_device, BLK, width)
    value_blocks = values.reshape(per_device, BLK, width)
    row_keys, row_values = (
        lax.all_to_all(
            keys.reshape(per_device, devices, row_share, width),
            "seq",
            split_axis=1,
            concat_axis=0,
            tiled=True,
        ),
        lax.all_to_all(
            values.reshape(per_device, devices, row_share, width),
            "seq",
            split_axis=1,
            concat_axis=0,
            tiled=True,
        ),
    )
    row_keys = row_keys.reshape(total_blocks, row_share, width)
    row_values = row_values.reshape(total_blocks, row_share, width)
    fetch_lists = fetch_table(
        jnp.arange(devices, dtype=jnp.int32), per_device, total_blocks, global_blocks, random_blocks
    )
    fetched = fetch_lists.shape[1]
    got_keys, got_values = (
        lax.all_to_all(row_keys[fetch_lists], "seq", split_axis=0, concat_axis=2, tiled=True),
        lax.all_to_all(row_values[fetch_lists], "seq", split_axis=0, concat_axis=2, tiled=True),
    )
    offset = 0
    window_keys = got_keys[:, 0:2]
    window_values = got_values[:, 0:2]
    offset = 2
    global_keys = got_keys[:, offset : offset + G]
    global_values = got_values[:, offset : offset + G]
    offset = offset + G
    random_keys = got_keys[:, offset:]
    random_values = got_values[:, offset:]
    tile_keys = jnp.concatenate(
        [key_blocks[:, None], window_keys, global_keys, random_keys], axis=1
    ).reshape(per_device, -1, width)
    tile_values = jnp.concatenate(
        [value_blocks[:, None], window_values, global_values, random_values], axis=1
    ).reshape(per_device, -1, width)
    attended, grad_query, tile_gkeys, tile_gvalues = lax.map(
        attend_block,
        (
            query.reshape(per_device, BLK, width),
            grad_out.reshape(per_device, BLK, width),
            tile_keys,
            tile_values,
        ),
    )
    tile_gkeys = tile_gkeys.reshape(per_device, -1, BLK, width)
    tile_gvalues = tile_gvalues.reshape(per_device, -1, BLK, width)
    window_gkeys = tile_gkeys[:, 1:3]
    window_gvalues = tile_gvalues[:, 1:3]
    global_gkeys = tile_gkeys[:, 3 : 3 + G]
    global_gvalues = tile_gvalues[:, 3 : 3 + G]
    back_keys = []
    back_values = []
    back_keys.append(window_gkeys)
    back_values.append(window_gvalues)
    back_keys.append(global_gkeys)
    back_values.append(global_gvalues)
    back_keys.append(tile_gkeys[:, 3 + G :])
    back_values.append(tile_gvalues[:, 3 + G :])
    back_keys = jnp.concatenate(back_keys, axis=1).reshape(1, fetched, devices, row_share, width)
    back_values = jnp.concatenate(back_values, axis=1).reshape(
        1, fetched, devices, row_share, width
    )
    recv_keys, recv_values = (
        lax.all_to_all(back_keys, "seq", split_axis=2, concat_axis=0, tiled=True),
        lax.all_to_all(back_values, "seq", split_axis=2, concat_axis=0, tiled=True),
    )
    flat_index = fetch_lists.reshape(-1)
    table_keys = (
        jnp.zeros((total_blocks, row_share, width), jnp.float32)
        .at[flat_index]
        .add(recv_keys.reshape(devices * fetched, row_share, width))
    )
    table_values = (
        jnp.zeros((total_blocks, row_share, width), jnp.float32)
        .at[flat_index]
        .add(recv_values.reshape(devices * fetched, row_share, width))
    )
    home_keys, home_values = (
        lax.all_to_all(
            table_keys.reshape(total_blocks, 1, row_share, width),
            "seq",
            split_axis=0,
            concat_axis=1,
            tiled=True,
        ),
        lax.all_to_all(
            table_values.reshape(total_blocks, 1, row_share, width),
            "seq",
            split_axis=0,
            concat_axis=1,
            tiled=True,
        ),
    )
    grad_key_blocks = tile_gkeys[:, 0] + home_keys.reshape(per_device, BLK, width)
    grad_value_blocks = tile_gvalues[:, 0] + home_values.reshape(per_device, BLK, width)
    return (
        attended.reshape(tok_rows, width),
        grad_query.reshape(tok_rows, width),
        grad_key_blocks.astype(jnp.bfloat16).reshape(tok_rows, width),
        grad_value_blocks.astype(jnp.bfloat16).reshape(tok_rows, width),
    )

SLOTS = 3 + G + 3


def _send(v, pairs):
    return lax.ppermute(v.astype(jnp.bfloat16), "seq", pairs).astype(v.dtype)


def gather_blocks(x, n):
    line_len = n // 4
    z = lax.axis_index("seq") // 4
    ups, downs = [], []
    up, down = x, x
    for k in range(1, line_len):
        up = _send(
            up, [(4 * z0 + r, 4 * (z0 + 1) + r) for z0 in range(k - 1, line_len - 1) for r in range(4)]
        )
        down = _send(
            down, [(4 * z0 + r, 4 * (z0 - 1) + r) for z0 in range(1, line_len - k + 1) for r in range(4)]
        )
        ups.append(up)
        downs.append(down)
    rel = jnp.stack(ups[::-1] + [x] + downs)
    line = lax.dynamic_slice_in_dim(rel, line_len - 1 - z, line_len, axis=0)
    other = _send(line, [(i, i ^ 2) for i in range(n)])
    pair = jnp.stack([line, other])
    sibling = _send(pair, [(i, i ^ 1) for i in range(n)])
    return jnp.stack([pair, sibling])


def _attend_kernel(pos_ref, q_ref, g_ref, *refs):
    k_refs = refs[:SLOTS]
    v_refs = refs[SLOTS : 2 * SLOTS]
    att_ref, gq_ref, dk_ref, dv_ref = refs[2 * SLOTS :]
    scale = HD ** (-0.5)
    nt = (((1,), (1,)), ((), ()))
    q = q_ref[...]
    g = g_ref[...]
    k_all = jnp.concatenate([r[...] for r in k_refs], axis=0)
    v_all = jnp.concatenate([r[...] for r in v_refs], axis=0)
    s = lax.dot_general(q, k_all, nt, preferred_element_type=jnp.float32) * scale
    e = jnp.exp(s - jnp.max(s, axis=-1, keepdims=True))
    p = e / jnp.sum(e, axis=-1, keepdims=True)
    w = p.astype(jnp.bfloat16)
    att = jnp.dot(w, v_all, preferred_element_type=jnp.float32).astype(jnp.bfloat16)
    att_ref[...] = att
    delta = jnp.sum(g.astype(jnp.float32) * att.astype(jnp.float32), axis=-1, keepdims=True)
    gp = lax.dot_general(g, v_all, nt, preferred_element_type=jnp.float32)
    gs32 = p * (gp - delta)
    gs = gs32.astype(jnp.bfloat16)
    gq_ref[...] = (jnp.dot(gs, k_all, preferred_element_type=jnp.float32) * scale).astype(
        jnp.bfloat16
    )
    gk = jnp.dot(gs32.T.astype(jnp.bfloat16), q, preferred_element_type=jnp.float32) * scale
    gv = jnp.dot(p.T.astype(jnp.bfloat16), g, preferred_element_type=jnp.float32)
    dk_ref[...] = jnp.zeros(dk_ref.shape, jnp.float32)
    dv_ref[...] = jnp.zeros(dv_ref.shape, jnp.float32)
    rows = q.shape[0]
    for j in range(SLOTS):
        at = pos_ref[j]
        dk_ref[at] = dk_ref[at] + gk[j * rows : (j + 1) * rows]
        dv_ref[at] = dv_ref[at] + gv[j * rows : (j + 1) * rows]


def attend_local(pos, query, grad_out, keys_local, values_local):
    rows, width = query.shape
    held = keys_local.shape[0]
    heads = width // HD
    head_spec = pl.BlockSpec((rows, HD), lambda h, pos: (0, h))
    slot_specs = [
        pl.BlockSpec((None, rows, HD), lambda h, pos, j=j: (pos[j], 0, h)) for j in range(SLOTS)
    ]
    part_spec = pl.BlockSpec((held, rows, HD), lambda h, pos: (0, 0, h))
    flops = 12 * rows * SLOTS * rows * HD * heads
    moved = 2 * SLOTS * rows * width * 2 + 4 * rows * width * 2 + 2 * held * rows * width * 4
    call = pl.pallas_call(
        _attend_kernel,
        out_shape=(
            jax.ShapeDtypeStruct((rows, width), jnp.bfloat16),
            jax.ShapeDtypeStruct((rows, width), jnp.bfloat16),
            jax.ShapeDtypeStruct((held, rows, width), jnp.float32),
            jax.ShapeDtypeStruct((held, rows, width), jnp.float32),
        ),
        grid_spec=pltpu.PrefetchScalarGridSpec(
            num_scalar_prefetch=1,
            grid=(heads,),
            in_specs=[head_spec, head_spec] + slot_specs + slot_specs,
            out_specs=(head_spec, head_spec, part_spec, part_spec),
        ),
        compiler_params=pltpu.CompilerParams(dimension_semantics=("arbitrary",)),
        cost_estimate=pl.CostEstimate(
            flops=flops, transcendentals=rows * SLOTS * rows * heads, bytes_accessed=moved
        ),
    )
    return call(
        pos, query, grad_out, *([keys_local] * SLOTS), *([values_local] * SLOTS)
    )


STREAMS = 2


def _stream(pos, query, grad_out, keys, values, after=None):
    n = lax.axis_size("seq")
    rows, width = query.shape
    line_len = n // 4
    if after is not None:
        keys, values, _ = lax.optimization_barrier((keys, values, after))
    keys_local = gather_blocks(keys, n).reshape(n, rows, width)
    values_local = gather_blocks(values, n).reshape(n, rows, width)
    attended, grad_query, part_keys, part_values = attend_local(
        pos, query, grad_out, keys_local, values_local
    )
    scatter = jax.linear_transpose(
        lambda t: gather_blocks(t, n), jax.ShapeDtypeStruct((rows, width), jnp.float32)
    )
    (grad_keys,) = scatter(part_keys.reshape(2, 2, line_len, rows, width))
    (grad_values,) = scatter(part_values.reshape(2, 2, line_len, rows, width))
    outs = (attended, grad_query, grad_keys.astype(jnp.bfloat16), grad_values.astype(jnp.bfloat16))
    return outs, (keys_local, values_local)


def shards_gather(query, keys, values, grad_out, global_blocks, random_blocks):
    n = lax.axis_size("seq")
    rows, width = query.shape
    line_len = n // 4
    idx = lax.axis_index("seq")
    listed = jnp.concatenate(
        [
            jnp.stack([idx, (idx - 1) % n, (idx + 1) % n]).astype(jnp.int32),
            global_blocks.astype(jnp.int32),
            random_blocks[idx].astype(jnp.int32),
        ]
    )
    listed = jnp.clip(listed, 0, n - 1)
    core = idx % 2
    ypos = (idx // 2) % 2
    pos = (((listed % 2) ^ core) * 2 + (((listed // 2) % 2) ^ ypos)) * line_len + listed // 4
    cut = width // STREAMS
    outs = []
    after = None
    for s in range(STREAMS):
        cols = slice(s * cut, (s + 1) * cut)
        with jax.named_scope(f"stream{s}"):
            out, after = _stream(
                pos, query[:, cols], grad_out[:, cols], keys[:, cols], values[:, cols], after
            )
            outs.append(out)
    return tuple(jnp.concatenate(parts, axis=1) for parts in zip(*outs))


def shards(query, keys, values, grad_out, global_blocks, random_blocks):
    n = lax.axis_size("seq")
    if query.shape[0] == BLK and n % 4 == 0 and n <= 32:
        return shards_gather(query, keys, values, grad_out, global_blocks, random_blocks)
    return shards_exchange(query, keys, values, grad_out, global_blocks, random_blocks)


def solution(mesh):
    placed = (
        P(("groups", "seq"), None),
        P(("groups", "seq"), None),
        P(("groups", "seq"), None),
        P(("groups", "seq"), None),
        P("groups"),
        P("groups", None),
    )
    return jax.shard_map(
        shards,
        mesh=mesh,
        in_specs=placed,
        out_specs=(
            P(("groups", "seq"), None),
            P(("groups", "seq"), None),
            P(("groups", "seq"), None),
            P(("groups", "seq"), None),
        ),
        check_vma=False,
    )
```

```python
import jax
import jax.numpy as jnp
from jax import lax
from jax.experimental import pallas as pl
from jax.experimental.pallas import tpu as pltpu
from jax.sharding import PartitionSpec as P

HD = 128
BLK = 128
G = 2


def attend_block(operands):
    query_blk, grad_blk, key_tiles, value_tiles = operands
    row_count, width = query_blk.shape
    keys_total = key_tiles.shape[0]
    head_size = HD
    head_count = width // head_size
    scaling = HD ** (-0.5)
    last_dims = (((1,), (1,)), ((), ()))
    first_dims = (((0,), (0,)), ((), ()))

    def one_head(head, carry):
        out_attended, out_gquery, out_gkeys, out_gvalues = carry
        start = head * head_size
        query_head = lax.dynamic_slice_in_dim(query_blk, start, head_size, 1)
        grad_head = lax.dynamic_slice_in_dim(grad_blk, start, head_size, 1)
        key_head = lax.dynamic_slice_in_dim(key_tiles, start, head_size, 1)
        value_head = lax.dynamic_slice_in_dim(value_tiles, start, head_size, 1)
        scores = (
            lax.dot_general(query_head, key_head, last_dims, preferred_element_type=jnp.float32)
            * scaling
        )
        probability = jax.nn.softmax(scores, axis=-1)
        weights = probability.astype(jnp.bfloat16)
        attended_head = jnp.dot(weights, value_head, preferred_element_type=jnp.float32).astype(
            jnp.bfloat16
        )
        deltas = jnp.sum(grad_head.astype(jnp.float32) * attended_head.astype(jnp.float32), axis=-1)
        grad_prob = lax.dot_general(
            grad_head, value_head, last_dims, preferred_element_type=jnp.float32
        )
        grad_score = (probability * (grad_prob - deltas[:, None])).astype(jnp.bfloat16)
        gquery_head = (
            jnp.dot(grad_score, key_head, preferred_element_type=jnp.float32) * scaling
        ).astype(jnp.bfloat16)
        gkeys_head = (
            lax.dot_general(grad_score, query_head, first_dims, preferred_element_type=jnp.float32)
            * scaling
        )
        gvalues_head = lax.dot_general(
            weights, grad_head, first_dims, preferred_element_type=jnp.float32
        )
        out_attended = lax.dynamic_update_slice_in_dim(out_attended, attended_head, start, 1)
        out_gquery = lax.dynamic_update_slice_in_dim(out_gquery, gquery_head, start, 1)
        out_gkeys = lax.dynamic_update_slice_in_dim(out_gkeys, gkeys_head, start, 1)
        out_gvalues = lax.dynamic_update_slice_in_dim(out_gvalues, gvalues_head, start, 1)
        return (out_attended, out_gquery, out_gkeys, out_gvalues)

    initial = (
        jnp.zeros((row_count, width), jnp.bfloat16),
        jnp.zeros((row_count, width), jnp.bfloat16),
        jnp.zeros((keys_total, width), jnp.float32),
        jnp.zeros((keys_total, width), jnp.float32),
    )
    return lax.fori_loop(0, head_count, one_head, initial)


def fetch_table(device_ids, block_count, total_blocks, global_blocks, random_blocks):
    owned_blocks = (
        device_ids[:, None] * block_count + jnp.arange(block_count, dtype=jnp.int32)[None, :]
    )
    pieces = []
    pieces.append(((owned_blocks - 1) % total_blocks)[:, :, None])
    pieces.append(((owned_blocks + 1) % total_blocks)[:, :, None])
    pieces.append(
        jnp.broadcast_to(
            global_blocks[None, None, :], owned_blocks.shape + (global_blocks.shape[0],)
        )
    )
    pieces.append(random_blocks[owned_blocks])
    return jnp.concatenate(pieces, axis=2).reshape(device_ids.shape[0], -1)


def shards_exchange(query, keys, values, grad_out, global_blocks, random_blocks):
    devices = lax.axis_size("seq")
    tok_rows, width = query.shape
    per_device = tok_rows // BLK
    total_blocks = per_device * devices
    row_share = BLK // devices
    key_blocks = keys.reshape(per_device, BLK, width)
    value_blocks = values.reshape(per_device, BLK, width)
    row_keys, row_values = (
        lax.all_to_all(
            keys.reshape(per_device, devices, row_share, width),
            "seq",
            split_axis=1,
            concat_axis=0,
            tiled=True,
        ),
        lax.all_to_all(
            values.reshape(per_device, devices, row_share, width),
            "seq",
            split_axis=1,
            concat_axis=0,
            tiled=True,
        ),
    )
    row_keys = row_keys.reshape(total_blocks, row_share, width)
    row_values = row_values.reshape(total_blocks, row_share, width)
    fetch_lists = fetch_table(
        jnp.arange(devices, dtype=jnp.int32), per_device, total_blocks, global_blocks, random_blocks
    )
    fetched = fetch_lists.shape[1]
    got_keys, got_values = (
        lax.all_to_all(row_keys[fetch_lists], "seq", split_axis=0, concat_axis=2, tiled=True),
        lax.all_to_all(row_values[fetch_lists], "seq", split_axis=0, concat_axis=2, tiled=True),
    )
    offset = 0
    window_keys = got_keys[:, 0:2]
    window_values = got_values[:, 0:2]
    offset = 2
    global_keys = got_keys[:, offset : offset + G]
    global_values = got_values[:, offset : offset + G]
    offset = offset + G
    random_keys = got_keys[:, offset:]
    random_values = got_values[:, offset:]
    tile_keys = jnp.concatenate(
        [key_blocks[:, None], window_keys, global_keys, random_keys], axis=1
    ).reshape(per_device, -1, width)
    tile_values = jnp.concatenate(
        [value_blocks[:, None], window_values, global_values, random_values], axis=1
    ).reshape(per_device, -1, width)
    attended, grad_query, tile_gkeys, tile_gvalues = lax.map(
        attend_block,
        (
            query.reshape(per_device, BLK, width),
            grad_out.reshape(per_device, BLK, width),
            tile_keys,
            tile_values,
        ),
    )
    tile_gkeys = tile_gkeys.reshape(per_device, -1, BLK, width)
    tile_gvalues = tile_gvalues.reshape(per_device, -1, BLK, width)
    window_gkeys = tile_gkeys[:, 1:3]
    window_gvalues = tile_gvalues[:, 1:3]
    global_gkeys = tile_gkeys[:, 3 : 3 + G]
    global_gvalues = tile_gvalues[:, 3 : 3 + G]
    back_keys = []
    back_values = []
    back_keys.append(window_gkeys)
    back_values.append(window_gvalues)
    back_keys.append(global_gkeys)
    back_values.append(global_gvalues)
    back_keys.append(tile_gkeys[:, 3 + G :])
    back_values.append(tile_gvalues[:, 3 + G :])
    back_keys = jnp.concatenate(back_keys, axis=1).reshape(1, fetched, devices, row_share, width)
    back_values = jnp.concatenate(back_values, axis=1).reshape(
        1, fetched, devices, row_share, width
    )
    recv_keys, recv_values = (
        lax.all_to_all(back_keys, "seq", split_axis=2, concat_axis=0, tiled=True),
        lax.all_to_all(back_values, "seq", split_axis=2, concat_axis=0, tiled=True),
    )
    flat_index = fetch_lists.reshape(-1)
    table_keys = (
        jnp.zeros((total_blocks, row_share, width), jnp.float32)
        .at[flat_index]
        .add(recv_keys.reshape(devices * fetched, row_share, width))
    )
    table_values = (
        jnp.zeros((total_blocks, row_share, width), jnp.float32)
        .at[flat_index]
        .add(recv_values.reshape(devices * fetched, row_share, width))
    )
    home_keys, home_values = (
        lax.all_to_all(
            table_keys.reshape(total_blocks, 1, row_share, width),
            "seq",
            split_axis=0,
            concat_axis=1,
            tiled=True,
        ),
        lax.all_to_all(
            table_values.reshape(total_blocks, 1, row_share, width),
            "seq",
            split_axis=0,
            concat_axis=1,
            tiled=True,
        ),
    )
    grad_key_blocks = tile_gkeys[:, 0] + home_keys.reshape(per_device, BLK, width)
    grad_value_blocks = tile_gvalues[:, 0] + home_values.reshape(per_device, BLK, width)
    return (
        attended.reshape(tok_rows, width),
        grad_query.reshape(tok_rows, width),
        grad_key_blocks.astype(jnp.bfloat16).reshape(tok_rows, width),
        grad_value_blocks.astype(jnp.bfloat16).reshape(tok_rows, width),
    )

SLOTS = 3 + G + 3


def _send(v, pairs):
    return lax.ppermute(v.astype(jnp.bfloat16), "seq", pairs).astype(v.dtype)


def gather_blocks(x, n):
    line_len = n // 4
    z = lax.axis_index("seq") // 4
    y_swap = [(i, i ^ 2) for i in range(n)]
    other_own = _send(x, y_swap)
    ups, downs = [], []
    up, down = x, x
    for k in range(1, line_len):
        up = _send(
            up, [(4 * z0 + r, 4 * (z0 + 1) + r) for z0 in range(k - 1, line_len - 1) for r in range(4)]
        )
        down = _send(
            down, [(4 * z0 + r, 4 * (z0 - 1) + r) for z0 in range(1, line_len - k + 1) for r in range(4)]
        )
        ups.append(up)
        downs.append(down)
    rest = lax.dynamic_slice_in_dim(
        jnp.stack(ups[::-1] + downs), line_len - 1 - z, line_len - 1, axis=0
    )
    mine = jnp.concatenate([x[None], rest])
    other = jnp.concatenate([other_own[None], _send(rest, y_swap)])
    pair = jnp.stack([mine, other])
    sibling = _send(pair, [(i, i ^ 1) for i in range(n)])
    return jnp.stack([pair, sibling])


def _attend_kernel(pos_ref, q_ref, g_ref, *refs):
    k_refs = refs[:SLOTS]
    v_refs = refs[SLOTS : 2 * SLOTS]
    att_ref, gq_ref, part_ref = refs[2 * SLOTS :]
    scale = HD ** (-0.5)
    nt = (((1,), (1,)), ((), ()))
    q = q_ref[...]
    g = g_ref[...]
    k_all = jnp.concatenate([r[...] for r in k_refs], axis=0)
    v_all = jnp.concatenate([r[...] for r in v_refs], axis=0)
    s = lax.dot_general(q, k_all, nt, preferred_element_type=jnp.float32) * scale
    e = jnp.exp(s - jnp.max(s, axis=-1, keepdims=True))
    p = e / jnp.sum(e, axis=-1, keepdims=True)
    w = p.astype(jnp.bfloat16)
    att = jnp.dot(w, v_all, preferred_element_type=jnp.float32).astype(jnp.bfloat16)
    att_ref[...] = att
    delta = jnp.sum(g.astype(jnp.float32) * att.astype(jnp.float32), axis=-1, keepdims=True)
    gp = lax.dot_general(g, v_all, nt, preferred_element_type=jnp.float32)
    gs32 = p * (gp - delta)
    gs = gs32.astype(jnp.bfloat16)
    gq_ref[...] = (jnp.dot(gs, k_all, preferred_element_type=jnp.float32) * scale).astype(
        jnp.bfloat16
    )
    gk = jnp.dot(gs32.T.astype(jnp.bfloat16), q, preferred_element_type=jnp.float32) * scale
    gv = jnp.dot(p.T.astype(jnp.bfloat16), g, preferred_element_type=jnp.float32)
    part_ref[...] = jnp.zeros(part_ref.shape, jnp.float32)
    rows = q.shape[0]
    for j in range(SLOTS):
        at = pos_ref[j]
        part_ref[at, 0] = part_ref[at, 0] + gk[j * rows : (j + 1) * rows]
        part_ref[at, 1] = part_ref[at, 1] + gv[j * rows : (j + 1) * rows]


def attend_local(pos, query, grad_out, kv_local):
    rows, width = query.shape
    held = kv_local.shape[0] // 2
    heads = width // HD
    head_spec = pl.BlockSpec((rows, HD), lambda h, pos: (0, h))
    key_specs = [
        pl.BlockSpec((None, rows, HD), lambda h, pos, j=j: (2 * pos[j], 0, h)) for j in range(SLOTS)
    ]
    value_specs = [
        pl.BlockSpec((None, rows, HD), lambda h, pos, j=j: (2 * pos[j] + 1, 0, h))
        for j in range(SLOTS)
    ]
    part_spec = pl.BlockSpec((held, 2, rows, HD), lambda h, pos: (0, 0, 0, h))
    flops = 12 * rows * SLOTS * rows * HD * heads
    moved = 2 * SLOTS * rows * width * 2 + 4 * rows * width * 2 + 2 * held * rows * width * 4
    call = pl.pallas_call(
        _attend_kernel,
        out_shape=(
            jax.ShapeDtypeStruct((rows, width), jnp.bfloat16),
            jax.ShapeDtypeStruct((rows, width), jnp.bfloat16),
            jax.ShapeDtypeStruct((held, 2, rows, width), jnp.float32),
        ),
        grid_spec=pltpu.PrefetchScalarGridSpec(
            num_scalar_prefetch=1,
            grid=(heads,),
            in_specs=[head_spec, head_spec] + key_specs + value_specs,
            out_specs=(head_spec, head_spec, part_spec),
        ),
        compiler_params=pltpu.CompilerParams(dimension_semantics=("arbitrary",)),
        cost_estimate=pl.CostEstimate(
            flops=flops, transcendentals=rows * SLOTS * rows * heads, bytes_accessed=moved
        ),
    )
    return call(pos, query, grad_out, *([kv_local] * (2 * SLOTS)))


STREAMS = 2


def _stream(pos, query, grad_out, keys, values, after=None):
    n = lax.axis_size("seq")
    rows, width = query.shape
    line_len = n // 4
    both = jnp.stack([keys, values])
    if after is not None:
        both, _ = lax.optimization_barrier((both, after))
    kv_local = gather_blocks(both, n).reshape(2 * n, rows, width)
    attended, grad_query, parts = attend_local(pos, query, grad_out, kv_local)
    scatter = jax.linear_transpose(
        lambda t: gather_blocks(t, n), jax.ShapeDtypeStruct((2, rows, width), jnp.float32)
    )
    (grads,) = scatter(parts.reshape(2, 2, line_len, 2, rows, width))
    grads = grads.astype(jnp.bfloat16)
    return (attended, grad_query, grads[0], grads[1]), kv_local


def shards_gather(query, keys, values, grad_out, global_blocks, random_blocks):
    n = lax.axis_size("seq")
    rows, width = query.shape
    line_len = n // 4
    idx = lax.axis_index("seq")
    listed = jnp.concatenate(
        [
            jnp.stack([idx, (idx - 1) % n, (idx + 1) % n]).astype(jnp.int32),
            global_blocks.astype(jnp.int32),
            random_blocks[idx].astype(jnp.int32),
        ]
    )
    listed = jnp.clip(listed, 0, n - 1)
    core = idx % 2
    ypos = (idx // 2) % 2
    zpos = idx // 4
    plane = listed // 4
    in_line = jnp.where(plane == zpos, 0, jnp.where(plane < zpos, plane + 1, plane))
    pos = (((listed % 2) ^ core) * 2 + (((listed // 2) % 2) ^ ypos)) * line_len + in_line
    cut = width // STREAMS
    outs = []
    after = None
    for s in range(STREAMS):
        cols = slice(s * cut, (s + 1) * cut)
        with jax.named_scope(f"stream{s}"):
            out, after = _stream(
                pos, query[:, cols], grad_out[:, cols], keys[:, cols], values[:, cols], after
            )
            outs.append(out)
    return tuple(jnp.concatenate(parts, axis=1) for parts in zip(*outs))


def shards(query, keys, values, grad_out, global_blocks, random_blocks):
    n = lax.axis_size("seq")
    if query.shape[0] == BLK and n % 4 == 0 and n <= 32:
        return shards_gather(query, keys, values, grad_out, global_blocks, random_blocks)
    return shards_exchange(query, keys, values, grad_out, global_blocks, random_blocks)


def solution(mesh):
    placed = (
        P(("groups", "seq"), None),
        P(("groups", "seq"), None),
        P(("groups", "seq"), None),
        P(("groups", "seq"), None),
        P("groups"),
        P("groups", None),
    )
    return jax.shard_map(
        shards,
        mesh=mesh,
        in_specs=placed,
        out_specs=(
            P(("groups", "seq"), None),
            P(("groups", "seq"), None),
            P(("groups", "seq"), None),
            P(("groups", "seq"), None),
        ),
        check_vma=False,
    )
```

```python
import jax
import jax.numpy as jnp
from jax import lax
from jax.experimental import pallas as pl
from jax.experimental.pallas import tpu as pltpu
from jax.sharding import PartitionSpec as P

HD = 128
BLK = 128
G = 2


def attend_block(operands):
    query_blk, grad_blk, key_tiles, value_tiles = operands
    row_count, width = query_blk.shape
    keys_total = key_tiles.shape[0]
    head_size = HD
    head_count = width // head_size
    scaling = HD ** (-0.5)
    last_dims = (((1,), (1,)), ((), ()))
    first_dims = (((0,), (0,)), ((), ()))

    def one_head(head, carry):
        out_attended, out_gquery, out_gkeys, out_gvalues = carry
        start = head * head_size
        query_head = lax.dynamic_slice_in_dim(query_blk, start, head_size, 1)
        grad_head = lax.dynamic_slice_in_dim(grad_blk, start, head_size, 1)
        key_head = lax.dynamic_slice_in_dim(key_tiles, start, head_size, 1)
        value_head = lax.dynamic_slice_in_dim(value_tiles, start, head_size, 1)
        scores = (
            lax.dot_general(query_head, key_head, last_dims, preferred_element_type=jnp.float32)
            * scaling
        )
        probability = jax.nn.softmax(scores, axis=-1)
        weights = probability.astype(jnp.bfloat16)
        attended_head = jnp.dot(weights, value_head, preferred_element_type=jnp.float32).astype(
            jnp.bfloat16
        )
        deltas = jnp.sum(grad_head.astype(jnp.float32) * attended_head.astype(jnp.float32), axis=-1)
        grad_prob = lax.dot_general(
            grad_head, value_head, last_dims, preferred_element_type=jnp.float32
        )
        grad_score = (probability * (grad_prob - deltas[:, None])).astype(jnp.bfloat16)
        gquery_head = (
            jnp.dot(grad_score, key_head, preferred_element_type=jnp.float32) * scaling
        ).astype(jnp.bfloat16)
        gkeys_head = (
            lax.dot_general(grad_score, query_head, first_dims, preferred_element_type=jnp.float32)
            * scaling
        )
        gvalues_head = lax.dot_general(
            weights, grad_head, first_dims, preferred_element_type=jnp.float32
        )
        out_attended = lax.dynamic_update_slice_in_dim(out_attended, attended_head, start, 1)
        out_gquery = lax.dynamic_update_slice_in_dim(out_gquery, gquery_head, start, 1)
        out_gkeys = lax.dynamic_update_slice_in_dim(out_gkeys, gkeys_head, start, 1)
        out_gvalues = lax.dynamic_update_slice_in_dim(out_gvalues, gvalues_head, start, 1)
        return (out_attended, out_gquery, out_gkeys, out_gvalues)

    initial = (
        jnp.zeros((row_count, width), jnp.bfloat16),
        jnp.zeros((row_count, width), jnp.bfloat16),
        jnp.zeros((keys_total, width), jnp.float32),
        jnp.zeros((keys_total, width), jnp.float32),
    )
    return lax.fori_loop(0, head_count, one_head, initial)


def fetch_table(device_ids, block_count, total_blocks, global_blocks, random_blocks):
    owned_blocks = (
        device_ids[:, None] * block_count + jnp.arange(block_count, dtype=jnp.int32)[None, :]
    )
    pieces = []
    pieces.append(((owned_blocks - 1) % total_blocks)[:, :, None])
    pieces.append(((owned_blocks + 1) % total_blocks)[:, :, None])
    pieces.append(
        jnp.broadcast_to(
            global_blocks[None, None, :], owned_blocks.shape + (global_blocks.shape[0],)
        )
    )
    pieces.append(random_blocks[owned_blocks])
    return jnp.concatenate(pieces, axis=2).reshape(device_ids.shape[0], -1)


def shards_exchange(query, keys, values, grad_out, global_blocks, random_blocks):
    devices = lax.axis_size("seq")
    tok_rows, width = query.shape
    per_device = tok_rows // BLK
    total_blocks = per_device * devices
    row_share = BLK // devices
    key_blocks = keys.reshape(per_device, BLK, width)
    value_blocks = values.reshape(per_device, BLK, width)
    row_keys, row_values = (
        lax.all_to_all(
            keys.reshape(per_device, devices, row_share, width),
            "seq",
            split_axis=1,
            concat_axis=0,
            tiled=True,
        ),
        lax.all_to_all(
            values.reshape(per_device, devices, row_share, width),
            "seq",
            split_axis=1,
            concat_axis=0,
            tiled=True,
        ),
    )
    row_keys = row_keys.reshape(total_blocks, row_share, width)
    row_values = row_values.reshape(total_blocks, row_share, width)
    fetch_lists = fetch_table(
        jnp.arange(devices, dtype=jnp.int32), per_device, total_blocks, global_blocks, random_blocks
    )
    fetched = fetch_lists.shape[1]
    got_keys, got_values = (
        lax.all_to_all(row_keys[fetch_lists], "seq", split_axis=0, concat_axis=2, tiled=True),
        lax.all_to_all(row_values[fetch_lists], "seq", split_axis=0, concat_axis=2, tiled=True),
    )
    offset = 0
    window_keys = got_keys[:, 0:2]
    window_values = got_values[:, 0:2]
    offset = 2
    global_keys = got_keys[:, offset : offset + G]
    global_values = got_values[:, offset : offset + G]
    offset = offset + G
    random_keys = got_keys[:, offset:]
    random_values = got_values[:, offset:]
    tile_keys = jnp.concatenate(
        [key_blocks[:, None], window_keys, global_keys, random_keys], axis=1
    ).reshape(per_device, -1, width)
    tile_values = jnp.concatenate(
        [value_blocks[:, None], window_values, global_values, random_values], axis=1
    ).reshape(per_device, -1, width)
    attended, grad_query, tile_gkeys, tile_gvalues = lax.map(
        attend_block,
        (
            query.reshape(per_device, BLK, width),
            grad_out.reshape(per_device, BLK, width),
            tile_keys,
            tile_values,
        ),
    )
    tile_gkeys = tile_gkeys.reshape(per_device, -1, BLK, width)
    tile_gvalues = tile_gvalues.reshape(per_device, -1, BLK, width)
    window_gkeys = tile_gkeys[:, 1:3]
    window_gvalues = tile_gvalues[:, 1:3]
    global_gkeys = tile_gkeys[:, 3 : 3 + G]
    global_gvalues = tile_gvalues[:, 3 : 3 + G]
    back_keys = []
    back_values = []
    back_keys.append(window_gkeys)
    back_values.append(window_gvalues)
    back_keys.append(global_gkeys)
    back_values.append(global_gvalues)
    back_keys.append(tile_gkeys[:, 3 + G :])
    back_values.append(tile_gvalues[:, 3 + G :])
    back_keys = jnp.concatenate(back_keys, axis=1).reshape(1, fetched, devices, row_share, width)
    back_values = jnp.concatenate(back_values, axis=1).reshape(
        1, fetched, devices, row_share, width
    )
    recv_keys, recv_values = (
        lax.all_to_all(back_keys, "seq", split_axis=2, concat_axis=0, tiled=True),
        lax.all_to_all(back_values, "seq", split_axis=2, concat_axis=0, tiled=True),
    )
    flat_index = fetch_lists.reshape(-1)
    table_keys = (
        jnp.zeros((total_blocks, row_share, width), jnp.float32)
        .at[flat_index]
        .add(recv_keys.reshape(devices * fetched, row_share, width))
    )
    table_values = (
        jnp.zeros((total_blocks, row_share, width), jnp.float32)
        .at[flat_index]
        .add(recv_values.reshape(devices * fetched, row_share, width))
    )
    home_keys, home_values = (
        lax.all_to_all(
            table_keys.reshape(total_blocks, 1, row_share, width),
            "seq",
            split_axis=0,
            concat_axis=1,
            tiled=True,
        ),
        lax.all_to_all(
            table_values.reshape(total_blocks, 1, row_share, width),
            "seq",
            split_axis=0,
            concat_axis=1,
            tiled=True,
        ),
    )
    grad_key_blocks = tile_gkeys[:, 0] + home_keys.reshape(per_device, BLK, width)
    grad_value_blocks = tile_gvalues[:, 0] + home_values.reshape(per_device, BLK, width)
    return (
        attended.reshape(tok_rows, width),
        grad_query.reshape(tok_rows, width),
        grad_key_blocks.astype(jnp.bfloat16).reshape(tok_rows, width),
        grad_value_blocks.astype(jnp.bfloat16).reshape(tok_rows, width),
    )

SLOTS = 3 + G + 3


def _send(v, pairs):
    return lax.ppermute(v.astype(jnp.bfloat16), "seq", pairs).astype(v.dtype)


def _line(x, n):
    line_len = n // 4
    z = lax.axis_index("seq") // 4
    ups, downs = [], []
    up, down = x, x
    for k in range(1, line_len):
        up = _send(
            up, [(4 * z0 + r, 4 * (z0 + 1) + r) for z0 in range(k - 1, line_len - 1) for r in range(4)]
        )
        down = _send(
            down, [(4 * z0 + r, 4 * (z0 - 1) + r) for z0 in range(1, line_len - k + 1) for r in range(4)]
        )
        ups.append(up)
        downs.append(down)
    rel = jnp.stack(ups[::-1] + [x] + downs)
    return lax.dynamic_slice_in_dim(rel, line_len - 1 - z, line_len, axis=0)


def _z_then_y(x, n):
    line = _line(x, n)
    pair = jnp.stack([line, _send(line, [(i, i ^ 2) for i in range(n)])])
    return jnp.stack([pair, _send(pair, [(i, i ^ 1) for i in range(n)])])


def _y_then_z(x, n):
    both = jnp.stack([x, _send(x, [(i, i ^ 2) for i in range(n)])])
    pair = jnp.moveaxis(_line(both, n), 1, 0)
    return jnp.stack([pair, _send(pair, [(i, i ^ 1) for i in range(n)])])


Y_FIRST_HEADS = 6


def gather_blocks(x, n):
    split = x.shape[-1] - Y_FIRST_HEADS * HD
    return jnp.concatenate(
        [_z_then_y(x[..., :split], n), _y_then_z(x[..., split:], n)], axis=-1
    )


def _attend_kernel(pos_ref, q_ref, g_ref, *refs):
    k_refs = refs[:SLOTS]
    v_refs = refs[SLOTS : 2 * SLOTS]
    att_ref, gq_ref, part_ref = refs[2 * SLOTS :]
    scale = HD ** (-0.5)
    nt = (((1,), (1,)), ((), ()))
    q = q_ref[...]
    g = g_ref[...]
    k_all = jnp.concatenate([r[...] for r in k_refs], axis=0)
    v_all = jnp.concatenate([r[...] for r in v_refs], axis=0)
    s = lax.dot_general(q, k_all, nt, preferred_element_type=jnp.float32) * scale
    e = jnp.exp(s - jnp.max(s, axis=-1, keepdims=True))
    p = e / jnp.sum(e, axis=-1, keepdims=True)
    w = p.astype(jnp.bfloat16)
    att = jnp.dot(w, v_all, preferred_element_type=jnp.float32).astype(jnp.bfloat16)
    att_ref[...] = att
    delta = jnp.sum(g.astype(jnp.float32) * att.astype(jnp.float32), axis=-1, keepdims=True)
    gp = lax.dot_general(g, v_all, nt, preferred_element_type=jnp.float32)
    gs32 = p * (gp - delta)
    gs = gs32.astype(jnp.bfloat16)
    gq_ref[...] = (jnp.dot(gs, k_all, preferred_element_type=jnp.float32) * scale).astype(
        jnp.bfloat16
    )
    gk = jnp.dot(gs32.T.astype(jnp.bfloat16), q, preferred_element_type=jnp.float32) * scale
    gv = jnp.dot(p.T.astype(jnp.bfloat16), g, preferred_element_type=jnp.float32)
    part_ref[...] = jnp.zeros(part_ref.shape, jnp.float32)
    rows = q.shape[0]
    for j in range(SLOTS):
        at = pos_ref[j]
        part_ref[at, 0] = part_ref[at, 0] + gk[j * rows : (j + 1) * rows]
        part_ref[at, 1] = part_ref[at, 1] + gv[j * rows : (j + 1) * rows]


def attend_local(pos, query, grad_out, kv_local):
    rows, width = query.shape
    held = kv_local.shape[0] // 2
    heads = width // HD
    head_spec = pl.BlockSpec((rows, HD), lambda h, pos: (0, h))
    key_specs = [
        pl.BlockSpec((None, rows, HD), lambda h, pos, j=j: (2 * pos[j], 0, h)) for j in range(SLOTS)
    ]
    value_specs = [
        pl.BlockSpec((None, rows, HD), lambda h, pos, j=j: (2 * pos[j] + 1, 0, h))
        for j in range(SLOTS)
    ]
    part_spec = pl.BlockSpec((held, 2, rows, HD), lambda h, pos: (0, 0, 0, h))
    flops = 12 * rows * SLOTS * rows * HD * heads
    moved = 2 * SLOTS * rows * width * 2 + 4 * rows * width * 2 + 2 * held * rows * width * 4
    call = pl.pallas_call(
        _attend_kernel,
        out_shape=(
            jax.ShapeDtypeStruct((rows, width), jnp.bfloat16),
            jax.ShapeDtypeStruct((rows, width), jnp.bfloat16),
            jax.ShapeDtypeStruct((held, 2, rows, width), jnp.float32),
        ),
        grid_spec=pltpu.PrefetchScalarGridSpec(
            num_scalar_prefetch=1,
            grid=(heads,),
            in_specs=[head_spec, head_spec] + key_specs + value_specs,
            out_specs=(head_spec, head_spec, part_spec),
        ),
        compiler_params=pltpu.CompilerParams(dimension_semantics=("arbitrary",)),
        cost_estimate=pl.CostEstimate(
            flops=flops, transcendentals=rows * SLOTS * rows * heads, bytes_accessed=moved
        ),
    )
    return call(pos, query, grad_out, *([kv_local] * (2 * SLOTS)))


STREAMS = 1


def _stream(pos, query, grad_out, keys, values, after=None):
    n = lax.axis_size("seq")
    rows, width = query.shape
    line_len = n // 4
    both = jnp.stack([keys, values])
    if after is not None:
        both, _ = lax.optimization_barrier((both, after))
    kv_local = gather_blocks(both, n).reshape(2 * n, rows, width)
    attended, grad_query, parts = attend_local(pos, query, grad_out, kv_local)
    scatter = jax.linear_transpose(
        lambda t: gather_blocks(t, n), jax.ShapeDtypeStruct((2, rows, width), jnp.float32)
    )
    (grads,) = scatter(parts.reshape(2, 2, line_len, 2, rows, width))
    grads = grads.astype(jnp.bfloat16)
    return (attended, grad_query, grads[0], grads[1]), kv_local


def shards_gather(query, keys, values, grad_out, global_blocks, random_blocks):
    n = lax.axis_size("seq")
    rows, width = query.shape
    line_len = n // 4
    idx = lax.axis_index("seq")
    listed = jnp.concatenate(
        [
            jnp.stack([idx, (idx - 1) % n, (idx + 1) % n]).astype(jnp.int32),
            global_blocks.astype(jnp.int32),
            random_blocks[idx].astype(jnp.int32),
        ]
    )
    listed = jnp.clip(listed, 0, n - 1)
    core = idx % 2
    ypos = (idx // 2) % 2
    pos = (((listed % 2) ^ core) * 2 + (((listed // 2) % 2) ^ ypos)) * line_len + listed // 4
    cut = width // STREAMS
    outs = []
    after = None
    for s in range(STREAMS):
        cols = slice(s * cut, (s + 1) * cut)
        with jax.named_scope(f"stream{s}"):
            out, after = _stream(
                pos, query[:, cols], grad_out[:, cols], keys[:, cols], values[:, cols], after
            )
            outs.append(out)
    return tuple(jnp.concatenate(parts, axis=1) for parts in zip(*outs))


def shards(query, keys, values, grad_out, global_blocks, random_blocks):
    n = lax.axis_size("seq")
    if query.shape[0] == BLK and n % 4 == 0 and n <= 32:
        return shards_gather(query, keys, values, grad_out, global_blocks, random_blocks)
    return shards_exchange(query, keys, values, grad_out, global_blocks, random_blocks)


def solution(mesh):
    placed = (
        P(("groups", "seq"), None),
        P(("groups", "seq"), None),
        P(("groups", "seq"), None),
        P(("groups", "seq"), None),
        P("groups"),
        P("groups", None),
    )
    return jax.shard_map(
        shards,
        mesh=mesh,
        in_specs=placed,
        out_specs=(
            P(("groups", "seq"), None),
            P(("groups", "seq"), None),
            P(("groups", "seq"), None),
            P(("groups", "seq"), None),
        ),
        check_vma=False,
    )
```

```python
import jax
import jax.numpy as jnp
from jax import lax
from jax.experimental import pallas as pl
from jax.experimental.pallas import tpu as pltpu
from jax.sharding import PartitionSpec as P

HD = 128
BLK = 128
G = 2


def attend_block(operands):
    query_blk, grad_blk, key_tiles, value_tiles = operands
    row_count, width = query_blk.shape
    keys_total = key_tiles.shape[0]
    head_size = HD
    head_count = width // head_size
    scaling = HD ** (-0.5)
    last_dims = (((1,), (1,)), ((), ()))
    first_dims = (((0,), (0,)), ((), ()))

    def one_head(head, carry):
        out_attended, out_gquery, out_gkeys, out_gvalues = carry
        start = head * head_size
        query_head = lax.dynamic_slice_in_dim(query_blk, start, head_size, 1)
        grad_head = lax.dynamic_slice_in_dim(grad_blk, start, head_size, 1)
        key_head = lax.dynamic_slice_in_dim(key_tiles, start, head_size, 1)
        value_head = lax.dynamic_slice_in_dim(value_tiles, start, head_size, 1)
        scores = (
            lax.dot_general(query_head, key_head, last_dims, preferred_element_type=jnp.float32)
            * scaling
        )
        probability = jax.nn.softmax(scores, axis=-1)
        weights = probability.astype(jnp.bfloat16)
        attended_head = jnp.dot(weights, value_head, preferred_element_type=jnp.float32).astype(
            jnp.bfloat16
        )
        deltas = jnp.sum(grad_head.astype(jnp.float32) * attended_head.astype(jnp.float32), axis=-1)
        grad_prob = lax.dot_general(
            grad_head, value_head, last_dims, preferred_element_type=jnp.float32
        )
        grad_score = (probability * (grad_prob - deltas[:, None])).astype(jnp.bfloat16)
        gquery_head = (
            jnp.dot(grad_score, key_head, preferred_element_type=jnp.float32) * scaling
        ).astype(jnp.bfloat16)
        gkeys_head = (
            lax.dot_general(grad_score, query_head, first_dims, preferred_element_type=jnp.float32)
            * scaling
        )
        gvalues_head = lax.dot_general(
            weights, grad_head, first_dims, preferred_element_type=jnp.float32
        )
        out_attended = lax.dynamic_update_slice_in_dim(out_attended, attended_head, start, 1)
        out_gquery = lax.dynamic_update_slice_in_dim(out_gquery, gquery_head, start, 1)
        out_gkeys = lax.dynamic_update_slice_in_dim(out_gkeys, gkeys_head, start, 1)
        out_gvalues = lax.dynamic_update_slice_in_dim(out_gvalues, gvalues_head, start, 1)
        return (out_attended, out_gquery, out_gkeys, out_gvalues)

    initial = (
        jnp.zeros((row_count, width), jnp.bfloat16),
        jnp.zeros((row_count, width), jnp.bfloat16),
        jnp.zeros((keys_total, width), jnp.float32),
        jnp.zeros((keys_total, width), jnp.float32),
    )
    return lax.fori_loop(0, head_count, one_head, initial)


def fetch_table(device_ids, block_count, total_blocks, global_blocks, random_blocks):
    owned_blocks = (
        device_ids[:, None] * block_count + jnp.arange(block_count, dtype=jnp.int32)[None, :]
    )
    pieces = []
    pieces.append(((owned_blocks - 1) % total_blocks)[:, :, None])
    pieces.append(((owned_blocks + 1) % total_blocks)[:, :, None])
    pieces.append(
        jnp.broadcast_to(
            global_blocks[None, None, :], owned_blocks.shape + (global_blocks.shape[0],)
        )
    )
    pieces.append(random_blocks[owned_blocks])
    return jnp.concatenate(pieces, axis=2).reshape(device_ids.shape[0], -1)


def shards_exchange(query, keys, values, grad_out, global_blocks, random_blocks):
    devices = lax.axis_size("seq")
    tok_rows, width = query.shape
    per_device = tok_rows // BLK
    total_blocks = per_device * devices
    row_share = BLK // devices
    key_blocks = keys.reshape(per_device, BLK, width)
    value_blocks = values.reshape(per_device, BLK, width)
    row_keys, row_values = (
        lax.all_to_all(
            keys.reshape(per_device, devices, row_share, width),
            "seq",
            split_axis=1,
            concat_axis=0,
            tiled=True,
        ),
        lax.all_to_all(
            values.reshape(per_device, devices, row_share, width),
            "seq",
            split_axis=1,
            concat_axis=0,
            tiled=True,
        ),
    )
    row_keys = row_keys.reshape(total_blocks, row_share, width)
    row_values = row_values.reshape(total_blocks, row_share, width)
    fetch_lists = fetch_table(
        jnp.arange(devices, dtype=jnp.int32), per_device, total_blocks, global_blocks, random_blocks
    )
    fetched = fetch_lists.shape[1]
    got_keys, got_values = (
        lax.all_to_all(row_keys[fetch_lists], "seq", split_axis=0, concat_axis=2, tiled=True),
        lax.all_to_all(row_values[fetch_lists], "seq", split_axis=0, concat_axis=2, tiled=True),
    )
    offset = 0
    window_keys = got_keys[:, 0:2]
    window_values = got_values[:, 0:2]
    offset = 2
    global_keys = got_keys[:, offset : offset + G]
    global_values = got_values[:, offset : offset + G]
    offset = offset + G
    random_keys = got_keys[:, offset:]
    random_values = got_values[:, offset:]
    tile_keys = jnp.concatenate(
        [key_blocks[:, None], window_keys, global_keys, random_keys], axis=1
    ).reshape(per_device, -1, width)
    tile_values = jnp.concatenate(
        [value_blocks[:, None], window_values, global_values, random_values], axis=1
    ).reshape(per_device, -1, width)
    attended, grad_query, tile_gkeys, tile_gvalues = lax.map(
        attend_block,
        (
            query.reshape(per_device, BLK, width),
            grad_out.reshape(per_device, BLK, width),
            tile_keys,
            tile_values,
        ),
    )
    tile_gkeys = tile_gkeys.reshape(per_device, -1, BLK, width)
    tile_gvalues = tile_gvalues.reshape(per_device, -1, BLK, width)
    window_gkeys = tile_gkeys[:, 1:3]
    window_gvalues = tile_gvalues[:, 1:3]
    global_gkeys = tile_gkeys[:, 3 : 3 + G]
    global_gvalues = tile_gvalues[:, 3 : 3 + G]
    back_keys = []
    back_values = []
    back_keys.append(window_gkeys)
    back_values.append(window_gvalues)
    back_keys.append(global_gkeys)
    back_values.append(global_gvalues)
    back_keys.append(tile_gkeys[:, 3 + G :])
    back_values.append(tile_gvalues[:, 3 + G :])
    back_keys = jnp.concatenate(back_keys, axis=1).reshape(1, fetched, devices, row_share, width)
    back_values = jnp.concatenate(back_values, axis=1).reshape(
        1, fetched, devices, row_share, width
    )
    recv_keys, recv_values = (
        lax.all_to_all(back_keys, "seq", split_axis=2, concat_axis=0, tiled=True),
        lax.all_to_all(back_values, "seq", split_axis=2, concat_axis=0, tiled=True),
    )
    flat_index = fetch_lists.reshape(-1)
    table_keys = (
        jnp.zeros((total_blocks, row_share, width), jnp.float32)
        .at[flat_index]
        .add(recv_keys.reshape(devices * fetched, row_share, width))
    )
    table_values = (
        jnp.zeros((total_blocks, row_share, width), jnp.float32)
        .at[flat_index]
        .add(recv_values.reshape(devices * fetched, row_share, width))
    )
    home_keys, home_values = (
        lax.all_to_all(
            table_keys.reshape(total_blocks, 1, row_share, width),
            "seq",
            split_axis=0,
            concat_axis=1,
            tiled=True,
        ),
        lax.all_to_all(
            table_values.reshape(total_blocks, 1, row_share, width),
            "seq",
            split_axis=0,
            concat_axis=1,
            tiled=True,
        ),
    )
    grad_key_blocks = tile_gkeys[:, 0] + home_keys.reshape(per_device, BLK, width)
    grad_value_blocks = tile_gvalues[:, 0] + home_values.reshape(per_device, BLK, width)
    return (
        attended.reshape(tok_rows, width),
        grad_query.reshape(tok_rows, width),
        grad_key_blocks.astype(jnp.bfloat16).reshape(tok_rows, width),
        grad_value_blocks.astype(jnp.bfloat16).reshape(tok_rows, width),
    )

SLOTS = 3 + G + 3


def _send(v, pairs):
    return lax.ppermute(v.astype(jnp.bfloat16), "seq", pairs).astype(v.dtype)


def _line(x, n):
    line_len = n // 4
    z = lax.axis_index("seq") // 4
    ups, downs = [], []
    up, down = x, x
    for k in range(1, line_len):
        up = _send(
            up, [(4 * z0 + r, 4 * (z0 + 1) + r) for z0 in range(k - 1, line_len - 1) for r in range(4)]
        )
        down = _send(
            down, [(4 * z0 + r, 4 * (z0 - 1) + r) for z0 in range(1, line_len - k + 1) for r in range(4)]
        )
        ups.append(up)
        downs.append(down)
    rel = jnp.stack(ups[::-1] + [x] + downs)
    return lax.dynamic_slice_in_dim(rel, line_len - 1 - z, line_len, axis=0)


Y_FIRST_HEADS = 6


def gather_blocks(x, n):
    split = x.shape[-1] - Y_FIRST_HEADS * HD
    x1, x2 = x[..., :split], x[..., split:]
    y_swap = [(i, i ^ 2) for i in range(n)]
    c_swap = [(i, i ^ 1) for i in range(n)]
    both2 = jnp.stack([x2, _send(x2, y_swap)])
    x1, both2 = lax.optimization_barrier((x1, both2))
    line1 = _line(x1, n)
    line1, both2 = lax.optimization_barrier((line1, both2))
    pair1 = jnp.stack([line1, _send(line1, y_swap)])
    pair2 = jnp.moveaxis(_line(both2, n), 1, 0)
    out1 = jnp.stack([pair1, _send(pair1, c_swap)])
    out2 = jnp.stack([pair2, _send(pair2, c_swap)])
    return jnp.concatenate([out1, out2], axis=-1)


def _attend_kernel(pos_ref, q_ref, g_ref, *refs):
    k_refs = refs[:SLOTS]
    v_refs = refs[SLOTS : 2 * SLOTS]
    att_ref, gq_ref, part_ref = refs[2 * SLOTS :]
    scale = HD ** (-0.5)
    nt = (((1,), (1,)), ((), ()))
    q = q_ref[...]
    g = g_ref[...]
    k_all = jnp.concatenate([r[...] for r in k_refs], axis=0)
    v_all = jnp.concatenate([r[...] for r in v_refs], axis=0)
    s = lax.dot_general(q, k_all, nt, preferred_element_type=jnp.float32) * scale
    e = jnp.exp(s - jnp.max(s, axis=-1, keepdims=True))
    p = e / jnp.sum(e, axis=-1, keepdims=True)
    w = p.astype(jnp.bfloat16)
    att = jnp.dot(w, v_all, preferred_element_type=jnp.float32).astype(jnp.bfloat16)
    att_ref[...] = att
    delta = jnp.sum(g.astype(jnp.float32) * att.astype(jnp.float32), axis=-1, keepdims=True)
    gp = lax.dot_general(g, v_all, nt, preferred_element_type=jnp.float32)
    gs32 = p * (gp - delta)
    gs = gs32.astype(jnp.bfloat16)
    gq_ref[...] = (jnp.dot(gs, k_all, preferred_element_type=jnp.float32) * scale).astype(
        jnp.bfloat16
    )
    gk = jnp.dot(gs32.T.astype(jnp.bfloat16), q, preferred_element_type=jnp.float32) * scale
    gv = jnp.dot(p.T.astype(jnp.bfloat16), g, preferred_element_type=jnp.float32)
    part_ref[...] = jnp.zeros(part_ref.shape, jnp.float32)
    rows = q.shape[0]
    for j in range(SLOTS):
        at = pos_ref[j]
        part_ref[at, 0] = part_ref[at, 0] + gk[j * rows : (j + 1) * rows]
        part_ref[at, 1] = part_ref[at, 1] + gv[j * rows : (j + 1) * rows]


def attend_local(pos, query, grad_out, kv_local):
    rows, width = query.shape
    held = kv_local.shape[0] // 2
    heads = width // HD
    head_spec = pl.BlockSpec((rows, HD), lambda h, pos: (0, h))
    key_specs = [
        pl.BlockSpec((None, rows, HD), lambda h, pos, j=j: (2 * pos[j], 0, h)) for j in range(SLOTS)
    ]
    value_specs = [
        pl.BlockSpec((None, rows, HD), lambda h, pos, j=j: (2 * pos[j] + 1, 0, h))
        for j in range(SLOTS)
    ]
    part_spec = pl.BlockSpec((held, 2, rows, HD), lambda h, pos: (0, 0, 0, h))
    flops = 12 * rows * SLOTS * rows * HD * heads
    moved = 2 * SLOTS * rows * width * 2 + 4 * rows * width * 2 + 2 * held * rows * width * 4
    call = pl.pallas_call(
        _attend_kernel,
        out_shape=(
            jax.ShapeDtypeStruct((rows, width), jnp.bfloat16),
            jax.ShapeDtypeStruct((rows, width), jnp.bfloat16),
            jax.ShapeDtypeStruct((held, 2, rows, width), jnp.float32),
        ),
        grid_spec=pltpu.PrefetchScalarGridSpec(
            num_scalar_prefetch=1,
            grid=(heads,),
            in_specs=[head_spec, head_spec] + key_specs + value_specs,
            out_specs=(head_spec, head_spec, part_spec),
        ),
        compiler_params=pltpu.CompilerParams(dimension_semantics=("arbitrary",)),
        cost_estimate=pl.CostEstimate(
            flops=flops, transcendentals=rows * SLOTS * rows * heads, bytes_accessed=moved
        ),
    )
    return call(pos, query, grad_out, *([kv_local] * (2 * SLOTS)))


STREAMS = 1


def _stream(pos, query, grad_out, keys, values, after=None):
    n = lax.axis_size("seq")
    rows, width = query.shape
    line_len = n // 4
    both = jnp.stack([keys, values])
    if after is not None:
        both, _ = lax.optimization_barrier((both, after))
    kv_local = gather_blocks(both, n).reshape(2 * n, rows, width)
    attended, grad_query, parts = attend_local(pos, query, grad_out, kv_local)
    scatter = jax.linear_transpose(
        lambda t: gather_blocks(t, n), jax.ShapeDtypeStruct((2, rows, width), jnp.float32)
    )
    (grads,) = scatter(parts.reshape(2, 2, line_len, 2, rows, width))
    grads = grads.astype(jnp.bfloat16)
    return (attended, grad_query, grads[0], grads[1]), kv_local


def shards_gather(query, keys, values, grad_out, global_blocks, random_blocks):
    n = lax.axis_size("seq")
    rows, width = query.shape
    line_len = n // 4
    idx = lax.axis_index("seq")
    listed = jnp.concatenate(
        [
            jnp.stack([idx, (idx - 1) % n, (idx + 1) % n]).astype(jnp.int32),
            global_blocks.astype(jnp.int32),
            random_blocks[idx].astype(jnp.int32),
        ]
    )
    listed = jnp.clip(listed, 0, n - 1)
    core = idx % 2
    ypos = (idx // 2) % 2
    pos = (((listed % 2) ^ core) * 2 + (((listed // 2) % 2) ^ ypos)) * line_len + listed // 4
    cut = width // STREAMS
    outs = []
    after = None
    for s in range(STREAMS):
        cols = slice(s * cut, (s + 1) * cut)
        with jax.named_scope(f"stream{s}"):
            out, after = _stream(
                pos, query[:, cols], grad_out[:, cols], keys[:, cols], values[:, cols], after
            )
            outs.append(out)
    return tuple(jnp.concatenate(parts, axis=1) for parts in zip(*outs))


def shards(query, keys, values, grad_out, global_blocks, random_blocks):
    n = lax.axis_size("seq")
    if query.shape[0] == BLK and n % 4 == 0 and n <= 32:
        return shards_gather(query, keys, values, grad_out, global_blocks, random_blocks)
    return shards_exchange(query, keys, values, grad_out, global_blocks, random_blocks)


def solution(mesh):
    placed = (
        P(("groups", "seq"), None),
        P(("groups", "seq"), None),
        P(("groups", "seq"), None),
        P(("groups", "seq"), None),
        P("groups"),
        P("groups", None),
    )
    return jax.shard_map(
        shards,
        mesh=mesh,
        in_specs=placed,
        out_specs=(
            P(("groups", "seq"), None),
            P(("groups", "seq"), None),
            P(("groups", "seq"), None),
            P(("groups", "seq"), None),
        ),
        check_vma=False,
    )
```

```python
import jax
import jax.numpy as jnp
from jax import lax
from jax.experimental import pallas as pl
from jax.experimental.pallas import tpu as pltpu
from jax.sharding import PartitionSpec as P

HD = 128
BLK = 128
G = 2


def attend_block(operands):
    query_blk, grad_blk, key_tiles, value_tiles = operands
    row_count, width = query_blk.shape
    keys_total = key_tiles.shape[0]
    head_size = HD
    head_count = width // head_size
    scaling = HD ** (-0.5)
    last_dims = (((1,), (1,)), ((), ()))
    first_dims = (((0,), (0,)), ((), ()))

    def one_head(head, carry):
        out_attended, out_gquery, out_gkeys, out_gvalues = carry
        start = head * head_size
        query_head = lax.dynamic_slice_in_dim(query_blk, start, head_size, 1)
        grad_head = lax.dynamic_slice_in_dim(grad_blk, start, head_size, 1)
        key_head = lax.dynamic_slice_in_dim(key_tiles, start, head_size, 1)
        value_head = lax.dynamic_slice_in_dim(value_tiles, start, head_size, 1)
        scores = (
            lax.dot_general(query_head, key_head, last_dims, preferred_element_type=jnp.float32)
            * scaling
        )
        probability = jax.nn.softmax(scores, axis=-1)
        weights = probability.astype(jnp.bfloat16)
        attended_head = jnp.dot(weights, value_head, preferred_element_type=jnp.float32).astype(
            jnp.bfloat16
        )
        deltas = jnp.sum(grad_head.astype(jnp.float32) * attended_head.astype(jnp.float32), axis=-1)
        grad_prob = lax.dot_general(
            grad_head, value_head, last_dims, preferred_element_type=jnp.float32
        )
        grad_score = (probability * (grad_prob - deltas[:, None])).astype(jnp.bfloat16)
        gquery_head = (
            jnp.dot(grad_score, key_head, preferred_element_type=jnp.float32) * scaling
        ).astype(jnp.bfloat16)
        gkeys_head = (
            lax.dot_general(grad_score, query_head, first_dims, preferred_element_type=jnp.float32)
            * scaling
        )
        gvalues_head = lax.dot_general(
            weights, grad_head, first_dims, preferred_element_type=jnp.float32
        )
        out_attended = lax.dynamic_update_slice_in_dim(out_attended, attended_head, start, 1)
        out_gquery = lax.dynamic_update_slice_in_dim(out_gquery, gquery_head, start, 1)
        out_gkeys = lax.dynamic_update_slice_in_dim(out_gkeys, gkeys_head, start, 1)
        out_gvalues = lax.dynamic_update_slice_in_dim(out_gvalues, gvalues_head, start, 1)
        return (out_attended, out_gquery, out_gkeys, out_gvalues)

    initial = (
        jnp.zeros((row_count, width), jnp.bfloat16),
        jnp.zeros((row_count, width), jnp.bfloat16),
        jnp.zeros((keys_total, width), jnp.float32),
        jnp.zeros((keys_total, width), jnp.float32),
    )
    return lax.fori_loop(0, head_count, one_head, initial)


def fetch_table(device_ids, block_count, total_blocks, global_blocks, random_blocks):
    owned_blocks = (
        device_ids[:, None] * block_count + jnp.arange(block_count, dtype=jnp.int32)[None, :]
    )
    pieces = []
    pieces.append(((owned_blocks - 1) % total_blocks)[:, :, None])
    pieces.append(((owned_blocks + 1) % total_blocks)[:, :, None])
    pieces.append(
        jnp.broadcast_to(
            global_blocks[None, None, :], owned_blocks.shape + (global_blocks.shape[0],)
        )
    )
    pieces.append(random_blocks[owned_blocks])
    return jnp.concatenate(pieces, axis=2).reshape(device_ids.shape[0], -1)


def shards_exchange(query, keys, values, grad_out, global_blocks, random_blocks):
    devices = lax.axis_size("seq")
    tok_rows, width = query.shape
    per_device = tok_rows // BLK
    total_blocks = per_device * devices
    row_share = BLK // devices
    key_blocks = keys.reshape(per_device, BLK, width)
    value_blocks = values.reshape(per_device, BLK, width)
    row_keys, row_values = (
        lax.all_to_all(
            keys.reshape(per_device, devices, row_share, width),
            "seq",
            split_axis=1,
            concat_axis=0,
            tiled=True,
        ),
        lax.all_to_all(
            values.reshape(per_device, devices, row_share, width),
            "seq",
            split_axis=1,
            concat_axis=0,
            tiled=True,
        ),
    )
    row_keys = row_keys.reshape(total_blocks, row_share, width)
    row_values = row_values.reshape(total_blocks, row_share, width)
    fetch_lists = fetch_table(
        jnp.arange(devices, dtype=jnp.int32), per_device, total_blocks, global_blocks, random_blocks
    )
    fetched = fetch_lists.shape[1]
    got_keys, got_values = (
        lax.all_to_all(row_keys[fetch_lists], "seq", split_axis=0, concat_axis=2, tiled=True),
        lax.all_to_all(row_values[fetch_lists], "seq", split_axis=0, concat_axis=2, tiled=True),
    )
    offset = 0
    window_keys = got_keys[:, 0:2]
    window_values = got_values[:, 0:2]
    offset = 2
    global_keys = got_keys[:, offset : offset + G]
    global_values = got_values[:, offset : offset + G]
    offset = offset + G
    random_keys = got_keys[:, offset:]
    random_values = got_values[:, offset:]
    tile_keys = jnp.concatenate(
        [key_blocks[:, None], window_keys, global_keys, random_keys], axis=1
    ).reshape(per_device, -1, width)
    tile_values = jnp.concatenate(
        [value_blocks[:, None], window_values, global_values, random_values], axis=1
    ).reshape(per_device, -1, width)
    attended, grad_query, tile_gkeys, tile_gvalues = lax.map(
        attend_block,
        (
            query.reshape(per_device, BLK, width),
            grad_out.reshape(per_device, BLK, width),
            tile_keys,
            tile_values,
        ),
    )
    tile_gkeys = tile_gkeys.reshape(per_device, -1, BLK, width)
    tile_gvalues = tile_gvalues.reshape(per_device, -1, BLK, width)
    window_gkeys = tile_gkeys[:, 1:3]
    window_gvalues = tile_gvalues[:, 1:3]
    global_gkeys = tile_gkeys[:, 3 : 3 + G]
    global_gvalues = tile_gvalues[:, 3 : 3 + G]
    back_keys = []
    back_values = []
    back_keys.append(window_gkeys)
    back_values.append(window_gvalues)
    back_keys.append(global_gkeys)
    back_values.append(global_gvalues)
    back_keys.append(tile_gkeys[:, 3 + G :])
    back_values.append(tile_gvalues[:, 3 + G :])
    back_keys = jnp.concatenate(back_keys, axis=1).reshape(1, fetched, devices, row_share, width)
    back_values = jnp.concatenate(back_values, axis=1).reshape(
        1, fetched, devices, row_share, width
    )
    recv_keys, recv_values = (
        lax.all_to_all(back_keys, "seq", split_axis=2, concat_axis=0, tiled=True),
        lax.all_to_all(back_values, "seq", split_axis=2, concat_axis=0, tiled=True),
    )
    flat_index = fetch_lists.reshape(-1)
    table_keys = (
        jnp.zeros((total_blocks, row_share, width), jnp.float32)
        .at[flat_index]
        .add(recv_keys.reshape(devices * fetched, row_share, width))
    )
    table_values = (
        jnp.zeros((total_blocks, row_share, width), jnp.float32)
        .at[flat_index]
        .add(recv_values.reshape(devices * fetched, row_share, width))
    )
    home_keys, home_values = (
        lax.all_to_all(
            table_keys.reshape(total_blocks, 1, row_share, width),
            "seq",
            split_axis=0,
            concat_axis=1,
            tiled=True,
        ),
        lax.all_to_all(
            table_values.reshape(total_blocks, 1, row_share, width),
            "seq",
            split_axis=0,
            concat_axis=1,
            tiled=True,
        ),
    )
    grad_key_blocks = tile_gkeys[:, 0] + home_keys.reshape(per_device, BLK, width)
    grad_value_blocks = tile_gvalues[:, 0] + home_values.reshape(per_device, BLK, width)
    return (
        attended.reshape(tok_rows, width),
        grad_query.reshape(tok_rows, width),
        grad_key_blocks.astype(jnp.bfloat16).reshape(tok_rows, width),
        grad_value_blocks.astype(jnp.bfloat16).reshape(tok_rows, width),
    )

SLOTS = 3 + G + 3


def _send(v, pairs):
    return lax.ppermute(v.astype(jnp.bfloat16), "seq", pairs).astype(v.dtype)


def _line(x, n):
    line_len = n // 4
    z = lax.axis_index("seq") // 4
    ups, downs = [], []
    up, down = x, x
    for k in range(1, line_len):
        up = _send(
            up, [(4 * z0 + r, 4 * (z0 + 1) + r) for z0 in range(k - 1, line_len - 1) for r in range(4)]
        )
        down = _send(
            down, [(4 * z0 + r, 4 * (z0 - 1) + r) for z0 in range(1, line_len - k + 1) for r in range(4)]
        )
        ups.append(up)
        downs.append(down)
    rel = jnp.stack(ups[::-1] + [x] + downs)
    return lax.dynamic_slice_in_dim(rel, line_len - 1 - z, line_len, axis=0)


def gather_blocks(x, n):
    line = _line(x, n)
    pair = jnp.stack([line, _send(line, [(i, i ^ 2) for i in range(n)])])
    return jnp.stack([pair, _send(pair, [(i, i ^ 1) for i in range(n)])])


def _attend_kernel(pos_ref, q_ref, g_ref, *refs):
    k_refs = refs[:SLOTS]
    v_refs = refs[SLOTS : 2 * SLOTS]
    att_ref, gq_ref, part_ref = refs[2 * SLOTS :]
    scale = HD ** (-0.5)
    nt = (((1,), (1,)), ((), ()))
    q = q_ref[...]
    g = g_ref[...]
    k_all = jnp.concatenate([r[...] for r in k_refs], axis=0)
    v_all = jnp.concatenate([r[...] for r in v_refs], axis=0)
    s = lax.dot_general(q, k_all, nt, preferred_element_type=jnp.float32) * scale
    e = jnp.exp(s - jnp.max(s, axis=-1, keepdims=True))
    p = e / jnp.sum(e, axis=-1, keepdims=True)
    w = p.astype(jnp.bfloat16)
    att = jnp.dot(w, v_all, preferred_element_type=jnp.float32).astype(jnp.bfloat16)
    att_ref[...] = att
    delta = jnp.sum(g.astype(jnp.float32) * att.astype(jnp.float32), axis=-1, keepdims=True)
    gp = lax.dot_general(g, v_all, nt, preferred_element_type=jnp.float32)
    gs32 = p * (gp - delta)
    gs = gs32.astype(jnp.bfloat16)
    gq_ref[...] = (jnp.dot(gs, k_all, preferred_element_type=jnp.float32) * scale).astype(
        jnp.bfloat16
    )
    gk = jnp.dot(gs32.T.astype(jnp.bfloat16), q, preferred_element_type=jnp.float32) * scale
    gv = jnp.dot(p.T.astype(jnp.bfloat16), g, preferred_element_type=jnp.float32)
    part_ref[...] = jnp.zeros(part_ref.shape, jnp.float32)
    rows = q.shape[0]
    for j in range(SLOTS):
        at = pos_ref[j]
        part_ref[at, 0] = part_ref[at, 0] + gk[j * rows : (j + 1) * rows]
        part_ref[at, 1] = part_ref[at, 1] + gv[j * rows : (j + 1) * rows]


def attend_local(pos, query, grad_out, kv_local):
    rows, width = query.shape
    held = kv_local.shape[0] // 2
    heads = width // HD
    head_spec = pl.BlockSpec((rows, HD), lambda h, pos: (0, h))
    key_specs = [
        pl.BlockSpec((None, rows, HD), lambda h, pos, j=j: (2 * pos[j], 0, h)) for j in range(SLOTS)
    ]
    value_specs = [
        pl.BlockSpec((None, rows, HD), lambda h, pos, j=j: (2 * pos[j] + 1, 0, h))
        for j in range(SLOTS)
    ]
    part_spec = pl.BlockSpec((held, 2, rows, HD), lambda h, pos: (0, 0, 0, h))
    flops = 12 * rows * SLOTS * rows * HD * heads
    moved = 2 * SLOTS * rows * width * 2 + 4 * rows * width * 2 + 2 * held * rows * width * 4
    call = pl.pallas_call(
        _attend_kernel,
        out_shape=(
            jax.ShapeDtypeStruct((rows, width), jnp.bfloat16),
            jax.ShapeDtypeStruct((rows, width), jnp.bfloat16),
            jax.ShapeDtypeStruct((held, 2, rows, width), jnp.float32),
        ),
        grid_spec=pltpu.PrefetchScalarGridSpec(
            num_scalar_prefetch=1,
            grid=(heads,),
            in_specs=[head_spec, head_spec] + key_specs + value_specs,
            out_specs=(head_spec, head_spec, part_spec),
        ),
        compiler_params=pltpu.CompilerParams(dimension_semantics=("arbitrary",)),
        cost_estimate=pl.CostEstimate(
            flops=flops, transcendentals=rows * SLOTS * rows * heads, bytes_accessed=moved
        ),
    )
    return call(pos, query, grad_out, *([kv_local] * (2 * SLOTS)))


STREAMS = 2


def _stream(pos, query, grad_out, keys, values, after=None):
    n = lax.axis_size("seq")
    rows, width = query.shape
    line_len = n // 4
    both = jnp.stack([keys, values])
    if after is not None:
        both, _ = lax.optimization_barrier((both, after))
    kv_local = gather_blocks(both, n).reshape(2 * n, rows, width)
    attended, grad_query, parts = attend_local(pos, query, grad_out, kv_local)
    scatter = jax.linear_transpose(
        lambda t: gather_blocks(t, n), jax.ShapeDtypeStruct((2, rows, width), jnp.float32)
    )
    (grads,) = scatter(parts.reshape(2, 2, line_len, 2, rows, width))
    grads = grads.astype(jnp.bfloat16)
    return (attended, grad_query, grads[0], grads[1]), kv_local


def shards_gather(query, keys, values, grad_out, global_blocks, random_blocks):
    n = lax.axis_size("seq")
    rows, width = query.shape
    line_len = n // 4
    idx = lax.axis_index("seq")
    listed = jnp.concatenate(
        [
            jnp.stack([idx, (idx - 1) % n, (idx + 1) % n]).astype(jnp.int32),
            global_blocks.astype(jnp.int32),
            random_blocks[idx].astype(jnp.int32),
        ]
    )
    listed = jnp.clip(listed, 0, n - 1)
    core = idx % 2
    ypos = (idx // 2) % 2
    pos = (((listed % 2) ^ core) * 2 + (((listed // 2) % 2) ^ ypos)) * line_len + listed // 4
    cut = width // STREAMS
    outs = []
    after = None
    for s in range(STREAMS):
        cols = slice(s * cut, (s + 1) * cut)
        with jax.named_scope(f"stream{s}"):
            out, after = _stream(
                pos, query[:, cols], grad_out[:, cols], keys[:, cols], values[:, cols], after
            )
            outs.append(out)
    return tuple(jnp.concatenate(parts, axis=1) for parts in zip(*outs))


def shards(query, keys, values, grad_out, global_blocks, random_blocks):
    n = lax.axis_size("seq")
    if query.shape[0] == BLK and n % 4 == 0 and n <= 32:
        return shards_gather(query, keys, values, grad_out, global_blocks, random_blocks)
    return shards_exchange(query, keys, values, grad_out, global_blocks, random_blocks)


def solution(mesh):
    placed = (
        P(("groups", "seq"), None),
        P(("groups", "seq"), None),
        P(("groups", "seq"), None),
        P(("groups", "seq"), None),
        P("groups"),
        P("groups", None),
    )
    return jax.shard_map(
        shards,
        mesh=mesh,
        in_specs=placed,
        out_specs=(
            P(("groups", "seq"), None),
            P(("groups", "seq"), None),
            P(("groups", "seq"), None),
            P(("groups", "seq"), None),
        ),
        check_vma=False,
    )
```

```python
import jax
import jax.numpy as jnp
from jax import lax
from jax.experimental import pallas as pl
from jax.experimental.pallas import tpu as pltpu
from jax.sharding import PartitionSpec as P

HD = 128
BLK = 128
G = 2


def attend_block(operands):
    query_blk, grad_blk, key_tiles, value_tiles = operands
    row_count, width = query_blk.shape
    keys_total = key_tiles.shape[0]
    head_size = HD
    head_count = width // head_size
    scaling = HD ** (-0.5)
    last_dims = (((1,), (1,)), ((), ()))
    first_dims = (((0,), (0,)), ((), ()))

    def one_head(head, carry):
        out_attended, out_gquery, out_gkeys, out_gvalues = carry
        start = head * head_size
        query_head = lax.dynamic_slice_in_dim(query_blk, start, head_size, 1)
        grad_head = lax.dynamic_slice_in_dim(grad_blk, start, head_size, 1)
        key_head = lax.dynamic_slice_in_dim(key_tiles, start, head_size, 1)
        value_head = lax.dynamic_slice_in_dim(value_tiles, start, head_size, 1)
        scores = (
            lax.dot_general(query_head, key_head, last_dims, preferred_element_type=jnp.float32)
            * scaling
        )
        probability = jax.nn.softmax(scores, axis=-1)
        weights = probability.astype(jnp.bfloat16)
        attended_head = jnp.dot(weights, value_head, preferred_element_type=jnp.float32).astype(
            jnp.bfloat16
        )
        deltas = jnp.sum(grad_head.astype(jnp.float32) * attended_head.astype(jnp.float32), axis=-1)
        grad_prob = lax.dot_general(
            grad_head, value_head, last_dims, preferred_element_type=jnp.float32
        )
        grad_score = (probability * (grad_prob - deltas[:, None])).astype(jnp.bfloat16)
        gquery_head = (
            jnp.dot(grad_score, key_head, preferred_element_type=jnp.float32) * scaling
        ).astype(jnp.bfloat16)
        gkeys_head = (
            lax.dot_general(grad_score, query_head, first_dims, preferred_element_type=jnp.float32)
            * scaling
        )
        gvalues_head = lax.dot_general(
            weights, grad_head, first_dims, preferred_element_type=jnp.float32
        )
        out_attended = lax.dynamic_update_slice_in_dim(out_attended, attended_head, start, 1)
        out_gquery = lax.dynamic_update_slice_in_dim(out_gquery, gquery_head, start, 1)
        out_gkeys = lax.dynamic_update_slice_in_dim(out_gkeys, gkeys_head, start, 1)
        out_gvalues = lax.dynamic_update_slice_in_dim(out_gvalues, gvalues_head, start, 1)
        return (out_attended, out_gquery, out_gkeys, out_gvalues)

    initial = (
        jnp.zeros((row_count, width), jnp.bfloat16),
        jnp.zeros((row_count, width), jnp.bfloat16),
        jnp.zeros((keys_total, width), jnp.float32),
        jnp.zeros((keys_total, width), jnp.float32),
    )
    return lax.fori_loop(0, head_count, one_head, initial)


def fetch_table(device_ids, block_count, total_blocks, global_blocks, random_blocks):
    owned_blocks = (
        device_ids[:, None] * block_count + jnp.arange(block_count, dtype=jnp.int32)[None, :]
    )
    pieces = []
    pieces.append(((owned_blocks - 1) % total_blocks)[:, :, None])
    pieces.append(((owned_blocks + 1) % total_blocks)[:, :, None])
    pieces.append(
        jnp.broadcast_to(
            global_blocks[None, None, :], owned_blocks.shape + (global_blocks.shape[0],)
        )
    )
    pieces.append(random_blocks[owned_blocks])
    return jnp.concatenate(pieces, axis=2).reshape(device_ids.shape[0], -1)


def shards_exchange(query, keys, values, grad_out, global_blocks, random_blocks):
    devices = lax.axis_size("seq")
    tok_rows, width = query.shape
    per_device = tok_rows // BLK
    total_blocks = per_device * devices
    row_share = BLK // devices
    key_blocks = keys.reshape(per_device, BLK, width)
    value_blocks = values.reshape(per_device, BLK, width)
    row_keys, row_values = (
        lax.all_to_all(
            keys.reshape(per_device, devices, row_share, width),
            "seq",
            split_axis=1,
            concat_axis=0,
            tiled=True,
        ),
        lax.all_to_all(
            values.reshape(per_device, devices, row_share, width),
            "seq",
            split_axis=1,
            concat_axis=0,
            tiled=True,
        ),
    )
    row_keys = row_keys.reshape(total_blocks, row_share, width)
    row_values = row_values.reshape(total_blocks, row_share, width)
    fetch_lists = fetch_table(
        jnp.arange(devices, dtype=jnp.int32), per_device, total_blocks, global_blocks, random_blocks
    )
    fetched = fetch_lists.shape[1]
    got_keys, got_values = (
        lax.all_to_all(row_keys[fetch_lists], "seq", split_axis=0, concat_axis=2, tiled=True),
        lax.all_to_all(row_values[fetch_lists], "seq", split_axis=0, concat_axis=2, tiled=True),
    )
    offset = 0
    window_keys = got_keys[:, 0:2]
    window_values = got_values[:, 0:2]
    offset = 2
    global_keys = got_keys[:, offset : offset + G]
    global_values = got_values[:, offset : offset + G]
    offset = offset + G
    random_keys = got_keys[:, offset:]
    random_values = got_values[:, offset:]
    tile_keys = jnp.concatenate(
        [key_blocks[:, None], window_keys, global_keys, random_keys], axis=1
    ).reshape(per_device, -1, width)
    tile_values = jnp.concatenate(
        [value_blocks[:, None], window_values, global_values, random_values], axis=1
    ).reshape(per_device, -1, width)
    attended, grad_query, tile_gkeys, tile_gvalues = lax.map(
        attend_block,
        (
            query.reshape(per_device, BLK, width),
            grad_out.reshape(per_device, BLK, width),
            tile_keys,
            tile_values,
        ),
    )
    tile_gkeys = tile_gkeys.reshape(per_device, -1, BLK, width)
    tile_gvalues = tile_gvalues.reshape(per_device, -1, BLK, width)
    window_gkeys = tile_gkeys[:, 1:3]
    window_gvalues = tile_gvalues[:, 1:3]
    global_gkeys = tile_gkeys[:, 3 : 3 + G]
    global_gvalues = tile_gvalues[:, 3 : 3 + G]
    back_keys = []
    back_values = []
    back_keys.append(window_gkeys)
    back_values.append(window_gvalues)
    back_keys.append(global_gkeys)
    back_values.append(global_gvalues)
    back_keys.append(tile_gkeys[:, 3 + G :])
    back_values.append(tile_gvalues[:, 3 + G :])
    back_keys = jnp.concatenate(back_keys, axis=1).reshape(1, fetched, devices, row_share, width)
    back_values = jnp.concatenate(back_values, axis=1).reshape(
        1, fetched, devices, row_share, width
    )
    recv_keys, recv_values = (
        lax.all_to_all(back_keys, "seq", split_axis=2, concat_axis=0, tiled=True),
        lax.all_to_all(back_values, "seq", split_axis=2, concat_axis=0, tiled=True),
    )
    flat_index = fetch_lists.reshape(-1)
    table_keys = (
        jnp.zeros((total_blocks, row_share, width), jnp.float32)
        .at[flat_index]
        .add(recv_keys.reshape(devices * fetched, row_share, width))
    )
    table_values = (
        jnp.zeros((total_blocks, row_share, width), jnp.float32)
        .at[flat_index]
        .add(recv_values.reshape(devices * fetched, row_share, width))
    )
    home_keys, home_values = (
        lax.all_to_all(
            table_keys.reshape(total_blocks, 1, row_share, width),
            "seq",
            split_axis=0,
            concat_axis=1,
            tiled=True,
        ),
        lax.all_to_all(
            table_values.reshape(total_blocks, 1, row_share, width),
            "seq",
            split_axis=0,
            concat_axis=1,
            tiled=True,
        ),
    )
    grad_key_blocks = tile_gkeys[:, 0] + home_keys.reshape(per_device, BLK, width)
    grad_value_blocks = tile_gvalues[:, 0] + home_values.reshape(per_device, BLK, width)
    return (
        attended.reshape(tok_rows, width),
        grad_query.reshape(tok_rows, width),
        grad_key_blocks.astype(jnp.bfloat16).reshape(tok_rows, width),
        grad_value_blocks.astype(jnp.bfloat16).reshape(tok_rows, width),
    )

SLOTS = 3 + G + 3


def _send(v, pairs):
    return lax.ppermute(v.astype(jnp.bfloat16), "seq", pairs).astype(v.dtype)


def gather_blocks(x, n):
    line_len = n // 4
    z = lax.axis_index("seq") // 4
    ups, downs = [], []
    up, down = x, x
    for k in range(1, line_len):
        up = _send(
            up, [(4 * z0 + r, 4 * (z0 + 1) + r) for z0 in range(k - 1, line_len - 1) for r in range(4)]
        )
        down = _send(
            down, [(4 * z0 + r, 4 * (z0 - 1) + r) for z0 in range(1, line_len - k + 1) for r in range(4)]
        )
        ups.append(up)
        downs.append(down)
    rel = jnp.stack(ups[::-1] + [x] + downs)
    line = lax.dynamic_slice_in_dim(rel, line_len - 1 - z, line_len, axis=0)
    other = _send(line, [(i, i ^ 2) for i in range(n)])
    pair = jnp.stack([line, other])
    sibling = _send(pair, [(i, i ^ 1) for i in range(n)])
    return jnp.stack([pair, sibling])


def _attend_kernel(pos_ref, q_ref, g_ref, *refs):
    k_refs = refs[:SLOTS]
    v_refs = refs[SLOTS : 2 * SLOTS]
    att_ref, gq_ref, dk_ref, dv_ref = refs[2 * SLOTS :]
    scale = HD ** (-0.5)
    nt = (((1,), (1,)), ((), ()))
    q = q_ref[...]
    g = g_ref[...]
    k_all = jnp.concatenate([r[...] for r in k_refs], axis=0)
    v_all = jnp.concatenate([r[...] for r in v_refs], axis=0)
    s = lax.dot_general(q, k_all, nt, preferred_element_type=jnp.float32) * scale
    e = jnp.exp(s - jnp.max(s, axis=-1, keepdims=True))
    p = e / jnp.sum(e, axis=-1, keepdims=True)
    w = p.astype(jnp.bfloat16)
    att = jnp.dot(w, v_all, preferred_element_type=jnp.float32).astype(jnp.bfloat16)
    att_ref[...] = att
    delta = jnp.sum(g.astype(jnp.float32) * att.astype(jnp.float32), axis=-1, keepdims=True)
    gp = lax.dot_general(g, v_all, nt, preferred_element_type=jnp.float32)
    gs32 = p * (gp - delta)
    gs = gs32.astype(jnp.bfloat16)
    gq_ref[...] = (jnp.dot(gs, k_all, preferred_element_type=jnp.float32) * scale).astype(
        jnp.bfloat16
    )
    gk = jnp.dot(gs32.T.astype(jnp.bfloat16), q, preferred_element_type=jnp.float32) * scale
    gv = jnp.dot(p.T.astype(jnp.bfloat16), g, preferred_element_type=jnp.float32)
    dk_ref[...] = jnp.zeros(dk_ref.shape, jnp.float32)
    dv_ref[...] = jnp.zeros(dv_ref.shape, jnp.float32)
    rows = q.shape[0]
    for j in range(SLOTS):
        at = pos_ref[j]
        dk_ref[at] = dk_ref[at] + gk[j * rows : (j + 1) * rows]
        dv_ref[at] = dv_ref[at] + gv[j * rows : (j + 1) * rows]


def attend_local(pos, query, grad_out, keys_local, values_local):
    rows, width = query.shape
    held = keys_local.shape[0]
    heads = width // HD
    head_spec = pl.BlockSpec((rows, HD), lambda h, pos: (0, h))
    slot_specs = [
        pl.BlockSpec((None, rows, HD), lambda h, pos, j=j: (pos[j], 0, h)) for j in range(SLOTS)
    ]
    part_spec = pl.BlockSpec((held, rows, HD), lambda h, pos: (0, 0, h))
    flops = 12 * rows * SLOTS * rows * HD * heads
    moved = 2 * SLOTS * rows * width * 2 + 4 * rows * width * 2 + 2 * held * rows * width * 4
    call = pl.pallas_call(
        _attend_kernel,
        out_shape=(
            jax.ShapeDtypeStruct((rows, width), jnp.bfloat16),
            jax.ShapeDtypeStruct((rows, width), jnp.bfloat16),
            jax.ShapeDtypeStruct((held, rows, width), jnp.float32),
            jax.ShapeDtypeStruct((held, rows, width), jnp.float32),
        ),
        grid_spec=pltpu.PrefetchScalarGridSpec(
            num_scalar_prefetch=1,
            grid=(heads,),
            in_specs=[head_spec, head_spec] + slot_specs + slot_specs,
            out_specs=(head_spec, head_spec, part_spec, part_spec),
        ),
        compiler_params=pltpu.CompilerParams(dimension_semantics=("arbitrary",)),
        cost_estimate=pl.CostEstimate(
            flops=flops, transcendentals=rows * SLOTS * rows * heads, bytes_accessed=moved
        ),
    )
    return call(
        pos, query, grad_out, *([keys_local] * SLOTS), *([values_local] * SLOTS)
    )


STREAMS = 2


def _stream(pos, query, grad_out, keys, values, after=None, before_kernel=None):
    n = lax.axis_size("seq")
    rows, width = query.shape
    line_len = n // 4
    if after is not None:
        keys, values, _ = lax.optimization_barrier((keys, values, after))
    keys_local = gather_blocks(keys, n).reshape(n, rows, width)
    values_local = gather_blocks(values, n).reshape(n, rows, width)
    if before_kernel is not None:
        keys_local, values_local, _ = lax.optimization_barrier(
            (keys_local, values_local, before_kernel)
        )
    attended, grad_query, part_keys, part_values = attend_local(
        pos, query, grad_out, keys_local, values_local
    )
    scatter = jax.linear_transpose(
        lambda t: gather_blocks(t, n), jax.ShapeDtypeStruct((rows, width), jnp.float32)
    )
    (grad_keys,) = scatter(part_keys.reshape(2, 2, line_len, rows, width))
    (grad_values,) = scatter(part_values.reshape(2, 2, line_len, rows, width))
    outs = (attended, grad_query, grad_keys.astype(jnp.bfloat16), grad_values.astype(jnp.bfloat16))
    return outs, (attended, outs[2:])


def shards_gather(query, keys, values, grad_out, global_blocks, random_blocks):
    n = lax.axis_size("seq")
    rows, width = query.shape
    line_len = n // 4
    idx = lax.axis_index("seq")
    listed = jnp.concatenate(
        [
            jnp.stack([idx, (idx - 1) % n, (idx + 1) % n]).astype(jnp.int32),
            global_blocks.astype(jnp.int32),
            random_blocks[idx].astype(jnp.int32),
        ]
    )
    listed = jnp.clip(listed, 0, n - 1)
    core = idx % 2
    ypos = (idx // 2) % 2
    pos = (((listed % 2) ^ core) * 2 + (((listed // 2) % 2) ^ ypos)) * line_len + listed // 4
    cut = width // STREAMS
    outs = []
    after = before_kernel = None
    for s in range(STREAMS):
        cols = slice(s * cut, (s + 1) * cut)
        with jax.named_scope(f"stream{s}"):
            out, tie = _stream(
                pos,
                query[:, cols],
                grad_out[:, cols],
                keys[:, cols],
                values[:, cols],
                after,
                before_kernel,
            )
            after, before_kernel = tie
            outs.append(out)
    return tuple(jnp.concatenate(parts, axis=1) for parts in zip(*outs))


def shards(query, keys, values, grad_out, global_blocks, random_blocks):
    n = lax.axis_size("seq")
    if query.shape[0] == BLK and n % 4 == 0 and n <= 32:
        return shards_gather(query, keys, values, grad_out, global_blocks, random_blocks)
    return shards_exchange(query, keys, values, grad_out, global_blocks, random_blocks)


def solution(mesh):
    placed = (
        P(("groups", "seq"), None),
        P(("groups", "seq"), None),
        P(("groups", "seq"), None),
        P(("groups", "seq"), None),
        P("groups"),
        P("groups", None),
    )
    return jax.shard_map(
        shards,
        mesh=mesh,
        in_specs=placed,
        out_specs=(
            P(("groups", "seq"), None),
            P(("groups", "seq"), None),
            P(("groups", "seq"), None),
            P(("groups", "seq"), None),
        ),
        check_vma=False,
    )
```

```python
import jax
import jax.numpy as jnp
from jax import lax
from jax.experimental import pallas as pl
from jax.experimental.pallas import tpu as pltpu
from jax.sharding import PartitionSpec as P

HD = 128
BLK = 128
G = 2


def attend_block(operands):
    query_blk, grad_blk, key_tiles, value_tiles = operands
    row_count, width = query_blk.shape
    keys_total = key_tiles.shape[0]
    head_size = HD
    head_count = width // head_size
    scaling = HD ** (-0.5)
    last_dims = (((1,), (1,)), ((), ()))
    first_dims = (((0,), (0,)), ((), ()))

    def one_head(head, carry):
        out_attended, out_gquery, out_gkeys, out_gvalues = carry
        start = head * head_size
        query_head = lax.dynamic_slice_in_dim(query_blk, start, head_size, 1)
        grad_head = lax.dynamic_slice_in_dim(grad_blk, start, head_size, 1)
        key_head = lax.dynamic_slice_in_dim(key_tiles, start, head_size, 1)
        value_head = lax.dynamic_slice_in_dim(value_tiles, start, head_size, 1)
        scores = (
            lax.dot_general(query_head, key_head, last_dims, preferred_element_type=jnp.float32)
            * scaling
        )
        probability = jax.nn.softmax(scores, axis=-1)
        weights = probability.astype(jnp.bfloat16)
        attended_head = jnp.dot(weights, value_head, preferred_element_type=jnp.float32).astype(
            jnp.bfloat16
        )
        deltas = jnp.sum(grad_head.astype(jnp.float32) * attended_head.astype(jnp.float32), axis=-1)
        grad_prob = lax.dot_general(
            grad_head, value_head, last_dims, preferred_element_type=jnp.float32
        )
        grad_score = (probability * (grad_prob - deltas[:, None])).astype(jnp.bfloat16)
        gquery_head = (
            jnp.dot(grad_score, key_head, preferred_element_type=jnp.float32) * scaling
        ).astype(jnp.bfloat16)
        gkeys_head = (
            lax.dot_general(grad_score, query_head, first_dims, preferred_element_type=jnp.float32)
            * scaling
        )
        gvalues_head = lax.dot_general(
            weights, grad_head, first_dims, preferred_element_type=jnp.float32
        )
        out_attended = lax.dynamic_update_slice_in_dim(out_attended, attended_head, start, 1)
        out_gquery = lax.dynamic_update_slice_in_dim(out_gquery, gquery_head, start, 1)
        out_gkeys = lax.dynamic_update_slice_in_dim(out_gkeys, gkeys_head, start, 1)
        out_gvalues = lax.dynamic_update_slice_in_dim(out_gvalues, gvalues_head, start, 1)
        return (out_attended, out_gquery, out_gkeys, out_gvalues)

    initial = (
        jnp.zeros((row_count, width), jnp.bfloat16),
        jnp.zeros((row_count, width), jnp.bfloat16),
        jnp.zeros((keys_total, width), jnp.float32),
        jnp.zeros((keys_total, width), jnp.float32),
    )
    return lax.fori_loop(0, head_count, one_head, initial)


def fetch_table(device_ids, block_count, total_blocks, global_blocks, random_blocks):
    owned_blocks = (
        device_ids[:, None] * block_count + jnp.arange(block_count, dtype=jnp.int32)[None, :]
    )
    pieces = []
    pieces.append(((owned_blocks - 1) % total_blocks)[:, :, None])
    pieces.append(((owned_blocks + 1) % total_blocks)[:, :, None])
    pieces.append(
        jnp.broadcast_to(
            global_blocks[None, None, :], owned_blocks.shape + (global_blocks.shape[0],)
        )
    )
    pieces.append(random_blocks[owned_blocks])
    return jnp.concatenate(pieces, axis=2).reshape(device_ids.shape[0], -1)


def shards_exchange(query, keys, values, grad_out, global_blocks, random_blocks):
    devices = lax.axis_size("seq")
    tok_rows, width = query.shape
    per_device = tok_rows // BLK
    total_blocks = per_device * devices
    row_share = BLK // devices
    key_blocks = keys.reshape(per_device, BLK, width)
    value_blocks = values.reshape(per_device, BLK, width)
    row_keys, row_values = (
        lax.all_to_all(
            keys.reshape(per_device, devices, row_share, width),
            "seq",
            split_axis=1,
            concat_axis=0,
            tiled=True,
        ),
        lax.all_to_all(
            values.reshape(per_device, devices, row_share, width),
            "seq",
            split_axis=1,
            concat_axis=0,
            tiled=True,
        ),
    )
    row_keys = row_keys.reshape(total_blocks, row_share, width)
    row_values = row_values.reshape(total_blocks, row_share, width)
    fetch_lists = fetch_table(
        jnp.arange(devices, dtype=jnp.int32), per_device, total_blocks, global_blocks, random_blocks
    )
    fetched = fetch_lists.shape[1]
    got_keys, got_values = (
        lax.all_to_all(row_keys[fetch_lists], "seq", split_axis=0, concat_axis=2, tiled=True),
        lax.all_to_all(row_values[fetch_lists], "seq", split_axis=0, concat_axis=2, tiled=True),
    )
    offset = 0
    window_keys = got_keys[:, 0:2]
    window_values = got_values[:, 0:2]
    offset = 2
    global_keys = got_keys[:, offset : offset + G]
    global_values = got_values[:, offset : offset + G]
    offset = offset + G
    random_keys = got_keys[:, offset:]
    random_values = got_values[:, offset:]
    tile_keys = jnp.concatenate(
        [key_blocks[:, None], window_keys, global_keys, random_keys], axis=1
    ).reshape(per_device, -1, width)
    tile_values = jnp.concatenate(
        [value_blocks[:, None], window_values, global_values, random_values], axis=1
    ).reshape(per_device, -1, width)
    attended, grad_query, tile_gkeys, tile_gvalues = lax.map(
        attend_block,
        (
            query.reshape(per_device, BLK, width),
            grad_out.reshape(per_device, BLK, width),
            tile_keys,
            tile_values,
        ),
    )
    tile_gkeys = tile_gkeys.reshape(per_device, -1, BLK, width)
    tile_gvalues = tile_gvalues.reshape(per_device, -1, BLK, width)
    window_gkeys = tile_gkeys[:, 1:3]
    window_gvalues = tile_gvalues[:, 1:3]
    global_gkeys = tile_gkeys[:, 3 : 3 + G]
    global_gvalues = tile_gvalues[:, 3 : 3 + G]
    back_keys = []
    back_values = []
    back_keys.append(window_gkeys)
    back_values.append(window_gvalues)
    back_keys.append(global_gkeys)
    back_values.append(global_gvalues)
    back_keys.append(tile_gkeys[:, 3 + G :])
    back_values.append(tile_gvalues[:, 3 + G :])
    back_keys = jnp.concatenate(back_keys, axis=1).reshape(1, fetched, devices, row_share, width)
    back_values = jnp.concatenate(back_values, axis=1).reshape(
        1, fetched, devices, row_share, width
    )
    recv_keys, recv_values = (
        lax.all_to_all(back_keys, "seq", split_axis=2, concat_axis=0, tiled=True),
        lax.all_to_all(back_values, "seq", split_axis=2, concat_axis=0, tiled=True),
    )
    flat_index = fetch_lists.reshape(-1)
    table_keys = (
        jnp.zeros((total_blocks, row_share, width), jnp.float32)
        .at[flat_index]
        .add(recv_keys.reshape(devices * fetched, row_share, width))
    )
    table_values = (
        jnp.zeros((total_blocks, row_share, width), jnp.float32)
        .at[flat_index]
        .add(recv_values.reshape(devices * fetched, row_share, width))
    )
    home_keys, home_values = (
        lax.all_to_all(
            table_keys.reshape(total_blocks, 1, row_share, width),
            "seq",
            split_axis=0,
            concat_axis=1,
            tiled=True,
        ),
        lax.all_to_all(
            table_values.reshape(total_blocks, 1, row_share, width),
            "seq",
            split_axis=0,
            concat_axis=1,
            tiled=True,
        ),
    )
    grad_key_blocks = tile_gkeys[:, 0] + home_keys.reshape(per_device, BLK, width)
    grad_value_blocks = tile_gvalues[:, 0] + home_values.reshape(per_device, BLK, width)
    return (
        attended.reshape(tok_rows, width),
        grad_query.reshape(tok_rows, width),
        grad_key_blocks.astype(jnp.bfloat16).reshape(tok_rows, width),
        grad_value_blocks.astype(jnp.bfloat16).reshape(tok_rows, width),
    )

SLOTS = 3 + G + 3


def _send(v, pairs):
    return lax.ppermute(v.astype(jnp.bfloat16), "seq", pairs).astype(v.dtype)


def gather_blocks(x, n):
    line_len = n // 4
    z = lax.axis_index("seq") // 4
    ups, downs = [], []
    up, down = x, x
    for k in range(1, line_len):
        up = _send(
            up, [(4 * z0 + r, 4 * (z0 + 1) + r) for z0 in range(k - 1, line_len - 1) for r in range(4)]
        )
        down = _send(
            down, [(4 * z0 + r, 4 * (z0 - 1) + r) for z0 in range(1, line_len - k + 1) for r in range(4)]
        )
        ups.append(up)
        downs.append(down)
    rel = jnp.stack(ups[::-1] + [x] + downs)
    line = lax.dynamic_slice_in_dim(rel, line_len - 1 - z, line_len, axis=0)
    other = _send(line, [(i, i ^ 2) for i in range(n)])
    pair = jnp.stack([line, other])
    sibling = _send(pair, [(i, i ^ 1) for i in range(n)])
    return jnp.stack([pair, sibling])


def _attend_kernel(pos_ref, q_ref, g_ref, *refs):
    k_refs = refs[:SLOTS]
    v_refs = refs[SLOTS : 2 * SLOTS]
    att_ref, gq_ref, dk_ref, dv_ref = refs[2 * SLOTS :]
    scale = HD ** (-0.5)
    nt = (((1,), (1,)), ((), ()))
    q = q_ref[...]
    g = g_ref[...]
    k_all = jnp.concatenate([r[...] for r in k_refs], axis=0)
    v_all = jnp.concatenate([r[...] for r in v_refs], axis=0)
    s = lax.dot_general(q, k_all, nt, preferred_element_type=jnp.float32) * scale
    e = jnp.exp(s - jnp.max(s, axis=-1, keepdims=True))
    p = e / jnp.sum(e, axis=-1, keepdims=True)
    w = p.astype(jnp.bfloat16)
    att = jnp.dot(w, v_all, preferred_element_type=jnp.float32).astype(jnp.bfloat16)
    att_ref[...] = att
    delta = jnp.sum(g.astype(jnp.float32) * att.astype(jnp.float32), axis=-1, keepdims=True)
    gp = lax.dot_general(g, v_all, nt, preferred_element_type=jnp.float32)
    gs32 = p * (gp - delta)
    gs = gs32.astype(jnp.bfloat16)
    gq_ref[...] = (jnp.dot(gs, k_all, preferred_element_type=jnp.float32) * scale).astype(
        jnp.bfloat16
    )
    tn = (((0,), (0,)), ((), ()))
    gk = lax.dot_general(gs, q, tn, preferred_element_type=jnp.float32) * scale
    gv = lax.dot_general(w, g, tn, preferred_element_type=jnp.float32)
    dk_ref[...] = jnp.zeros(dk_ref.shape, jnp.float32)
    dv_ref[...] = jnp.zeros(dv_ref.shape, jnp.float32)
    rows = q.shape[0]
    for j in range(SLOTS):
        at = pos_ref[j]
        dk_ref[at] = dk_ref[at] + gk[j * rows : (j + 1) * rows]
        dv_ref[at] = dv_ref[at] + gv[j * rows : (j + 1) * rows]


def attend_local(pos, query, grad_out, keys_local, values_local):
    rows, width = query.shape
    held = keys_local.shape[0]
    heads = width // HD
    head_spec = pl.BlockSpec((rows, HD), lambda h, pos: (0, h))
    slot_specs = [
        pl.BlockSpec((None, rows, HD), lambda h, pos, j=j: (pos[j], 0, h)) for j in range(SLOTS)
    ]
    part_spec = pl.BlockSpec((held, rows, HD), lambda h, pos: (0, 0, h))
    flops = 12 * rows * SLOTS * rows * HD * heads
    moved = 2 * SLOTS * rows * width * 2 + 4 * rows * width * 2 + 2 * held * rows * width * 4
    call = pl.pallas_call(
        _attend_kernel,
        out_shape=(
            jax.ShapeDtypeStruct((rows, width), jnp.bfloat16),
            jax.ShapeDtypeStruct((rows, width), jnp.bfloat16),
            jax.ShapeDtypeStruct((held, rows, width), jnp.float32),
            jax.ShapeDtypeStruct((held, rows, width), jnp.float32),
        ),
        grid_spec=pltpu.PrefetchScalarGridSpec(
            num_scalar_prefetch=1,
            grid=(heads,),
            in_specs=[head_spec, head_spec] + slot_specs + slot_specs,
            out_specs=(head_spec, head_spec, part_spec, part_spec),
        ),
        compiler_params=pltpu.CompilerParams(dimension_semantics=("arbitrary",)),
        cost_estimate=pl.CostEstimate(
            flops=flops, transcendentals=rows * SLOTS * rows * heads, bytes_accessed=moved
        ),
    )
    return call(
        pos, query, grad_out, *([keys_local] * SLOTS), *([values_local] * SLOTS)
    )


STREAMS = 2


def _stream(pos, query, grad_out, keys, values, after=None):
    n = lax.axis_size("seq")
    rows, width = query.shape
    line_len = n // 4
    if after is not None:
        keys, values, _ = lax.optimization_barrier((keys, values, after))
    keys_local = gather_blocks(keys, n).reshape(n, rows, width)
    values_local = gather_blocks(values, n).reshape(n, rows, width)
    attended, grad_query, part_keys, part_values = attend_local(
        pos, query, grad_out, keys_local, values_local
    )
    scatter = jax.linear_transpose(
        lambda t: gather_blocks(t, n), jax.ShapeDtypeStruct((rows, width), jnp.float32)
    )
    (grad_keys,) = scatter(part_keys.reshape(2, 2, line_len, rows, width))
    (grad_values,) = scatter(part_values.reshape(2, 2, line_len, rows, width))
    outs = (attended, grad_query, grad_keys.astype(jnp.bfloat16), grad_values.astype(jnp.bfloat16))
    return outs, (keys_local, values_local)


def shards_gather(query, keys, values, grad_out, global_blocks, random_blocks):
    n = lax.axis_size("seq")
    rows, width = query.shape
    line_len = n // 4
    idx = lax.axis_index("seq")
    listed = jnp.concatenate(
        [
            jnp.stack([idx, (idx - 1) % n, (idx + 1) % n]).astype(jnp.int32),
            global_blocks.astype(jnp.int32),
            random_blocks[idx].astype(jnp.int32),
        ]
    )
    listed = jnp.clip(listed, 0, n - 1)
    core = idx % 2
    ypos = (idx // 2) % 2
    pos = (((listed % 2) ^ core) * 2 + (((listed // 2) % 2) ^ ypos)) * line_len + listed // 4
    cut = width // STREAMS
    outs = []
    after = None
    for s in range(STREAMS):
        cols = slice(s * cut, (s + 1) * cut)
        with jax.named_scope(f"stream{s}"):
            out, after = _stream(
                pos, query[:, cols], grad_out[:, cols], keys[:, cols], values[:, cols], after
            )
            outs.append(out)
    return tuple(jnp.concatenate(parts, axis=1) for parts in zip(*outs))


def shards(query, keys, values, grad_out, global_blocks, random_blocks):
    n = lax.axis_size("seq")
    if query.shape[0] == BLK and n % 4 == 0 and n <= 32:
        return shards_gather(query, keys, values, grad_out, global_blocks, random_blocks)
    return shards_exchange(query, keys, values, grad_out, global_blocks, random_blocks)


def solution(mesh):
    placed = (
        P(("groups", "seq"), None),
        P(("groups", "seq"), None),
        P(("groups", "seq"), None),
        P(("groups", "seq"), None),
        P("groups"),
        P("groups", None),
    )
    return jax.shard_map(
        shards,
        mesh=mesh,
        in_specs=placed,
        out_specs=(
            P(("groups", "seq"), None),
            P(("groups", "seq"), None),
            P(("groups", "seq"), None),
            P(("groups", "seq"), None),
        ),
        check_vma=False,
    )
```

```python
import jax
import jax.numpy as jnp
from jax import lax
from jax.experimental import pallas as pl
from jax.experimental.pallas import tpu as pltpu
from jax.sharding import PartitionSpec as P

HD = 128
BLK = 128
G = 2


def attend_block(operands):
    query_blk, grad_blk, key_tiles, value_tiles = operands
    row_count, width = query_blk.shape
    keys_total = key_tiles.shape[0]
    head_size = HD
    head_count = width // head_size
    scaling = HD ** (-0.5)
    last_dims = (((1,), (1,)), ((), ()))
    first_dims = (((0,), (0,)), ((), ()))

    def one_head(head, carry):
        out_attended, out_gquery, out_gkeys, out_gvalues = carry
        start = head * head_size
        query_head = lax.dynamic_slice_in_dim(query_blk, start, head_size, 1)
        grad_head = lax.dynamic_slice_in_dim(grad_blk, start, head_size, 1)
        key_head = lax.dynamic_slice_in_dim(key_tiles, start, head_size, 1)
        value_head = lax.dynamic_slice_in_dim(value_tiles, start, head_size, 1)
        scores = (
            lax.dot_general(query_head, key_head, last_dims, preferred_element_type=jnp.float32)
            * scaling
        )
        probability = jax.nn.softmax(scores, axis=-1)
        weights = probability.astype(jnp.bfloat16)
        attended_head = jnp.dot(weights, value_head, preferred_element_type=jnp.float32).astype(
            jnp.bfloat16
        )
        deltas = jnp.sum(grad_head.astype(jnp.float32) * attended_head.astype(jnp.float32), axis=-1)
        grad_prob = lax.dot_general(
            grad_head, value_head, last_dims, preferred_element_type=jnp.float32
        )
        grad_score = (probability * (grad_prob - deltas[:, None])).astype(jnp.bfloat16)
        gquery_head = (
            jnp.dot(grad_score, key_head, preferred_element_type=jnp.float32) * scaling
        ).astype(jnp.bfloat16)
        gkeys_head = (
            lax.dot_general(grad_score, query_head, first_dims, preferred_element_type=jnp.float32)
            * scaling
        )
        gvalues_head = lax.dot_general(
            weights, grad_head, first_dims, preferred_element_type=jnp.float32
        )
        out_attended = lax.dynamic_update_slice_in_dim(out_attended, attended_head, start, 1)
        out_gquery = lax.dynamic_update_slice_in_dim(out_gquery, gquery_head, start, 1)
        out_gkeys = lax.dynamic_update_slice_in_dim(out_gkeys, gkeys_head, start, 1)
        out_gvalues = lax.dynamic_update_slice_in_dim(out_gvalues, gvalues_head, start, 1)
        return (out_attended, out_gquery, out_gkeys, out_gvalues)

    initial = (
        jnp.zeros((row_count, width), jnp.bfloat16),
        jnp.zeros((row_count, width), jnp.bfloat16),
        jnp.zeros((keys_total, width), jnp.float32),
        jnp.zeros((keys_total, width), jnp.float32),
    )
    return lax.fori_loop(0, head_count, one_head, initial)


def fetch_table(device_ids, block_count, total_blocks, global_blocks, random_blocks):
    owned_blocks = (
        device_ids[:, None] * block_count + jnp.arange(block_count, dtype=jnp.int32)[None, :]
    )
    pieces = []
    pieces.append(((owned_blocks - 1) % total_blocks)[:, :, None])
    pieces.append(((owned_blocks + 1) % total_blocks)[:, :, None])
    pieces.append(
        jnp.broadcast_to(
            global_blocks[None, None, :], owned_blocks.shape + (global_blocks.shape[0],)
        )
    )
    pieces.append(random_blocks[owned_blocks])
    return jnp.concatenate(pieces, axis=2).reshape(device_ids.shape[0], -1)


def shards_exchange(query, keys, values, grad_out, global_blocks, random_blocks):
    devices = lax.axis_size("seq")
    tok_rows, width = query.shape
    per_device = tok_rows // BLK
    total_blocks = per_device * devices
    row_share = BLK // devices
    key_blocks = keys.reshape(per_device, BLK, width)
    value_blocks = values.reshape(per_device, BLK, width)
    row_keys, row_values = (
        lax.all_to_all(
            keys.reshape(per_device, devices, row_share, width),
            "seq",
            split_axis=1,
            concat_axis=0,
            tiled=True,
        ),
        lax.all_to_all(
            values.reshape(per_device, devices, row_share, width),
            "seq",
            split_axis=1,
            concat_axis=0,
            tiled=True,
        ),
    )
    row_keys = row_keys.reshape(total_blocks, row_share, width)
    row_values = row_values.reshape(total_blocks, row_share, width)
    fetch_lists = fetch_table(
        jnp.arange(devices, dtype=jnp.int32), per_device, total_blocks, global_blocks, random_blocks
    )
    fetched = fetch_lists.shape[1]
    got_keys, got_values = (
        lax.all_to_all(row_keys[fetch_lists], "seq", split_axis=0, concat_axis=2, tiled=True),
        lax.all_to_all(row_values[fetch_lists], "seq", split_axis=0, concat_axis=2, tiled=True),
    )
    offset = 0
    window_keys = got_keys[:, 0:2]
    window_values = got_values[:, 0:2]
    offset = 2
    global_keys = got_keys[:, offset : offset + G]
    global_values = got_values[:, offset : offset + G]
    offset = offset + G
    random_keys = got_keys[:, offset:]
    random_values = got_values[:, offset:]
    tile_keys = jnp.concatenate(
        [key_blocks[:, None], window_keys, global_keys, random_keys], axis=1
    ).reshape(per_device, -1, width)
    tile_values = jnp.concatenate(
        [value_blocks[:, None], window_values, global_values, random_values], axis=1
    ).reshape(per_device, -1, width)
    attended, grad_query, tile_gkeys, tile_gvalues = lax.map(
        attend_block,
        (
            query.reshape(per_device, BLK, width),
            grad_out.reshape(per_device, BLK, width),
            tile_keys,
            tile_values,
        ),
    )
    tile_gkeys = tile_gkeys.reshape(per_device, -1, BLK, width)
    tile_gvalues = tile_gvalues.reshape(per_device, -1, BLK, width)
    window_gkeys = tile_gkeys[:, 1:3]
    window_gvalues = tile_gvalues[:, 1:3]
    global_gkeys = tile_gkeys[:, 3 : 3 + G]
    global_gvalues = tile_gvalues[:, 3 : 3 + G]
    back_keys = []
    back_values = []
    back_keys.append(window_gkeys)
    back_values.append(window_gvalues)
    back_keys.append(global_gkeys)
    back_values.append(global_gvalues)
    back_keys.append(tile_gkeys[:, 3 + G :])
    back_values.append(tile_gvalues[:, 3 + G :])
    back_keys = jnp.concatenate(back_keys, axis=1).reshape(1, fetched, devices, row_share, width)
    back_values = jnp.concatenate(back_values, axis=1).reshape(
        1, fetched, devices, row_share, width
    )
    recv_keys, recv_values = (
        lax.all_to_all(back_keys, "seq", split_axis=2, concat_axis=0, tiled=True),
        lax.all_to_all(back_values, "seq", split_axis=2, concat_axis=0, tiled=True),
    )
    flat_index = fetch_lists.reshape(-1)
    table_keys = (
        jnp.zeros((total_blocks, row_share, width), jnp.float32)
        .at[flat_index]
        .add(recv_keys.reshape(devices * fetched, row_share, width))
    )
    table_values = (
        jnp.zeros((total_blocks, row_share, width), jnp.float32)
        .at[flat_index]
        .add(recv_values.reshape(devices * fetched, row_share, width))
    )
    home_keys, home_values = (
        lax.all_to_all(
            table_keys.reshape(total_blocks, 1, row_share, width),
            "seq",
            split_axis=0,
            concat_axis=1,
            tiled=True,
        ),
        lax.all_to_all(
            table_values.reshape(total_blocks, 1, row_share, width),
            "seq",
            split_axis=0,
            concat_axis=1,
            tiled=True,
        ),
    )
    grad_key_blocks = tile_gkeys[:, 0] + home_keys.reshape(per_device, BLK, width)
    grad_value_blocks = tile_gvalues[:, 0] + home_values.reshape(per_device, BLK, width)
    return (
        attended.reshape(tok_rows, width),
        grad_query.reshape(tok_rows, width),
        grad_key_blocks.astype(jnp.bfloat16).reshape(tok_rows, width),
        grad_value_blocks.astype(jnp.bfloat16).reshape(tok_rows, width),
    )

SLOTS = 3 + G + 3


def _send(v, pairs):
    return lax.ppermute(v.astype(jnp.bfloat16), "seq", pairs).astype(v.dtype)


def gather_blocks(x, n):
    line_len = n // 4
    z = lax.axis_index("seq") // 4
    ups, downs = [], []
    up, down = x, x
    for k in range(1, line_len):
        up = _send(
            up, [(4 * z0 + r, 4 * (z0 + 1) + r) for z0 in range(k - 1, line_len - 1) for r in range(4)]
        )
        down = _send(
            down, [(4 * z0 + r, 4 * (z0 - 1) + r) for z0 in range(1, line_len - k + 1) for r in range(4)]
        )
        ups.append(up)
        downs.append(down)
    rel = jnp.stack(ups[::-1] + [x] + downs)
    line = lax.dynamic_slice_in_dim(rel, line_len - 1 - z, line_len, axis=0)
    other = _send(line, [(i, i ^ 2) for i in range(n)])
    pair = jnp.stack([line, other])
    sibling = _send(pair, [(i, i ^ 1) for i in range(n)])
    return jnp.stack([pair, sibling])


def _attend_kernel(pos_ref, q_ref, g_ref, *refs):
    k_refs = refs[:SLOTS]
    v_refs = refs[SLOTS : 2 * SLOTS]
    att_ref, gq_ref, dk_ref, dv_ref, dk_acc, dv_acc = refs[2 * SLOTS :]
    scale = HD ** (-0.5)
    nt = (((1,), (1,)), ((), ()))
    q = q_ref[...]
    g = g_ref[...]
    k_all = jnp.concatenate([r[...] for r in k_refs], axis=0)
    v_all = jnp.concatenate([r[...] for r in v_refs], axis=0)
    s = lax.dot_general(q, k_all, nt, preferred_element_type=jnp.float32) * scale
    e = jnp.exp(s - jnp.max(s, axis=-1, keepdims=True))
    p = e / jnp.sum(e, axis=-1, keepdims=True)
    w = p.astype(jnp.bfloat16)
    att = jnp.dot(w, v_all, preferred_element_type=jnp.float32).astype(jnp.bfloat16)
    att_ref[...] = att
    delta = jnp.sum(g.astype(jnp.float32) * att.astype(jnp.float32), axis=-1, keepdims=True)
    gp = lax.dot_general(g, v_all, nt, preferred_element_type=jnp.float32)
    gs32 = p * (gp - delta)
    gs = gs32.astype(jnp.bfloat16)
    gq_ref[...] = (jnp.dot(gs, k_all, preferred_element_type=jnp.float32) * scale).astype(
        jnp.bfloat16
    )
    tn = (((0,), (0,)), ((), ()))
    gk = lax.dot_general(gs, q, tn, preferred_element_type=jnp.float32) * scale
    gv = lax.dot_general(w, g, tn, preferred_element_type=jnp.float32)
    dk_acc[...] = jnp.zeros(dk_acc.shape, jnp.float32)
    dv_acc[...] = jnp.zeros(dv_acc.shape, jnp.float32)
    rows = q.shape[0]
    for j in range(SLOTS):
        at = pos_ref[j]
        dk_acc[at] = dk_acc[at] + gk[j * rows : (j + 1) * rows]
        dv_acc[at] = dv_acc[at] + gv[j * rows : (j + 1) * rows]
    dk_ref[...] = dk_acc[...].astype(dk_ref.dtype)
    dv_ref[...] = dv_acc[...].astype(dv_ref.dtype)


def attend_local(pos, query, grad_out, keys_local, values_local):
    rows, width = query.shape
    held = keys_local.shape[0]
    heads = width // HD
    head_spec = pl.BlockSpec((rows, HD), lambda h, pos: (0, h))
    slot_specs = [
        pl.BlockSpec((None, rows, HD), lambda h, pos, j=j: (pos[j], 0, h)) for j in range(SLOTS)
    ]
    part_spec = pl.BlockSpec((held, rows, HD), lambda h, pos: (0, 0, h))
    flops = 12 * rows * SLOTS * rows * HD * heads
    moved = 2 * SLOTS * rows * width * 2 + 4 * rows * width * 2 + 2 * held * rows * width * 2
    call = pl.pallas_call(
        _attend_kernel,
        out_shape=(
            jax.ShapeDtypeStruct((rows, width), jnp.bfloat16),
            jax.ShapeDtypeStruct((rows, width), jnp.bfloat16),
            jax.ShapeDtypeStruct((held, rows, width), jnp.bfloat16),
            jax.ShapeDtypeStruct((held, rows, width), jnp.bfloat16),
        ),
        grid_spec=pltpu.PrefetchScalarGridSpec(
            num_scalar_prefetch=1,
            grid=(heads,),
            in_specs=[head_spec, head_spec] + slot_specs + slot_specs,
            out_specs=(head_spec, head_spec, part_spec, part_spec),
            scratch_shapes=[pltpu.VMEM((held, rows, HD), jnp.float32)] * 2,
        ),
        compiler_params=pltpu.CompilerParams(dimension_semantics=("arbitrary",)),
        cost_estimate=pl.CostEstimate(
            flops=flops, transcendentals=rows * SLOTS * rows * heads, bytes_accessed=moved
        ),
    )
    return call(
        pos, query, grad_out, *([keys_local] * SLOTS), *([values_local] * SLOTS)
    )


STREAMS = 2


def _stream(pos, query, grad_out, keys, values, after=None):
    n = lax.axis_size("seq")
    rows, width = query.shape
    line_len = n // 4
    if after is not None:
        keys, values, _ = lax.optimization_barrier((keys, values, after))
    keys_local = gather_blocks(keys, n).reshape(n, rows, width)
    values_local = gather_blocks(values, n).reshape(n, rows, width)
    attended, grad_query, part_keys, part_values = attend_local(
        pos, query, grad_out, keys_local, values_local
    )
    scatter = jax.linear_transpose(
        lambda t: gather_blocks(t, n), jax.ShapeDtypeStruct((rows, width), jnp.float32)
    )
    (grad_keys,) = scatter(part_keys.astype(jnp.float32).reshape(2, 2, line_len, rows, width))
    (grad_values,) = scatter(part_values.astype(jnp.float32).reshape(2, 2, line_len, rows, width))
    outs = (attended, grad_query, grad_keys.astype(jnp.bfloat16), grad_values.astype(jnp.bfloat16))
    return outs, (keys_local, values_local)


def shards_gather(query, keys, values, grad_out, global_blocks, random_blocks):
    n = lax.axis_size("seq")
    rows, width = query.shape
    line_len = n // 4
    idx = lax.axis_index("seq")
    listed = jnp.concatenate(
        [
            jnp.stack([idx, (idx - 1) % n, (idx + 1) % n]).astype(jnp.int32),
            global_blocks.astype(jnp.int32),
            random_blocks[idx].astype(jnp.int32),
        ]
    )
    listed = jnp.clip(listed, 0, n - 1)
    core = idx % 2
    ypos = (idx // 2) % 2
    pos = (((listed % 2) ^ core) * 2 + (((listed // 2) % 2) ^ ypos)) * line_len + listed // 4
    cut = width // STREAMS
    outs = []
    after = None
    for s in range(STREAMS):
        cols = slice(s * cut, (s + 1) * cut)
        with jax.named_scope(f"stream{s}"):
            out, after = _stream(
                pos, query[:, cols], grad_out[:, cols], keys[:, cols], values[:, cols], after
            )
            outs.append(out)
    return tuple(jnp.concatenate(parts, axis=1) for parts in zip(*outs))


def shards(query, keys, values, grad_out, global_blocks, random_blocks):
    n = lax.axis_size("seq")
    if query.shape[0] == BLK and n % 4 == 0 and n <= 32:
        return shards_gather(query, keys, values, grad_out, global_blocks, random_blocks)
    return shards_exchange(query, keys, values, grad_out, global_blocks, random_blocks)


def solution(mesh):
    placed = (
        P(("groups", "seq"), None),
        P(("groups", "seq"), None),
        P(("groups", "seq"), None),
        P(("groups", "seq"), None),
        P("groups"),
        P("groups", None),
    )
    return jax.shard_map(
        shards,
        mesh=mesh,
        in_specs=placed,
        out_specs=(
            P(("groups", "seq"), None),
            P(("groups", "seq"), None),
            P(("groups", "seq"), None),
            P(("groups", "seq"), None),
        ),
        check_vma=False,
    )
```

```python
import jax
import jax.numpy as jnp
from jax import lax
from jax.experimental import pallas as pl
from jax.experimental.pallas import tpu as pltpu
from jax.sharding import PartitionSpec as P

HD = 128
BLK = 128
G = 2


def attend_block(operands):
    query_blk, grad_blk, key_tiles, value_tiles = operands
    row_count, width = query_blk.shape
    keys_total = key_tiles.shape[0]
    head_size = HD
    head_count = width // head_size
    scaling = HD ** (-0.5)
    last_dims = (((1,), (1,)), ((), ()))
    first_dims = (((0,), (0,)), ((), ()))

    def one_head(head, carry):
        out_attended, out_gquery, out_gkeys, out_gvalues = carry
        start = head * head_size
        query_head = lax.dynamic_slice_in_dim(query_blk, start, head_size, 1)
        grad_head = lax.dynamic_slice_in_dim(grad_blk, start, head_size, 1)
        key_head = lax.dynamic_slice_in_dim(key_tiles, start, head_size, 1)
        value_head = lax.dynamic_slice_in_dim(value_tiles, start, head_size, 1)
        scores = (
            lax.dot_general(query_head, key_head, last_dims, preferred_element_type=jnp.float32)
            * scaling
        )
        probability = jax.nn.softmax(scores, axis=-1)
        weights = probability.astype(jnp.bfloat16)
        attended_head = jnp.dot(weights, value_head, preferred_element_type=jnp.float32).astype(
            jnp.bfloat16
        )
        deltas = jnp.sum(grad_head.astype(jnp.float32) * attended_head.astype(jnp.float32), axis=-1)
        grad_prob = lax.dot_general(
            grad_head, value_head, last_dims, preferred_element_type=jnp.float32
        )
        grad_score = (probability * (grad_prob - deltas[:, None])).astype(jnp.bfloat16)
        gquery_head = (
            jnp.dot(grad_score, key_head, preferred_element_type=jnp.float32) * scaling
        ).astype(jnp.bfloat16)
        gkeys_head = (
            lax.dot_general(grad_score, query_head, first_dims, preferred_element_type=jnp.float32)
            * scaling
        )
        gvalues_head = lax.dot_general(
            weights, grad_head, first_dims, preferred_element_type=jnp.float32
        )
        out_attended = lax.dynamic_update_slice_in_dim(out_attended, attended_head, start, 1)
        out_gquery = lax.dynamic_update_slice_in_dim(out_gquery, gquery_head, start, 1)
        out_gkeys = lax.dynamic_update_slice_in_dim(out_gkeys, gkeys_head, start, 1)
        out_gvalues = lax.dynamic_update_slice_in_dim(out_gvalues, gvalues_head, start, 1)
        return (out_attended, out_gquery, out_gkeys, out_gvalues)

    initial = (
        jnp.zeros((row_count, width), jnp.bfloat16),
        jnp.zeros((row_count, width), jnp.bfloat16),
        jnp.zeros((keys_total, width), jnp.float32),
        jnp.zeros((keys_total, width), jnp.float32),
    )
    return lax.fori_loop(0, head_count, one_head, initial)


def fetch_table(device_ids, block_count, total_blocks, global_blocks, random_blocks):
    owned_blocks = (
        device_ids[:, None] * block_count + jnp.arange(block_count, dtype=jnp.int32)[None, :]
    )
    pieces = []
    pieces.append(((owned_blocks - 1) % total_blocks)[:, :, None])
    pieces.append(((owned_blocks + 1) % total_blocks)[:, :, None])
    pieces.append(
        jnp.broadcast_to(
            global_blocks[None, None, :], owned_blocks.shape + (global_blocks.shape[0],)
        )
    )
    pieces.append(random_blocks[owned_blocks])
    return jnp.concatenate(pieces, axis=2).reshape(device_ids.shape[0], -1)


def shards_exchange(query, keys, values, grad_out, global_blocks, random_blocks):
    devices = lax.axis_size("seq")
    tok_rows, width = query.shape
    per_device = tok_rows // BLK
    total_blocks = per_device * devices
    row_share = BLK // devices
    key_blocks = keys.reshape(per_device, BLK, width)
    value_blocks = values.reshape(per_device, BLK, width)
    row_keys, row_values = (
        lax.all_to_all(
            keys.reshape(per_device, devices, row_share, width),
            "seq",
            split_axis=1,
            concat_axis=0,
            tiled=True,
        ),
        lax.all_to_all(
            values.reshape(per_device, devices, row_share, width),
            "seq",
            split_axis=1,
            concat_axis=0,
            tiled=True,
        ),
    )
    row_keys = row_keys.reshape(total_blocks, row_share, width)
    row_values = row_values.reshape(total_blocks, row_share, width)
    fetch_lists = fetch_table(
        jnp.arange(devices, dtype=jnp.int32), per_device, total_blocks, global_blocks, random_blocks
    )
    fetched = fetch_lists.shape[1]
    got_keys, got_values = (
        lax.all_to_all(row_keys[fetch_lists], "seq", split_axis=0, concat_axis=2, tiled=True),
        lax.all_to_all(row_values[fetch_lists], "seq", split_axis=0, concat_axis=2, tiled=True),
    )
    offset = 0
    window_keys = got_keys[:, 0:2]
    window_values = got_values[:, 0:2]
    offset = 2
    global_keys = got_keys[:, offset : offset + G]
    global_values = got_values[:, offset : offset + G]
    offset = offset + G
    random_keys = got_keys[:, offset:]
    random_values = got_values[:, offset:]
    tile_keys = jnp.concatenate(
        [key_blocks[:, None], window_keys, global_keys, random_keys], axis=1
    ).reshape(per_device, -1, width)
    tile_values = jnp.concatenate(
        [value_blocks[:, None], window_values, global_values, random_values], axis=1
    ).reshape(per_device, -1, width)
    attended, grad_query, tile_gkeys, tile_gvalues = lax.map(
        attend_block,
        (
            query.reshape(per_device, BLK, width),
            grad_out.reshape(per_device, BLK, width),
            tile_keys,
            tile_values,
        ),
    )
    tile_gkeys = tile_gkeys.reshape(per_device, -1, BLK, width)
    tile_gvalues = tile_gvalues.reshape(per_device, -1, BLK, width)
    window_gkeys = tile_gkeys[:, 1:3]
    window_gvalues = tile_gvalues[:, 1:3]
    global_gkeys = tile_gkeys[:, 3 : 3 + G]
    global_gvalues = tile_gvalues[:, 3 : 3 + G]
    back_keys = []
    back_values = []
    back_keys.append(window_gkeys)
    back_values.append(window_gvalues)
    back_keys.append(global_gkeys)
    back_values.append(global_gvalues)
    back_keys.append(tile_gkeys[:, 3 + G :])
    back_values.append(tile_gvalues[:, 3 + G :])
    back_keys = jnp.concatenate(back_keys, axis=1).reshape(1, fetched, devices, row_share, width)
    back_values = jnp.concatenate(back_values, axis=1).reshape(
        1, fetched, devices, row_share, width
    )
    recv_keys, recv_values = (
        lax.all_to_all(back_keys, "seq", split_axis=2, concat_axis=0, tiled=True),
        lax.all_to_all(back_values, "seq", split_axis=2, concat_axis=0, tiled=True),
    )
    flat_index = fetch_lists.reshape(-1)
    table_keys = (
        jnp.zeros((total_blocks, row_share, width), jnp.float32)
        .at[flat_index]
        .add(recv_keys.reshape(devices * fetched, row_share, width))
    )
    table_values = (
        jnp.zeros((total_blocks, row_share, width), jnp.float32)
        .at[flat_index]
        .add(recv_values.reshape(devices * fetched, row_share, width))
    )
    home_keys, home_values = (
        lax.all_to_all(
            table_keys.reshape(total_blocks, 1, row_share, width),
            "seq",
            split_axis=0,
            concat_axis=1,
            tiled=True,
        ),
        lax.all_to_all(
            table_values.reshape(total_blocks, 1, row_share, width),
            "seq",
            split_axis=0,
            concat_axis=1,
            tiled=True,
        ),
    )
    grad_key_blocks = tile_gkeys[:, 0] + home_keys.reshape(per_device, BLK, width)
    grad_value_blocks = tile_gvalues[:, 0] + home_values.reshape(per_device, BLK, width)
    return (
        attended.reshape(tok_rows, width),
        grad_query.reshape(tok_rows, width),
        grad_key_blocks.astype(jnp.bfloat16).reshape(tok_rows, width),
        grad_value_blocks.astype(jnp.bfloat16).reshape(tok_rows, width),
    )

SLOTS = 3 + G + 3


def _send(v, pairs):
    return lax.ppermute(v.astype(jnp.bfloat16), "seq", pairs).astype(v.dtype)


def gather_blocks(x, n):
    line_len = n // 4
    z = lax.axis_index("seq") // 4
    ups, downs = [], []
    up, down = x, x
    for k in range(1, line_len):
        up = _send(
            up, [(4 * z0 + r, 4 * (z0 + 1) + r) for z0 in range(k - 1, line_len - 1) for r in range(4)]
        )
        down = _send(
            down, [(4 * z0 + r, 4 * (z0 - 1) + r) for z0 in range(1, line_len - k + 1) for r in range(4)]
        )
        ups.append(up)
        downs.append(down)
    rel = jnp.stack(ups[::-1] + [x] + downs)
    line = lax.dynamic_slice_in_dim(rel, line_len - 1 - z, line_len, axis=0)
    other = _send(line, [(i, i ^ 2) for i in range(n)])
    pair = jnp.stack([line, other])
    sibling = _send(pair, [(i, i ^ 1) for i in range(n)])
    return jnp.stack([pair, sibling])


def _attend_kernel(pos_ref, q_ref, g_ref, *refs):
    k_refs = refs[:SLOTS]
    v_refs = refs[SLOTS : 2 * SLOTS]
    att_ref, gq_ref, dk_ref, dv_ref, dk_acc, dv_acc = refs[2 * SLOTS :]
    scale = HD ** (-0.5)
    nt = (((1,), (1,)), ((), ()))
    q = q_ref[...]
    g = g_ref[...]
    k_all = jnp.concatenate([r[...] for r in k_refs], axis=0)
    v_all = jnp.concatenate([r[...] for r in v_refs], axis=0)
    s = lax.dot_general(q, k_all, nt, preferred_element_type=jnp.float32) * scale
    e = jnp.exp(s - jnp.max(s, axis=-1, keepdims=True))
    p = e / jnp.sum(e, axis=-1, keepdims=True)
    w = p.astype(jnp.bfloat16)
    att = jnp.dot(w, v_all, preferred_element_type=jnp.float32).astype(jnp.bfloat16)
    att_ref[...] = att
    delta = jnp.sum(g.astype(jnp.float32) * att.astype(jnp.float32), axis=-1, keepdims=True)
    gp = lax.dot_general(g, v_all, nt, preferred_element_type=jnp.float32)
    gs32 = p * (gp - delta)
    gs = gs32.astype(jnp.bfloat16)
    gq_ref[...] = (jnp.dot(gs, k_all, preferred_element_type=jnp.float32) * scale).astype(
        jnp.bfloat16
    )
    tn = (((0,), (0,)), ((), ()))
    gk = lax.dot_general(gs, q, tn, preferred_element_type=jnp.float32) * scale
    gv = lax.dot_general(w, g, tn, preferred_element_type=jnp.float32)
    dk_acc[...] = jnp.zeros(dk_acc.shape, jnp.float32)
    dv_acc[...] = jnp.zeros(dv_acc.shape, jnp.float32)
    rows = q.shape[0]
    for j in range(SLOTS):
        at = pos_ref[j]
        dk_acc[at] = dk_acc[at] + gk[j * rows : (j + 1) * rows]
        dv_acc[at] = dv_acc[at] + gv[j * rows : (j + 1) * rows]
    dk_ref[...] = dk_acc[...].astype(dk_ref.dtype)
    dv_ref[...] = dv_acc[...].astype(dv_ref.dtype)


def attend_local(pos, query, grad_out, keys_local, values_local):
    rows, width = query.shape
    held = keys_local.shape[0]
    heads = width // HD
    head_spec = pl.BlockSpec((rows, HD), lambda h, pos: (0, h))
    slot_specs = [
        pl.BlockSpec((None, rows, HD), lambda h, pos, j=j: (pos[j], 0, h)) for j in range(SLOTS)
    ]
    part_spec = pl.BlockSpec((held, rows, HD), lambda h, pos: (0, 0, h))
    flops = 12 * rows * SLOTS * rows * HD * heads
    moved = 2 * SLOTS * rows * width * 2 + 4 * rows * width * 2 + 2 * held * rows * width * 2
    call = pl.pallas_call(
        _attend_kernel,
        out_shape=(
            jax.ShapeDtypeStruct((rows, width), jnp.bfloat16),
            jax.ShapeDtypeStruct((rows, width), jnp.bfloat16),
            jax.ShapeDtypeStruct((held, rows, width), jnp.bfloat16),
            jax.ShapeDtypeStruct((held, rows, width), jnp.bfloat16),
        ),
        grid_spec=pltpu.PrefetchScalarGridSpec(
            num_scalar_prefetch=1,
            grid=(heads,),
            in_specs=[head_spec, head_spec] + slot_specs + slot_specs,
            out_specs=(head_spec, head_spec, part_spec, part_spec),
            scratch_shapes=[pltpu.VMEM((held, rows, HD), jnp.float32)] * 2,
        ),
        compiler_params=pltpu.CompilerParams(dimension_semantics=("arbitrary",)),
        cost_estimate=pl.CostEstimate(
            flops=flops, transcendentals=rows * SLOTS * rows * heads, bytes_accessed=moved
        ),
    )
    return call(
        pos, query, grad_out, *([keys_local] * SLOTS), *([values_local] * SLOTS)
    )


STREAMS = 3


def _stream(pos, query, grad_out, keys, values, after=None):
    n = lax.axis_size("seq")
    rows, width = query.shape
    line_len = n // 4
    if after is not None:
        keys, values, _ = lax.optimization_barrier((keys, values, after))
    keys_local = gather_blocks(keys, n).reshape(n, rows, width)
    values_local = gather_blocks(values, n).reshape(n, rows, width)
    attended, grad_query, part_keys, part_values = attend_local(
        pos, query, grad_out, keys_local, values_local
    )
    scatter = jax.linear_transpose(
        lambda t: gather_blocks(t, n), jax.ShapeDtypeStruct((rows, width), jnp.float32)
    )
    (grad_keys,) = scatter(part_keys.astype(jnp.float32).reshape(2, 2, line_len, rows, width))
    (grad_values,) = scatter(part_values.astype(jnp.float32).reshape(2, 2, line_len, rows, width))
    outs = (attended, grad_query, grad_keys.astype(jnp.bfloat16), grad_values.astype(jnp.bfloat16))
    return outs, (keys_local, values_local)


def shards_gather(query, keys, values, grad_out, global_blocks, random_blocks):
    n = lax.axis_size("seq")
    rows, width = query.shape
    line_len = n // 4
    idx = lax.axis_index("seq")
    listed = jnp.concatenate(
        [
            jnp.stack([idx, (idx - 1) % n, (idx + 1) % n]).astype(jnp.int32),
            global_blocks.astype(jnp.int32),
            random_blocks[idx].astype(jnp.int32),
        ]
    )
    listed = jnp.clip(listed, 0, n - 1)
    core = idx % 2
    ypos = (idx // 2) % 2
    pos = (((listed % 2) ^ core) * 2 + (((listed // 2) % 2) ^ ypos)) * line_len + listed // 4
    heads = width // HD
    shares = [heads // STREAMS + (1 if s < heads % STREAMS else 0) for s in range(STREAMS)]
    edges = [sum(shares[:s]) * HD for s in range(STREAMS + 1)]
    outs = []
    after = None
    for s in range(STREAMS):
        cols = slice(edges[s], edges[s + 1])
        with jax.named_scope(f"stream{s}"):
            out, after = _stream(
                pos, query[:, cols], grad_out[:, cols], keys[:, cols], values[:, cols], after
            )
            outs.append(out)
    return tuple(jnp.concatenate(parts, axis=1) for parts in zip(*outs))


def shards(query, keys, values, grad_out, global_blocks, random_blocks):
    n = lax.axis_size("seq")
    if query.shape[0] == BLK and n % 4 == 0 and n <= 32:
        return shards_gather(query, keys, values, grad_out, global_blocks, random_blocks)
    return shards_exchange(query, keys, values, grad_out, global_blocks, random_blocks)


def solution(mesh):
    placed = (
        P(("groups", "seq"), None),
        P(("groups", "seq"), None),
        P(("groups", "seq"), None),
        P(("groups", "seq"), None),
        P("groups"),
        P("groups", None),
    )
    return jax.shard_map(
        shards,
        mesh=mesh,
        in_specs=placed,
        out_specs=(
            P(("groups", "seq"), None),
            P(("groups", "seq"), None),
            P(("groups", "seq"), None),
            P(("groups", "seq"), None),
        ),
        check_vma=False,
    )
```

```python
import jax
import jax.numpy as jnp
from jax import lax
from jax.experimental import pallas as pl
from jax.experimental.pallas import tpu as pltpu
from jax.sharding import PartitionSpec as P

HD = 128
BLK = 128
G = 2


def attend_block(operands):
    query_blk, grad_blk, key_tiles, value_tiles = operands
    row_count, width = query_blk.shape
    keys_total = key_tiles.shape[0]
    head_size = HD
    head_count = width // head_size
    scaling = HD ** (-0.5)
    last_dims = (((1,), (1,)), ((), ()))
    first_dims = (((0,), (0,)), ((), ()))

    def one_head(head, carry):
        out_attended, out_gquery, out_gkeys, out_gvalues = carry
        start = head * head_size
        query_head = lax.dynamic_slice_in_dim(query_blk, start, head_size, 1)
        grad_head = lax.dynamic_slice_in_dim(grad_blk, start, head_size, 1)
        key_head = lax.dynamic_slice_in_dim(key_tiles, start, head_size, 1)
        value_head = lax.dynamic_slice_in_dim(value_tiles, start, head_size, 1)
        scores = (
            lax.dot_general(query_head, key_head, last_dims, preferred_element_type=jnp.float32)
            * scaling
        )
        probability = jax.nn.softmax(scores, axis=-1)
        weights = probability.astype(jnp.bfloat16)
        attended_head = jnp.dot(weights, value_head, preferred_element_type=jnp.float32).astype(
            jnp.bfloat16
        )
        deltas = jnp.sum(grad_head.astype(jnp.float32) * attended_head.astype(jnp.float32), axis=-1)
        grad_prob = lax.dot_general(
            grad_head, value_head, last_dims, preferred_element_type=jnp.float32
        )
        grad_score = (probability * (grad_prob - deltas[:, None])).astype(jnp.bfloat16)
        gquery_head = (
            jnp.dot(grad_score, key_head, preferred_element_type=jnp.float32) * scaling
        ).astype(jnp.bfloat16)
        gkeys_head = (
            lax.dot_general(grad_score, query_head, first_dims, preferred_element_type=jnp.float32)
            * scaling
        )
        gvalues_head = lax.dot_general(
            weights, grad_head, first_dims, preferred_element_type=jnp.float32
        )
        out_attended = lax.dynamic_update_slice_in_dim(out_attended, attended_head, start, 1)
        out_gquery = lax.dynamic_update_slice_in_dim(out_gquery, gquery_head, start, 1)
        out_gkeys = lax.dynamic_update_slice_in_dim(out_gkeys, gkeys_head, start, 1)
        out_gvalues = lax.dynamic_update_slice_in_dim(out_gvalues, gvalues_head, start, 1)
        return (out_attended, out_gquery, out_gkeys, out_gvalues)

    initial = (
        jnp.zeros((row_count, width), jnp.bfloat16),
        jnp.zeros((row_count, width), jnp.bfloat16),
        jnp.zeros((keys_total, width), jnp.float32),
        jnp.zeros((keys_total, width), jnp.float32),
    )
    return lax.fori_loop(0, head_count, one_head, initial)


def fetch_table(device_ids, block_count, total_blocks, global_blocks, random_blocks):
    owned_blocks = (
        device_ids[:, None] * block_count + jnp.arange(block_count, dtype=jnp.int32)[None, :]
    )
    pieces = []
    pieces.append(((owned_blocks - 1) % total_blocks)[:, :, None])
    pieces.append(((owned_blocks + 1) % total_blocks)[:, :, None])
    pieces.append(
        jnp.broadcast_to(
            global_blocks[None, None, :], owned_blocks.shape + (global_blocks.shape[0],)
        )
    )
    pieces.append(random_blocks[owned_blocks])
    return jnp.concatenate(pieces, axis=2).reshape(device_ids.shape[0], -1)


def shards_exchange(query, keys, values, grad_out, global_blocks, random_blocks):
    devices = lax.axis_size("seq")
    tok_rows, width = query.shape
    per_device = tok_rows // BLK
    total_blocks = per_device * devices
    row_share = BLK // devices
    key_blocks = keys.reshape(per_device, BLK, width)
    value_blocks = values.reshape(per_device, BLK, width)
    row_keys, row_values = (
        lax.all_to_all(
            keys.reshape(per_device, devices, row_share, width),
            "seq",
            split_axis=1,
            concat_axis=0,
            tiled=True,
        ),
        lax.all_to_all(
            values.reshape(per_device, devices, row_share, width),
            "seq",
            split_axis=1,
            concat_axis=0,
            tiled=True,
        ),
    )
    row_keys = row_keys.reshape(total_blocks, row_share, width)
    row_values = row_values.reshape(total_blocks, row_share, width)
    fetch_lists = fetch_table(
        jnp.arange(devices, dtype=jnp.int32), per_device, total_blocks, global_blocks, random_blocks
    )
    fetched = fetch_lists.shape[1]
    got_keys, got_values = (
        lax.all_to_all(row_keys[fetch_lists], "seq", split_axis=0, concat_axis=2, tiled=True),
        lax.all_to_all(row_values[fetch_lists], "seq", split_axis=0, concat_axis=2, tiled=True),
    )
    offset = 0
    window_keys = got_keys[:, 0:2]
    window_values = got_values[:, 0:2]
    offset = 2
    global_keys = got_keys[:, offset : offset + G]
    global_values = got_values[:, offset : offset + G]
    offset = offset + G
    random_keys = got_keys[:, offset:]
    random_values = got_values[:, offset:]
    tile_keys = jnp.concatenate(
        [key_blocks[:, None], window_keys, global_keys, random_keys], axis=1
    ).reshape(per_device, -1, width)
    tile_values = jnp.concatenate(
        [value_blocks[:, None], window_values, global_values, random_values], axis=1
    ).reshape(per_device, -1, width)
    attended, grad_query, tile_gkeys, tile_gvalues = lax.map(
        attend_block,
        (
            query.reshape(per_device, BLK, width),
            grad_out.reshape(per_device, BLK, width),
            tile_keys,
            tile_values,
        ),
    )
    tile_gkeys = tile_gkeys.reshape(per_device, -1, BLK, width)
    tile_gvalues = tile_gvalues.reshape(per_device, -1, BLK, width)
    window_gkeys = tile_gkeys[:, 1:3]
    window_gvalues = tile_gvalues[:, 1:3]
    global_gkeys = tile_gkeys[:, 3 : 3 + G]
    global_gvalues = tile_gvalues[:, 3 : 3 + G]
    back_keys = []
    back_values = []
    back_keys.append(window_gkeys)
    back_values.append(window_gvalues)
    back_keys.append(global_gkeys)
    back_values.append(global_gvalues)
    back_keys.append(tile_gkeys[:, 3 + G :])
    back_values.append(tile_gvalues[:, 3 + G :])
    back_keys = jnp.concatenate(back_keys, axis=1).reshape(1, fetched, devices, row_share, width)
    back_values = jnp.concatenate(back_values, axis=1).reshape(
        1, fetched, devices, row_share, width
    )
    recv_keys, recv_values = (
        lax.all_to_all(back_keys, "seq", split_axis=2, concat_axis=0, tiled=True),
        lax.all_to_all(back_values, "seq", split_axis=2, concat_axis=0, tiled=True),
    )
    flat_index = fetch_lists.reshape(-1)
    table_keys = (
        jnp.zeros((total_blocks, row_share, width), jnp.float32)
        .at[flat_index]
        .add(recv_keys.reshape(devices * fetched, row_share, width))
    )
    table_values = (
        jnp.zeros((total_blocks, row_share, width), jnp.float32)
        .at[flat_index]
        .add(recv_values.reshape(devices * fetched, row_share, width))
    )
    home_keys, home_values = (
        lax.all_to_all(
            table_keys.reshape(total_blocks, 1, row_share, width),
            "seq",
            split_axis=0,
            concat_axis=1,
            tiled=True,
        ),
        lax.all_to_all(
            table_values.reshape(total_blocks, 1, row_share, width),
            "seq",
            split_axis=0,
            concat_axis=1,
            tiled=True,
        ),
    )
    grad_key_blocks = tile_gkeys[:, 0] + home_keys.reshape(per_device, BLK, width)
    grad_value_blocks = tile_gvalues[:, 0] + home_values.reshape(per_device, BLK, width)
    return (
        attended.reshape(tok_rows, width),
        grad_query.reshape(tok_rows, width),
        grad_key_blocks.astype(jnp.bfloat16).reshape(tok_rows, width),
        grad_value_blocks.astype(jnp.bfloat16).reshape(tok_rows, width),
    )

SLOTS = 3 + G + 3


def _send(v, pairs):
    return lax.ppermute(v.astype(jnp.bfloat16), "seq", pairs).astype(v.dtype)


def gather_blocks(x, n):
    line_len = n // 4
    z = lax.axis_index("seq") // 4
    y_swap = [(i, i ^ 2) for i in range(n)]
    other_own = _send(x, y_swap)
    ups, downs = [], []
    up, down = x, x
    for k in range(1, line_len):
        up = _send(
            up, [(4 * z0 + r, 4 * (z0 + 1) + r) for z0 in range(k - 1, line_len - 1) for r in range(4)]
        )
        down = _send(
            down, [(4 * z0 + r, 4 * (z0 - 1) + r) for z0 in range(1, line_len - k + 1) for r in range(4)]
        )
        ups.append(up)
        downs.append(down)
    rest = lax.dynamic_slice_in_dim(
        jnp.stack(ups[::-1] + downs), line_len - 1 - z, line_len - 1, axis=0
    )
    mine = jnp.concatenate([x[None], rest])
    other = jnp.concatenate([other_own[None], _send(rest, y_swap)])
    pair = jnp.stack([mine, other])
    sibling = _send(pair, [(i, i ^ 1) for i in range(n)])
    return jnp.stack([pair, sibling])


def _attend_kernel(pos_ref, q_ref, g_ref, *refs):
    k_refs = refs[:SLOTS]
    v_refs = refs[SLOTS : 2 * SLOTS]
    att_ref, gq_ref, dk_ref, dv_ref, dk_acc, dv_acc = refs[2 * SLOTS :]
    scale = HD ** (-0.5)
    nt = (((1,), (1,)), ((), ()))
    q = q_ref[...]
    g = g_ref[...]
    k_all = jnp.concatenate([r[...] for r in k_refs], axis=0)
    v_all = jnp.concatenate([r[...] for r in v_refs], axis=0)
    s = lax.dot_general(q, k_all, nt, preferred_element_type=jnp.float32) * scale
    e = jnp.exp(s - jnp.max(s, axis=-1, keepdims=True))
    p = e / jnp.sum(e, axis=-1, keepdims=True)
    w = p.astype(jnp.bfloat16)
    att = jnp.dot(w, v_all, preferred_element_type=jnp.float32).astype(jnp.bfloat16)
    att_ref[...] = att
    delta = jnp.sum(g.astype(jnp.float32) * att.astype(jnp.float32), axis=-1, keepdims=True)
    gp = lax.dot_general(g, v_all, nt, preferred_element_type=jnp.float32)
    gs32 = p * (gp - delta)
    gs = gs32.astype(jnp.bfloat16)
    gq_ref[...] = (jnp.dot(gs, k_all, preferred_element_type=jnp.float32) * scale).astype(
        jnp.bfloat16
    )
    tn = (((0,), (0,)), ((), ()))
    gk = lax.dot_general(gs, q, tn, preferred_element_type=jnp.float32) * scale
    gv = lax.dot_general(w, g, tn, preferred_element_type=jnp.float32)
    dk_acc[...] = jnp.zeros(dk_acc.shape, jnp.float32)
    dv_acc[...] = jnp.zeros(dv_acc.shape, jnp.float32)
    rows = q.shape[0]
    for j in range(SLOTS):
        at = pos_ref[j]
        dk_acc[at] = dk_acc[at] + gk[j * rows : (j + 1) * rows]
        dv_acc[at] = dv_acc[at] + gv[j * rows : (j + 1) * rows]
    dk_ref[...] = dk_acc[...].astype(dk_ref.dtype)
    dv_ref[...] = dv_acc[...].astype(dv_ref.dtype)


def attend_local(pos, query, grad_out, keys_local, values_local):
    rows, width = query.shape
    held = keys_local.shape[0]
    heads = width // HD
    head_spec = pl.BlockSpec((rows, HD), lambda h, pos: (0, h))
    slot_specs = [
        pl.BlockSpec((None, rows, HD), lambda h, pos, j=j: (pos[j], 0, h)) for j in range(SLOTS)
    ]
    part_spec = pl.BlockSpec((held, rows, HD), lambda h, pos: (0, 0, h))
    flops = 12 * rows * SLOTS * rows * HD * heads
    moved = 2 * SLOTS * rows * width * 2 + 4 * rows * width * 2 + 2 * held * rows * width * 2
    call = pl.pallas_call(
        _attend_kernel,
        out_shape=(
            jax.ShapeDtypeStruct((rows, width), jnp.bfloat16),
            jax.ShapeDtypeStruct((rows, width), jnp.bfloat16),
            jax.ShapeDtypeStruct((held, rows, width), jnp.bfloat16),
            jax.ShapeDtypeStruct((held, rows, width), jnp.bfloat16),
        ),
        grid_spec=pltpu.PrefetchScalarGridSpec(
            num_scalar_prefetch=1,
            grid=(heads,),
            in_specs=[head_spec, head_spec] + slot_specs + slot_specs,
            out_specs=(head_spec, head_spec, part_spec, part_spec),
            scratch_shapes=[pltpu.VMEM((held, rows, HD), jnp.float32)] * 2,
        ),
        compiler_params=pltpu.CompilerParams(dimension_semantics=("arbitrary",)),
        cost_estimate=pl.CostEstimate(
            flops=flops, transcendentals=rows * SLOTS * rows * heads, bytes_accessed=moved
        ),
    )
    return call(
        pos, query, grad_out, *([keys_local] * SLOTS), *([values_local] * SLOTS)
    )


STREAMS = 2


def _stream(pos, query, grad_out, keys, values, after=None):
    n = lax.axis_size("seq")
    rows, width = query.shape
    line_len = n // 4
    if after is not None:
        keys, values, _ = lax.optimization_barrier((keys, values, after))
    keys_local = gather_blocks(keys, n).reshape(n, rows, width)
    values_local = gather_blocks(values, n).reshape(n, rows, width)
    attended, grad_query, part_keys, part_values = attend_local(
        pos, query, grad_out, keys_local, values_local
    )
    scatter = jax.linear_transpose(
        lambda t: gather_blocks(t, n), jax.ShapeDtypeStruct((rows, width), jnp.float32)
    )
    (grad_keys,) = scatter(part_keys.astype(jnp.float32).reshape(2, 2, line_len, rows, width))
    (grad_values,) = scatter(part_values.astype(jnp.float32).reshape(2, 2, line_len, rows, width))
    outs = (attended, grad_query, grad_keys.astype(jnp.bfloat16), grad_values.astype(jnp.bfloat16))
    return outs, (keys_local, values_local)


def shards_gather(query, keys, values, grad_out, global_blocks, random_blocks):
    n = lax.axis_size("seq")
    rows, width = query.shape
    line_len = n // 4
    idx = lax.axis_index("seq")
    listed = jnp.concatenate(
        [
            jnp.stack([idx, (idx - 1) % n, (idx + 1) % n]).astype(jnp.int32),
            global_blocks.astype(jnp.int32),
            random_blocks[idx].astype(jnp.int32),
        ]
    )
    listed = jnp.clip(listed, 0, n - 1)
    core = idx % 2
    ypos = (idx // 2) % 2
    zpos = idx // 4
    plane = listed // 4
    in_line = jnp.where(plane == zpos, 0, jnp.where(plane < zpos, plane + 1, plane))
    pos = (((listed % 2) ^ core) * 2 + (((listed // 2) % 2) ^ ypos)) * line_len + in_line
    cut = width // STREAMS
    outs = []
    after = None
    for s in range(STREAMS):
        cols = slice(s * cut, (s + 1) * cut)
        with jax.named_scope(f"stream{s}"):
            out, after = _stream(
                pos, query[:, cols], grad_out[:, cols], keys[:, cols], values[:, cols], after
            )
            outs.append(out)
    return tuple(jnp.concatenate(parts, axis=1) for parts in zip(*outs))


def shards(query, keys, values, grad_out, global_blocks, random_blocks):
    n = lax.axis_size("seq")
    if query.shape[0] == BLK and n % 4 == 0 and n <= 32:
        return shards_gather(query, keys, values, grad_out, global_blocks, random_blocks)
    return shards_exchange(query, keys, values, grad_out, global_blocks, random_blocks)


def solution(mesh):
    placed = (
        P(("groups", "seq"), None),
        P(("groups", "seq"), None),
        P(("groups", "seq"), None),
        P(("groups", "seq"), None),
        P("groups"),
        P("groups", None),
    )
    return jax.shard_map(
        shards,
        mesh=mesh,
        in_specs=placed,
        out_specs=(
            P(("groups", "seq"), None),
            P(("groups", "seq"), None),
            P(("groups", "seq"), None),
            P(("groups", "seq"), None),
        ),
        check_vma=False,
    )
```

```python
import jax
import jax.numpy as jnp
from jax import lax
from jax.experimental import pallas as pl
from jax.experimental.pallas import tpu as pltpu
from jax.sharding import PartitionSpec as P

HD = 128
BLK = 128
G = 2


def attend_block(operands):
    query_blk, grad_blk, key_tiles, value_tiles = operands
    row_count, width = query_blk.shape
    keys_total = key_tiles.shape[0]
    head_size = HD
    head_count = width // head_size
    scaling = HD ** (-0.5)
    last_dims = (((1,), (1,)), ((), ()))
    first_dims = (((0,), (0,)), ((), ()))

    def one_head(head, carry):
        out_attended, out_gquery, out_gkeys, out_gvalues = carry
        start = head * head_size
        query_head = lax.dynamic_slice_in_dim(query_blk, start, head_size, 1)
        grad_head = lax.dynamic_slice_in_dim(grad_blk, start, head_size, 1)
        key_head = lax.dynamic_slice_in_dim(key_tiles, start, head_size, 1)
        value_head = lax.dynamic_slice_in_dim(value_tiles, start, head_size, 1)
        scores = (
            lax.dot_general(query_head, key_head, last_dims, preferred_element_type=jnp.float32)
            * scaling
        )
        probability = jax.nn.softmax(scores, axis=-1)
        weights = probability.astype(jnp.bfloat16)
        attended_head = jnp.dot(weights, value_head, preferred_element_type=jnp.float32).astype(
            jnp.bfloat16
        )
        deltas = jnp.sum(grad_head.astype(jnp.float32) * attended_head.astype(jnp.float32), axis=-1)
        grad_prob = lax.dot_general(
            grad_head, value_head, last_dims, preferred_element_type=jnp.float32
        )
        grad_score = (probability * (grad_prob - deltas[:, None])).astype(jnp.bfloat16)
        gquery_head = (
            jnp.dot(grad_score, key_head, preferred_element_type=jnp.float32) * scaling
        ).astype(jnp.bfloat16)
        gkeys_head = (
            lax.dot_general(grad_score, query_head, first_dims, preferred_element_type=jnp.float32)
            * scaling
        )
        gvalues_head = lax.dot_general(
            weights, grad_head, first_dims, preferred_element_type=jnp.float32
        )
        out_attended = lax.dynamic_update_slice_in_dim(out_attended, attended_head, start, 1)
        out_gquery = lax.dynamic_update_slice_in_dim(out_gquery, gquery_head, start, 1)
        out_gkeys = lax.dynamic_update_slice_in_dim(out_gkeys, gkeys_head, start, 1)
        out_gvalues = lax.dynamic_update_slice_in_dim(out_gvalues, gvalues_head, start, 1)
        return (out_attended, out_gquery, out_gkeys, out_gvalues)

    initial = (
        jnp.zeros((row_count, width), jnp.bfloat16),
        jnp.zeros((row_count, width), jnp.bfloat16),
        jnp.zeros((keys_total, width), jnp.float32),
        jnp.zeros((keys_total, width), jnp.float32),
    )
    return lax.fori_loop(0, head_count, one_head, initial)


def fetch_table(device_ids, block_count, total_blocks, global_blocks, random_blocks):
    owned_blocks = (
        device_ids[:, None] * block_count + jnp.arange(block_count, dtype=jnp.int32)[None, :]
    )
    pieces = []
    pieces.append(((owned_blocks - 1) % total_blocks)[:, :, None])
    pieces.append(((owned_blocks + 1) % total_blocks)[:, :, None])
    pieces.append(
        jnp.broadcast_to(
            global_blocks[None, None, :], owned_blocks.shape + (global_blocks.shape[0],)
        )
    )
    pieces.append(random_blocks[owned_blocks])
    return jnp.concatenate(pieces, axis=2).reshape(device_ids.shape[0], -1)


def shards_exchange(query, keys, values, grad_out, global_blocks, random_blocks):
    devices = lax.axis_size("seq")
    tok_rows, width = query.shape
    per_device = tok_rows // BLK
    total_blocks = per_device * devices
    row_share = BLK // devices
    key_blocks = keys.reshape(per_device, BLK, width)
    value_blocks = values.reshape(per_device, BLK, width)
    row_keys, row_values = (
        lax.all_to_all(
            keys.reshape(per_device, devices, row_share, width),
            "seq",
            split_axis=1,
            concat_axis=0,
            tiled=True,
        ),
        lax.all_to_all(
            values.reshape(per_device, devices, row_share, width),
            "seq",
            split_axis=1,
            concat_axis=0,
            tiled=True,
        ),
    )
    row_keys = row_keys.reshape(total_blocks, row_share, width)
    row_values = row_values.reshape(total_blocks, row_share, width)
    fetch_lists = fetch_table(
        jnp.arange(devices, dtype=jnp.int32), per_device, total_blocks, global_blocks, random_blocks
    )
    fetched = fetch_lists.shape[1]
    got_keys, got_values = (
        lax.all_to_all(row_keys[fetch_lists], "seq", split_axis=0, concat_axis=2, tiled=True),
        lax.all_to_all(row_values[fetch_lists], "seq", split_axis=0, concat_axis=2, tiled=True),
    )
    offset = 0
    window_keys = got_keys[:, 0:2]
    window_values = got_values[:, 0:2]
    offset = 2
    global_keys = got_keys[:, offset : offset + G]
    global_values = got_values[:, offset : offset + G]
    offset = offset + G
    random_keys = got_keys[:, offset:]
    random_values = got_values[:, offset:]
    tile_keys = jnp.concatenate(
        [key_blocks[:, None], window_keys, global_keys, random_keys], axis=1
    ).reshape(per_device, -1, width)
    tile_values = jnp.concatenate(
        [value_blocks[:, None], window_values, global_values, random_values], axis=1
    ).reshape(per_device, -1, width)
    attended, grad_query, tile_gkeys, tile_gvalues = lax.map(
        attend_block,
        (
            query.reshape(per_device, BLK, width),
            grad_out.reshape(per_device, BLK, width),
            tile_keys,
            tile_values,
        ),
    )
    tile_gkeys = tile_gkeys.reshape(per_device, -1, BLK, width)
    tile_gvalues = tile_gvalues.reshape(per_device, -1, BLK, width)
    window_gkeys = tile_gkeys[:, 1:3]
    window_gvalues = tile_gvalues[:, 1:3]
    global_gkeys = tile_gkeys[:, 3 : 3 + G]
    global_gvalues = tile_gvalues[:, 3 : 3 + G]
    back_keys = []
    back_values = []
    back_keys.append(window_gkeys)
    back_values.append(window_gvalues)
    back_keys.append(global_gkeys)
    back_values.append(global_gvalues)
    back_keys.append(tile_gkeys[:, 3 + G :])
    back_values.append(tile_gvalues[:, 3 + G :])
    back_keys = jnp.concatenate(back_keys, axis=1).reshape(1, fetched, devices, row_share, width)
    back_values = jnp.concatenate(back_values, axis=1).reshape(
        1, fetched, devices, row_share, width
    )
    recv_keys, recv_values = (
        lax.all_to_all(back_keys, "seq", split_axis=2, concat_axis=0, tiled=True),
        lax.all_to_all(back_values, "seq", split_axis=2, concat_axis=0, tiled=True),
    )
    flat_index = fetch_lists.reshape(-1)
    table_keys = (
        jnp.zeros((total_blocks, row_share, width), jnp.float32)
        .at[flat_index]
        .add(recv_keys.reshape(devices * fetched, row_share, width))
    )
    table_values = (
        jnp.zeros((total_blocks, row_share, width), jnp.float32)
        .at[flat_index]
        .add(recv_values.reshape(devices * fetched, row_share, width))
    )
    home_keys, home_values = (
        lax.all_to_all(
            table_keys.reshape(total_blocks, 1, row_share, width),
            "seq",
            split_axis=0,
            concat_axis=1,
            tiled=True,
        ),
        lax.all_to_all(
            table_values.reshape(total_blocks, 1, row_share, width),
            "seq",
            split_axis=0,
            concat_axis=1,
            tiled=True,
        ),
    )
    grad_key_blocks = tile_gkeys[:, 0] + home_keys.reshape(per_device, BLK, width)
    grad_value_blocks = tile_gvalues[:, 0] + home_values.reshape(per_device, BLK, width)
    return (
        attended.reshape(tok_rows, width),
        grad_query.reshape(tok_rows, width),
        grad_key_blocks.astype(jnp.bfloat16).reshape(tok_rows, width),
        grad_value_blocks.astype(jnp.bfloat16).reshape(tok_rows, width),
    )

SLOTS = 3 + G + 3


def _send(v, pairs):
    return lax.ppermute(v.astype(jnp.bfloat16), "seq", pairs).astype(v.dtype)


def gather_blocks(x, n):
    line_len = n // 4
    z = lax.axis_index("seq") // 4
    ups, downs = [], []
    up, down = x, x
    for k in range(1, line_len):
        up = _send(
            up, [(4 * z0 + r, 4 * (z0 + 1) + r) for z0 in range(k - 1, line_len - 1) for r in range(4)]
        )
        down = _send(
            down, [(4 * z0 + r, 4 * (z0 - 1) + r) for z0 in range(1, line_len - k + 1) for r in range(4)]
        )
        ups.append(up)
        downs.append(down)
    rel = jnp.stack(ups[::-1] + [x] + downs)
    line = lax.dynamic_slice_in_dim(rel, line_len - 1 - z, line_len, axis=0)
    other = _send(line, [(i, i ^ 2) for i in range(n)])
    pair = jnp.stack([line, other])
    sibling = _send(pair, [(i, i ^ 1) for i in range(n)])
    return jnp.stack([pair, sibling])


def _attend_kernel(pos_ref, q_ref, g_ref, *refs):
    k_refs = refs[:SLOTS]
    v_refs = refs[SLOTS : 2 * SLOTS]
    att_ref, gq_ref, dk_ref, dv_ref, dk_acc, dv_acc = refs[2 * SLOTS :]
    scale = HD ** (-0.5)
    nt = (((1,), (1,)), ((), ()))
    q = q_ref[...]
    g = g_ref[...]
    k_all = jnp.concatenate([r[...] for r in k_refs], axis=0)
    v_all = jnp.concatenate([r[...] for r in v_refs], axis=0)
    s = lax.dot_general(q, k_all, nt, preferred_element_type=jnp.float32) * scale
    e = jnp.exp(s - jnp.max(s, axis=-1, keepdims=True))
    p = e / jnp.sum(e, axis=-1, keepdims=True)
    w = p.astype(jnp.bfloat16)
    att = jnp.dot(w, v_all, preferred_element_type=jnp.float32).astype(jnp.bfloat16)
    att_ref[...] = att
    delta = jnp.sum(g.astype(jnp.float32) * att.astype(jnp.float32), axis=-1, keepdims=True)
    gp = lax.dot_general(g, v_all, nt, preferred_element_type=jnp.float32)
    gs32 = p * (gp - delta)
    gs = gs32.astype(jnp.bfloat16)
    gq_ref[...] = (jnp.dot(gs, k_all, preferred_element_type=jnp.float32) * scale).astype(
        jnp.bfloat16
    )
    tn = (((0,), (0,)), ((), ()))
    gk = lax.dot_general(gs, q, tn, preferred_element_type=jnp.float32) * scale
    gv = lax.dot_general(w, g, tn, preferred_element_type=jnp.float32)
    rows = q.shape[0]
    empty = jnp.zeros((rows, HD), jnp.float32)
    for j in range(SLOTS):
        dk_acc[pos_ref[j]] = empty
        dv_acc[pos_ref[j]] = empty
    for j in range(SLOTS):
        at = pos_ref[j]
        dk_acc[at] = dk_acc[at] + gk[j * rows : (j + 1) * rows]
        dv_acc[at] = dv_acc[at] + gv[j * rows : (j + 1) * rows]
    dk_ref[...] = jnp.zeros(dk_ref.shape, dk_ref.dtype)
    dv_ref[...] = jnp.zeros(dv_ref.shape, dv_ref.dtype)
    for j in range(SLOTS):
        at = pos_ref[j]
        dk_ref[at] = dk_acc[at].astype(dk_ref.dtype)
        dv_ref[at] = dv_acc[at].astype(dv_ref.dtype)


def attend_local(pos, query, grad_out, keys_local, values_local):
    rows, width = query.shape
    held = keys_local.shape[0]
    heads = width // HD
    head_spec = pl.BlockSpec((rows, HD), lambda h, pos: (0, h))
    slot_specs = [
        pl.BlockSpec((None, rows, HD), lambda h, pos, j=j: (pos[j], 0, h)) for j in range(SLOTS)
    ]
    part_spec = pl.BlockSpec((held, rows, HD), lambda h, pos: (0, 0, h))
    flops = 12 * rows * SLOTS * rows * HD * heads
    moved = 2 * SLOTS * rows * width * 2 + 4 * rows * width * 2 + 2 * held * rows * width * 2
    call = pl.pallas_call(
        _attend_kernel,
        out_shape=(
            jax.ShapeDtypeStruct((rows, width), jnp.bfloat16),
            jax.ShapeDtypeStruct((rows, width), jnp.bfloat16),
            jax.ShapeDtypeStruct((held, rows, width), jnp.bfloat16),
            jax.ShapeDtypeStruct((held, rows, width), jnp.bfloat16),
        ),
        grid_spec=pltpu.PrefetchScalarGridSpec(
            num_scalar_prefetch=1,
            grid=(heads,),
            in_specs=[head_spec, head_spec] + slot_specs + slot_specs,
            out_specs=(head_spec, head_spec, part_spec, part_spec),
            scratch_shapes=[pltpu.VMEM((held, rows, HD), jnp.float32)] * 2,
        ),
        compiler_params=pltpu.CompilerParams(dimension_semantics=("arbitrary",)),
        cost_estimate=pl.CostEstimate(
            flops=flops, transcendentals=rows * SLOTS * rows * heads, bytes_accessed=moved
        ),
    )
    return call(
        pos, query, grad_out, *([keys_local] * SLOTS), *([values_local] * SLOTS)
    )


STREAMS = 2


def _stream(pos, query, grad_out, keys, values, after=None):
    n = lax.axis_size("seq")
    rows, width = query.shape
    line_len = n // 4
    if after is not None:
        keys, values, _ = lax.optimization_barrier((keys, values, after))
    keys_local = gather_blocks(keys, n).reshape(n, rows, width)
    values_local = gather_blocks(values, n).reshape(n, rows, width)
    attended, grad_query, part_keys, part_values = attend_local(
        pos, query, grad_out, keys_local, values_local
    )
    scatter = jax.linear_transpose(
        lambda t: gather_blocks(t, n), jax.ShapeDtypeStruct((rows, width), jnp.float32)
    )
    (grad_keys,) = scatter(part_keys.astype(jnp.float32).reshape(2, 2, line_len, rows, width))
    (grad_values,) = scatter(part_values.astype(jnp.float32).reshape(2, 2, line_len, rows, width))
    outs = (attended, grad_query, grad_keys.astype(jnp.bfloat16), grad_values.astype(jnp.bfloat16))
    return outs, (keys_local, values_local)


def shards_gather(query, keys, values, grad_out, global_blocks, random_blocks):
    n = lax.axis_size("seq")
    rows, width = query.shape
    line_len = n // 4
    idx = lax.axis_index("seq")
    listed = jnp.concatenate(
        [
            jnp.stack([idx, (idx - 1) % n, (idx + 1) % n]).astype(jnp.int32),
            global_blocks.astype(jnp.int32),
            random_blocks[idx].astype(jnp.int32),
        ]
    )
    listed = jnp.clip(listed, 0, n - 1)
    core = idx % 2
    ypos = (idx // 2) % 2
    pos = (((listed % 2) ^ core) * 2 + (((listed // 2) % 2) ^ ypos)) * line_len + listed // 4
    cut = width // STREAMS
    outs = []
    after = None
    for s in range(STREAMS):
        cols = slice(s * cut, (s + 1) * cut)
        with jax.named_scope(f"stream{s}"):
            out, after = _stream(
                pos, query[:, cols], grad_out[:, cols], keys[:, cols], values[:, cols], after
            )
            outs.append(out)
    return tuple(jnp.concatenate(parts, axis=1) for parts in zip(*outs))


def shards(query, keys, values, grad_out, global_blocks, random_blocks):
    n = lax.axis_size("seq")
    if query.shape[0] == BLK and n % 4 == 0 and n <= 32:
        return shards_gather(query, keys, values, grad_out, global_blocks, random_blocks)
    return shards_exchange(query, keys, values, grad_out, global_blocks, random_blocks)


def solution(mesh):
    placed = (
        P(("groups", "seq"), None),
        P(("groups", "seq"), None),
        P(("groups", "seq"), None),
        P(("groups", "seq"), None),
        P("groups"),
        P("groups", None),
    )
    return jax.shard_map(
        shards,
        mesh=mesh,
        in_specs=placed,
        out_specs=(
            P(("groups", "seq"), None),
            P(("groups", "seq"), None),
            P(("groups", "seq"), None),
            P(("groups", "seq"), None),
        ),
        check_vma=False,
    )
```

```python
import jax
import jax.numpy as jnp
from jax import lax
from jax.experimental import pallas as pl
from jax.experimental.pallas import tpu as pltpu
from jax.sharding import PartitionSpec as P

HD = 128
BLK = 128
G = 2


def attend_block(operands):
    query_blk, grad_blk, key_tiles, value_tiles = operands
    row_count, width = query_blk.shape
    keys_total = key_tiles.shape[0]
    head_size = HD
    head_count = width // head_size
    scaling = HD ** (-0.5)
    last_dims = (((1,), (1,)), ((), ()))
    first_dims = (((0,), (0,)), ((), ()))

    def one_head(head, carry):
        out_attended, out_gquery, out_gkeys, out_gvalues = carry
        start = head * head_size
        query_head = lax.dynamic_slice_in_dim(query_blk, start, head_size, 1)
        grad_head = lax.dynamic_slice_in_dim(grad_blk, start, head_size, 1)
        key_head = lax.dynamic_slice_in_dim(key_tiles, start, head_size, 1)
        value_head = lax.dynamic_slice_in_dim(value_tiles, start, head_size, 1)
        scores = (
            lax.dot_general(query_head, key_head, last_dims, preferred_element_type=jnp.float32)
            * scaling
        )
        probability = jax.nn.softmax(scores, axis=-1)
        weights = probability.astype(jnp.bfloat16)
        attended_head = jnp.dot(weights, value_head, preferred_element_type=jnp.float32).astype(
            jnp.bfloat16
        )
        deltas = jnp.sum(grad_head.astype(jnp.float32) * attended_head.astype(jnp.float32), axis=-1)
        grad_prob = lax.dot_general(
            grad_head, value_head, last_dims, preferred_element_type=jnp.float32
        )
        grad_score = (probability * (grad_prob - deltas[:, None])).astype(jnp.bfloat16)
        gquery_head = (
            jnp.dot(grad_score, key_head, preferred_element_type=jnp.float32) * scaling
        ).astype(jnp.bfloat16)
        gkeys_head = (
            lax.dot_general(grad_score, query_head, first_dims, preferred_element_type=jnp.float32)
            * scaling
        )
        gvalues_head = lax.dot_general(
            weights, grad_head, first_dims, preferred_element_type=jnp.float32
        )
        out_attended = lax.dynamic_update_slice_in_dim(out_attended, attended_head, start, 1)
        out_gquery = lax.dynamic_update_slice_in_dim(out_gquery, gquery_head, start, 1)
        out_gkeys = lax.dynamic_update_slice_in_dim(out_gkeys, gkeys_head, start, 1)
        out_gvalues = lax.dynamic_update_slice_in_dim(out_gvalues, gvalues_head, start, 1)
        return (out_attended, out_gquery, out_gkeys, out_gvalues)

    initial = (
        jnp.zeros((row_count, width), jnp.bfloat16),
        jnp.zeros((row_count, width), jnp.bfloat16),
        jnp.zeros((keys_total, width), jnp.float32),
        jnp.zeros((keys_total, width), jnp.float32),
    )
    return lax.fori_loop(0, head_count, one_head, initial)


def fetch_table(device_ids, block_count, total_blocks, global_blocks, random_blocks):
    owned_blocks = (
        device_ids[:, None] * block_count + jnp.arange(block_count, dtype=jnp.int32)[None, :]
    )
    pieces = []
    pieces.append(((owned_blocks - 1) % total_blocks)[:, :, None])
    pieces.append(((owned_blocks + 1) % total_blocks)[:, :, None])
    pieces.append(
        jnp.broadcast_to(
            global_blocks[None, None, :], owned_blocks.shape + (global_blocks.shape[0],)
        )
    )
    pieces.append(random_blocks[owned_blocks])
    return jnp.concatenate(pieces, axis=2).reshape(device_ids.shape[0], -1)


def shards_exchange(query, keys, values, grad_out, global_blocks, random_blocks):
    devices = lax.axis_size("seq")
    tok_rows, width = query.shape
    per_device = tok_rows // BLK
    total_blocks = per_device * devices
    row_share = BLK // devices
    key_blocks = keys.reshape(per_device, BLK, width)
    value_blocks = values.reshape(per_device, BLK, width)
    row_keys, row_values = (
        lax.all_to_all(
            keys.reshape(per_device, devices, row_share, width),
            "seq",
            split_axis=1,
            concat_axis=0,
            tiled=True,
        ),
        lax.all_to_all(
            values.reshape(per_device, devices, row_share, width),
            "seq",
            split_axis=1,
            concat_axis=0,
            tiled=True,
        ),
    )
    row_keys = row_keys.reshape(total_blocks, row_share, width)
    row_values = row_values.reshape(total_blocks, row_share, width)
    fetch_lists = fetch_table(
        jnp.arange(devices, dtype=jnp.int32), per_device, total_blocks, global_blocks, random_blocks
    )
    fetched = fetch_lists.shape[1]
    got_keys, got_values = (
        lax.all_to_all(row_keys[fetch_lists], "seq", split_axis=0, concat_axis=2, tiled=True),
        lax.all_to_all(row_values[fetch_lists], "seq", split_axis=0, concat_axis=2, tiled=True),
    )
    offset = 0
    window_keys = got_keys[:, 0:2]
    window_values = got_values[:, 0:2]
    offset = 2
    global_keys = got_keys[:, offset : offset + G]
    global_values = got_values[:, offset : offset + G]
    offset = offset + G
    random_keys = got_keys[:, offset:]
    random_values = got_values[:, offset:]
    tile_keys = jnp.concatenate(
        [key_blocks[:, None], window_keys, global_keys, random_keys], axis=1
    ).reshape(per_device, -1, width)
    tile_values = jnp.concatenate(
        [value_blocks[:, None], window_values, global_values, random_values], axis=1
    ).reshape(per_device, -1, width)
    attended, grad_query, tile_gkeys, tile_gvalues = lax.map(
        attend_block,
        (
            query.reshape(per_device, BLK, width),
            grad_out.reshape(per_device, BLK, width),
            tile_keys,
            tile_values,
        ),
    )
    tile_gkeys = tile_gkeys.reshape(per_device, -1, BLK, width)
    tile_gvalues = tile_gvalues.reshape(per_device, -1, BLK, width)
    window_gkeys = tile_gkeys[:, 1:3]
    window_gvalues = tile_gvalues[:, 1:3]
    global_gkeys = tile_gkeys[:, 3 : 3 + G]
    global_gvalues = tile_gvalues[:, 3 : 3 + G]
    back_keys = []
    back_values = []
    back_keys.append(window_gkeys)
    back_values.append(window_gvalues)
    back_keys.append(global_gkeys)
    back_values.append(global_gvalues)
    back_keys.append(tile_gkeys[:, 3 + G :])
    back_values.append(tile_gvalues[:, 3 + G :])
    back_keys = jnp.concatenate(back_keys, axis=1).reshape(1, fetched, devices, row_share, width)
    back_values = jnp.concatenate(back_values, axis=1).reshape(
        1, fetched, devices, row_share, width
    )
    recv_keys, recv_values = (
        lax.all_to_all(back_keys, "seq", split_axis=2, concat_axis=0, tiled=True),
        lax.all_to_all(back_values, "seq", split_axis=2, concat_axis=0, tiled=True),
    )
    flat_index = fetch_lists.reshape(-1)
    table_keys = (
        jnp.zeros((total_blocks, row_share, width), jnp.float32)
        .at[flat_index]
        .add(recv_keys.reshape(devices * fetched, row_share, width))
    )
    table_values = (
        jnp.zeros((total_blocks, row_share, width), jnp.float32)
        .at[flat_index]
        .add(recv_values.reshape(devices * fetched, row_share, width))
    )
    home_keys, home_values = (
        lax.all_to_all(
            table_keys.reshape(total_blocks, 1, row_share, width),
            "seq",
            split_axis=0,
            concat_axis=1,
            tiled=True,
        ),
        lax.all_to_all(
            table_values.reshape(total_blocks, 1, row_share, width),
            "seq",
            split_axis=0,
            concat_axis=1,
            tiled=True,
        ),
    )
    grad_key_blocks = tile_gkeys[:, 0] + home_keys.reshape(per_device, BLK, width)
    grad_value_blocks = tile_gvalues[:, 0] + home_values.reshape(per_device, BLK, width)
    return (
        attended.reshape(tok_rows, width),
        grad_query.reshape(tok_rows, width),
        grad_key_blocks.astype(jnp.bfloat16).reshape(tok_rows, width),
        grad_value_blocks.astype(jnp.bfloat16).reshape(tok_rows, width),
    )

SLOTS = 3 + G + 3


def _send(v, pairs):
    return lax.ppermute(v.astype(jnp.bfloat16), "seq", pairs).astype(v.dtype)


def gather_blocks(x, n):
    line_len = n // 4
    z = lax.axis_index("seq") // 4
    ups, downs = [], []
    up, down = x, x
    for k in range(1, line_len):
        up = _send(
            up, [(4 * z0 + r, 4 * (z0 + 1) + r) for z0 in range(k - 1, line_len - 1) for r in range(4)]
        )
        down = _send(
            down, [(4 * z0 + r, 4 * (z0 - 1) + r) for z0 in range(1, line_len - k + 1) for r in range(4)]
        )
        ups.append(up)
        downs.append(down)
    rel = jnp.stack(ups[::-1] + [x] + downs)
    line = lax.dynamic_slice_in_dim(rel, line_len - 1 - z, line_len, axis=0)
    other = _send(line, [(i, i ^ 2) for i in range(n)])
    pair = jnp.stack([line, other])
    sibling = _send(pair, [(i, i ^ 1) for i in range(n)])
    return jnp.stack([pair, sibling])


HEADS_PER_STEP = 2


def _attend_kernel(pos_ref, q_ref, g_ref, *refs):
    k_refs = refs[:SLOTS]
    v_refs = refs[SLOTS : 2 * SLOTS]
    att_ref, gq_ref, dk_ref, dv_ref, dk_acc, dv_acc = refs[2 * SLOTS :]
    scale = HD ** (-0.5)
    nt = (((1,), (1,)), ((), ()))
    tn = (((0,), (0,)), ((), ()))
    rows = q_ref.shape[0]
    empty = jnp.zeros((rows, dk_acc.shape[-1]), jnp.float32)
    for j in range(SLOTS):
        dk_acc[pos_ref[j]] = empty
        dv_acc[pos_ref[j]] = empty
    for hh in range(q_ref.shape[1] // HD):
        cols = slice(hh * HD, (hh + 1) * HD)
        q = q_ref[:, cols]
        g = g_ref[:, cols]
        k_all = jnp.concatenate([r[:, cols] for r in k_refs], axis=0)
        v_all = jnp.concatenate([r[:, cols] for r in v_refs], axis=0)
        s = lax.dot_general(q, k_all, nt, preferred_element_type=jnp.float32) * scale
        e = jnp.exp(s - jnp.max(s, axis=-1, keepdims=True))
        p = e / jnp.sum(e, axis=-1, keepdims=True)
        w = p.astype(jnp.bfloat16)
        att = jnp.dot(w, v_all, preferred_element_type=jnp.float32).astype(jnp.bfloat16)
        att_ref[:, cols] = att
        delta = jnp.sum(g.astype(jnp.float32) * att.astype(jnp.float32), axis=-1, keepdims=True)
        gp = lax.dot_general(g, v_all, nt, preferred_element_type=jnp.float32)
        gs = (p * (gp - delta)).astype(jnp.bfloat16)
        gq_ref[:, cols] = (jnp.dot(gs, k_all, preferred_element_type=jnp.float32) * scale).astype(
            jnp.bfloat16
        )
        gk = lax.dot_general(gs, q, tn, preferred_element_type=jnp.float32) * scale
        gv = lax.dot_general(w, g, tn, preferred_element_type=jnp.float32)
        for j in range(SLOTS):
            at = pos_ref[j]
            dk_acc[at, :, cols] = dk_acc[at, :, cols] + gk[j * rows : (j + 1) * rows]
            dv_acc[at, :, cols] = dv_acc[at, :, cols] + gv[j * rows : (j + 1) * rows]
    dk_ref[...] = jnp.zeros(dk_ref.shape, dk_ref.dtype)
    dv_ref[...] = jnp.zeros(dv_ref.shape, dv_ref.dtype)
    for j in range(SLOTS):
        at = pos_ref[j]
        dk_ref[at] = dk_acc[at].astype(dk_ref.dtype)
        dv_ref[at] = dv_acc[at].astype(dv_ref.dtype)


def attend_local(pos, query, grad_out, keys_local, values_local):
    rows, width = query.shape
    held = keys_local.shape[0]
    step = HEADS_PER_STEP * HD if (width // HD) % HEADS_PER_STEP == 0 else HD
    heads = width // HD
    head_spec = pl.BlockSpec((rows, step), lambda h, pos: (0, h))
    slot_specs = [
        pl.BlockSpec((None, rows, step), lambda h, pos, j=j: (pos[j], 0, h)) for j in range(SLOTS)
    ]
    part_spec = pl.BlockSpec((held, rows, step), lambda h, pos: (0, 0, h))
    flops = 12 * rows * SLOTS * rows * HD * heads
    moved = 2 * SLOTS * rows * width * 2 + 4 * rows * width * 2 + 2 * held * rows * width * 2
    call = pl.pallas_call(
        _attend_kernel,
        out_shape=(
            jax.ShapeDtypeStruct((rows, width), jnp.bfloat16),
            jax.ShapeDtypeStruct((rows, width), jnp.bfloat16),
            jax.ShapeDtypeStruct((held, rows, width), jnp.bfloat16),
            jax.ShapeDtypeStruct((held, rows, width), jnp.bfloat16),
        ),
        grid_spec=pltpu.PrefetchScalarGridSpec(
            num_scalar_prefetch=1,
            grid=(width // step,),
            in_specs=[head_spec, head_spec] + slot_specs + slot_specs,
            out_specs=(head_spec, head_spec, part_spec, part_spec),
            scratch_shapes=[pltpu.VMEM((held, rows, step), jnp.float32)] * 2,
        ),
        compiler_params=pltpu.CompilerParams(dimension_semantics=("arbitrary",)),
        cost_estimate=pl.CostEstimate(
            flops=flops, transcendentals=rows * SLOTS * rows * heads, bytes_accessed=moved
        ),
    )
    return call(
        pos, query, grad_out, *([keys_local] * SLOTS), *([values_local] * SLOTS)
    )


STREAMS = 2


def _stream(pos, query, grad_out, keys, values, after=None):
    n = lax.axis_size("seq")
    rows, width = query.shape
    line_len = n // 4
    if after is not None:
        keys, values, _ = lax.optimization_barrier((keys, values, after))
    keys_local = gather_blocks(keys, n).reshape(n, rows, width)
    values_local = gather_blocks(values, n).reshape(n, rows, width)
    attended, grad_query, part_keys, part_values = attend_local(
        pos, query, grad_out, keys_local, values_local
    )
    scatter = jax.linear_transpose(
        lambda t: gather_blocks(t, n), jax.ShapeDtypeStruct((rows, width), jnp.float32)
    )
    (grad_keys,) = scatter(part_keys.astype(jnp.float32).reshape(2, 2, line_len, rows, width))
    (grad_values,) = scatter(part_values.astype(jnp.float32).reshape(2, 2, line_len, rows, width))
    outs = (attended, grad_query, grad_keys.astype(jnp.bfloat16), grad_values.astype(jnp.bfloat16))
    return outs, (keys_local, values_local)


def shards_gather(query, keys, values, grad_out, global_blocks, random_blocks):
    n = lax.axis_size("seq")
    rows, width = query.shape
    line_len = n // 4
    idx = lax.axis_index("seq")
    listed = jnp.concatenate(
        [
            jnp.stack([idx, (idx - 1) % n, (idx + 1) % n]).astype(jnp.int32),
            global_blocks.astype(jnp.int32),
            random_blocks[idx].astype(jnp.int32),
        ]
    )
    listed = jnp.clip(listed, 0, n - 1)
    core = idx % 2
    ypos = (idx // 2) % 2
    pos = (((listed % 2) ^ core) * 2 + (((listed // 2) % 2) ^ ypos)) * line_len + listed // 4
    cut = width // STREAMS
    outs = []
    after = None
    for s in range(STREAMS):
        cols = slice(s * cut, (s + 1) * cut)
        with jax.named_scope(f"stream{s}"):
            out, after = _stream(
                pos, query[:, cols], grad_out[:, cols], keys[:, cols], values[:, cols], after
            )
            outs.append(out)
    return tuple(jnp.concatenate(parts, axis=1) for parts in zip(*outs))


def shards(query, keys, values, grad_out, global_blocks, random_blocks):
    n = lax.axis_size("seq")
    if query.shape[0] == BLK and n % 4 == 0 and n <= 32:
        return shards_gather(query, keys, values, grad_out, global_blocks, random_blocks)
    return shards_exchange(query, keys, values, grad_out, global_blocks, random_blocks)


def solution(mesh):
    placed = (
        P(("groups", "seq"), None),
        P(("groups", "seq"), None),
        P(("groups", "seq"), None),
        P(("groups", "seq"), None),
        P("groups"),
        P("groups", None),
    )
    return jax.shard_map(
        shards,
        mesh=mesh,
        in_specs=placed,
        out_specs=(
            P(("groups", "seq"), None),
            P(("groups", "seq"), None),
            P(("groups", "seq"), None),
            P(("groups", "seq"), None),
        ),
        check_vma=False,
    )
```

```python
import jax
import jax.numpy as jnp
from jax import lax
from jax.experimental import pallas as pl
from jax.experimental.pallas import tpu as pltpu
from jax.sharding import PartitionSpec as P

HD = 128
BLK = 128
G = 2


def attend_block(operands):
    query_blk, grad_blk, key_tiles, value_tiles = operands
    row_count, width = query_blk.shape
    keys_total = key_tiles.shape[0]
    head_size = HD
    head_count = width // head_size
    scaling = HD ** (-0.5)
    last_dims = (((1,), (1,)), ((), ()))
    first_dims = (((0,), (0,)), ((), ()))

    def one_head(head, carry):
        out_attended, out_gquery, out_gkeys, out_gvalues = carry
        start = head * head_size
        query_head = lax.dynamic_slice_in_dim(query_blk, start, head_size, 1)
        grad_head = lax.dynamic_slice_in_dim(grad_blk, start, head_size, 1)
        key_head = lax.dynamic_slice_in_dim(key_tiles, start, head_size, 1)
        value_head = lax.dynamic_slice_in_dim(value_tiles, start, head_size, 1)
        scores = (
            lax.dot_general(query_head, key_head, last_dims, preferred_element_type=jnp.float32)
            * scaling
        )
        probability = jax.nn.softmax(scores, axis=-1)
        weights = probability.astype(jnp.bfloat16)
        attended_head = jnp.dot(weights, value_head, preferred_element_type=jnp.float32).astype(
            jnp.bfloat16
        )
        deltas = jnp.sum(grad_head.astype(jnp.float32) * attended_head.astype(jnp.float32), axis=-1)
        grad_prob = lax.dot_general(
            grad_head, value_head, last_dims, preferred_element_type=jnp.float32
        )
        grad_score = (probability * (grad_prob - deltas[:, None])).astype(jnp.bfloat16)
        gquery_head = (
            jnp.dot(grad_score, key_head, preferred_element_type=jnp.float32) * scaling
        ).astype(jnp.bfloat16)
        gkeys_head = (
            lax.dot_general(grad_score, query_head, first_dims, preferred_element_type=jnp.float32)
            * scaling
        )
        gvalues_head = lax.dot_general(
            weights, grad_head, first_dims, preferred_element_type=jnp.float32
        )
        out_attended = lax.dynamic_update_slice_in_dim(out_attended, attended_head, start, 1)
        out_gquery = lax.dynamic_update_slice_in_dim(out_gquery, gquery_head, start, 1)
        out_gkeys = lax.dynamic_update_slice_in_dim(out_gkeys, gkeys_head, start, 1)
        out_gvalues = lax.dynamic_update_slice_in_dim(out_gvalues, gvalues_head, start, 1)
        return (out_attended, out_gquery, out_gkeys, out_gvalues)

    initial = (
        jnp.zeros((row_count, width), jnp.bfloat16),
        jnp.zeros((row_count, width), jnp.bfloat16),
        jnp.zeros((keys_total, width), jnp.float32),
        jnp.zeros((keys_total, width), jnp.float32),
    )
    return lax.fori_loop(0, head_count, one_head, initial)


def fetch_table(device_ids, block_count, total_blocks, global_blocks, random_blocks):
    owned_blocks = (
        device_ids[:, None] * block_count + jnp.arange(block_count, dtype=jnp.int32)[None, :]
    )
    pieces = []
    pieces.append(((owned_blocks - 1) % total_blocks)[:, :, None])
    pieces.append(((owned_blocks + 1) % total_blocks)[:, :, None])
    pieces.append(
        jnp.broadcast_to(
            global_blocks[None, None, :], owned_blocks.shape + (global_blocks.shape[0],)
        )
    )
    pieces.append(random_blocks[owned_blocks])
    return jnp.concatenate(pieces, axis=2).reshape(device_ids.shape[0], -1)


def shards_exchange(query, keys, values, grad_out, global_blocks, random_blocks):
    devices = lax.axis_size("seq")
    tok_rows, width = query.shape
    per_device = tok_rows // BLK
    total_blocks = per_device * devices
    row_share = BLK // devices
    key_blocks = keys.reshape(per_device, BLK, width)
    value_blocks = values.reshape(per_device, BLK, width)
    row_keys, row_values = (
        lax.all_to_all(
            keys.reshape(per_device, devices, row_share, width),
            "seq",
            split_axis=1,
            concat_axis=0,
            tiled=True,
        ),
        lax.all_to_all(
            values.reshape(per_device, devices, row_share, width),
            "seq",
            split_axis=1,
            concat_axis=0,
            tiled=True,
        ),
    )
    row_keys = row_keys.reshape(total_blocks, row_share, width)
    row_values = row_values.reshape(total_blocks, row_share, width)
    fetch_lists = fetch_table(
        jnp.arange(devices, dtype=jnp.int32), per_device, total_blocks, global_blocks, random_blocks
    )
    fetched = fetch_lists.shape[1]
    got_keys, got_values = (
        lax.all_to_all(row_keys[fetch_lists], "seq", split_axis=0, concat_axis=2, tiled=True),
        lax.all_to_all(row_values[fetch_lists], "seq", split_axis=0, concat_axis=2, tiled=True),
    )
    offset = 0
    window_keys = got_keys[:, 0:2]
    window_values = got_values[:, 0:2]
    offset = 2
    global_keys = got_keys[:, offset : offset + G]
    global_values = got_values[:, offset : offset + G]
    offset = offset + G
    random_keys = got_keys[:, offset:]
    random_values = got_values[:, offset:]
    tile_keys = jnp.concatenate(
        [key_blocks[:, None], window_keys, global_keys, random_keys], axis=1
    ).reshape(per_device, -1, width)
    tile_values = jnp.concatenate(
        [value_blocks[:, None], window_values, global_values, random_values], axis=1
    ).reshape(per_device, -1, width)
    attended, grad_query, tile_gkeys, tile_gvalues = lax.map(
        attend_block,
        (
            query.reshape(per_device, BLK, width),
            grad_out.reshape(per_device, BLK, width),
            tile_keys,
            tile_values,
        ),
    )
    tile_gkeys = tile_gkeys.reshape(per_device, -1, BLK, width)
    tile_gvalues = tile_gvalues.reshape(per_device, -1, BLK, width)
    window_gkeys = tile_gkeys[:, 1:3]
    window_gvalues = tile_gvalues[:, 1:3]
    global_gkeys = tile_gkeys[:, 3 : 3 + G]
    global_gvalues = tile_gvalues[:, 3 : 3 + G]
    back_keys = []
    back_values = []
    back_keys.append(window_gkeys)
    back_values.append(window_gvalues)
    back_keys.append(global_gkeys)
    back_values.append(global_gvalues)
    back_keys.append(tile_gkeys[:, 3 + G :])
    back_values.append(tile_gvalues[:, 3 + G :])
    back_keys = jnp.concatenate(back_keys, axis=1).reshape(1, fetched, devices, row_share, width)
    back_values = jnp.concatenate(back_values, axis=1).reshape(
        1, fetched, devices, row_share, width
    )
    recv_keys, recv_values = (
        lax.all_to_all(back_keys, "seq", split_axis=2, concat_axis=0, tiled=True),
        lax.all_to_all(back_values, "seq", split_axis=2, concat_axis=0, tiled=True),
    )
    flat_index = fetch_lists.reshape(-1)
    table_keys = (
        jnp.zeros((total_blocks, row_share, width), jnp.float32)
        .at[flat_index]
        .add(recv_keys.reshape(devices * fetched, row_share, width))
    )
    table_values = (
        jnp.zeros((total_blocks, row_share, width), jnp.float32)
        .at[flat_index]
        .add(recv_values.reshape(devices * fetched, row_share, width))
    )
    home_keys, home_values = (
        lax.all_to_all(
            table_keys.reshape(total_blocks, 1, row_share, width),
            "seq",
            split_axis=0,
            concat_axis=1,
            tiled=True,
        ),
        lax.all_to_all(
            table_values.reshape(total_blocks, 1, row_share, width),
            "seq",
            split_axis=0,
            concat_axis=1,
            tiled=True,
        ),
    )
    grad_key_blocks = tile_gkeys[:, 0] + home_keys.reshape(per_device, BLK, width)
    grad_value_blocks = tile_gvalues[:, 0] + home_values.reshape(per_device, BLK, width)
    return (
        attended.reshape(tok_rows, width),
        grad_query.reshape(tok_rows, width),
        grad_key_blocks.astype(jnp.bfloat16).reshape(tok_rows, width),
        grad_value_blocks.astype(jnp.bfloat16).reshape(tok_rows, width),
    )

SLOTS = 3 + G + 3


def _send(v, pairs):
    return lax.ppermute(v.astype(jnp.bfloat16), "seq", pairs).astype(v.dtype)


def gather_blocks(x, n):
    line_len = n // 4
    z = lax.axis_index("seq") // 4
    ups, downs = [], []
    up, down = x, x
    for k in range(1, line_len):
        up = _send(
            up, [(4 * z0 + r, 4 * (z0 + 1) + r) for z0 in range(k - 1, line_len - 1) for r in range(4)]
        )
        down = _send(
            down, [(4 * z0 + r, 4 * (z0 - 1) + r) for z0 in range(1, line_len - k + 1) for r in range(4)]
        )
        ups.append(up)
        downs.append(down)
    rel = jnp.stack(ups[::-1] + [x] + downs)
    line = lax.dynamic_slice_in_dim(rel, line_len - 1 - z, line_len, axis=0)
    other = _send(line, [(i, i ^ 2) for i in range(n)])
    pair = jnp.stack([line, other])
    sibling = _send(pair, [(i, i ^ 1) for i in range(n)])
    return jnp.stack([pair, sibling])


HEADS_PER_STEP = 4


def _attend_kernel(pos_ref, q_ref, g_ref, *refs):
    k_refs = refs[:SLOTS]
    v_refs = refs[SLOTS : 2 * SLOTS]
    att_ref, gq_ref, dk_ref, dv_ref, dk_acc, dv_acc = refs[2 * SLOTS :]
    scale = HD ** (-0.5)
    nt = (((1,), (1,)), ((), ()))
    tn = (((0,), (0,)), ((), ()))
    rows = q_ref.shape[0]
    empty = jnp.zeros((rows, dk_acc.shape[-1]), jnp.float32)
    for j in range(SLOTS):
        dk_acc[pos_ref[j]] = empty
        dv_acc[pos_ref[j]] = empty
    for hh in range(q_ref.shape[1] // HD):
        cols = slice(hh * HD, (hh + 1) * HD)
        q = q_ref[:, cols]
        g = g_ref[:, cols]
        k_all = jnp.concatenate([r[:, cols] for r in k_refs], axis=0)
        v_all = jnp.concatenate([r[:, cols] for r in v_refs], axis=0)
        s = lax.dot_general(q, k_all, nt, preferred_element_type=jnp.float32) * scale
        e = jnp.exp(s - jnp.max(s, axis=-1, keepdims=True))
        p = e / jnp.sum(e, axis=-1, keepdims=True)
        w = p.astype(jnp.bfloat16)
        att = jnp.dot(w, v_all, preferred_element_type=jnp.float32).astype(jnp.bfloat16)
        att_ref[:, cols] = att
        delta = jnp.sum(g.astype(jnp.float32) * att.astype(jnp.float32), axis=-1, keepdims=True)
        gp = lax.dot_general(g, v_all, nt, preferred_element_type=jnp.float32)
        gs = (p * (gp - delta)).astype(jnp.bfloat16)
        gq_ref[:, cols] = (jnp.dot(gs, k_all, preferred_element_type=jnp.float32) * scale).astype(
            jnp.bfloat16
        )
        gk = lax.dot_general(gs, q, tn, preferred_element_type=jnp.float32) * scale
        gv = lax.dot_general(w, g, tn, preferred_element_type=jnp.float32)
        for j in range(SLOTS):
            at = pos_ref[j]
            dk_acc[at, :, cols] = dk_acc[at, :, cols] + gk[j * rows : (j + 1) * rows]
            dv_acc[at, :, cols] = dv_acc[at, :, cols] + gv[j * rows : (j + 1) * rows]
    dk_ref[...] = jnp.zeros(dk_ref.shape, dk_ref.dtype)
    dv_ref[...] = jnp.zeros(dv_ref.shape, dv_ref.dtype)
    for j in range(SLOTS):
        at = pos_ref[j]
        dk_ref[at] = dk_acc[at].astype(dk_ref.dtype)
        dv_ref[at] = dv_acc[at].astype(dv_ref.dtype)


def attend_local(pos, query, grad_out, keys_local, values_local):
    rows, width = query.shape
    held = keys_local.shape[0]
    step = HEADS_PER_STEP * HD if (width // HD) % HEADS_PER_STEP == 0 else HD
    heads = width // HD
    head_spec = pl.BlockSpec((rows, step), lambda h, pos: (0, h))
    slot_specs = [
        pl.BlockSpec((None, rows, step), lambda h, pos, j=j: (pos[j], 0, h)) for j in range(SLOTS)
    ]
    part_spec = pl.BlockSpec((held, rows, step), lambda h, pos: (0, 0, h))
    flops = 12 * rows * SLOTS * rows * HD * heads
    moved = 2 * SLOTS * rows * width * 2 + 4 * rows * width * 2 + 2 * held * rows * width * 2
    call = pl.pallas_call(
        _attend_kernel,
        out_shape=(
            jax.ShapeDtypeStruct((rows, width), jnp.bfloat16),
            jax.ShapeDtypeStruct((rows, width), jnp.bfloat16),
            jax.ShapeDtypeStruct((held, rows, width), jnp.bfloat16),
            jax.ShapeDtypeStruct((held, rows, width), jnp.bfloat16),
        ),
        grid_spec=pltpu.PrefetchScalarGridSpec(
            num_scalar_prefetch=1,
            grid=(width // step,),
            in_specs=[head_spec, head_spec] + slot_specs + slot_specs,
            out_specs=(head_spec, head_spec, part_spec, part_spec),
            scratch_shapes=[pltpu.VMEM((held, rows, step), jnp.float32)] * 2,
        ),
        compiler_params=pltpu.CompilerParams(dimension_semantics=("arbitrary",)),
        cost_estimate=pl.CostEstimate(
            flops=flops, transcendentals=rows * SLOTS * rows * heads, bytes_accessed=moved
        ),
    )
    return call(
        pos, query, grad_out, *([keys_local] * SLOTS), *([values_local] * SLOTS)
    )


STREAMS = 2


def _stream(pos, query, grad_out, keys, values, after=None):
    n = lax.axis_size("seq")
    rows, width = query.shape
    line_len = n // 4
    if after is not None:
        keys, values, _ = lax.optimization_barrier((keys, values, after))
    keys_local = gather_blocks(keys, n).reshape(n, rows, width)
    values_local = gather_blocks(values, n).reshape(n, rows, width)
    attended, grad_query, part_keys, part_values = attend_local(
        pos, query, grad_out, keys_local, values_local
    )
    scatter = jax.linear_transpose(
        lambda t: gather_blocks(t, n), jax.ShapeDtypeStruct((rows, width), jnp.float32)
    )
    (grad_keys,) = scatter(part_keys.astype(jnp.float32).reshape(2, 2, line_len, rows, width))
    (grad_values,) = scatter(part_values.astype(jnp.float32).reshape(2, 2, line_len, rows, width))
    outs = (attended, grad_query, grad_keys.astype(jnp.bfloat16), grad_values.astype(jnp.bfloat16))
    return outs, (keys_local, values_local)


def shards_gather(query, keys, values, grad_out, global_blocks, random_blocks):
    n = lax.axis_size("seq")
    rows, width = query.shape
    line_len = n // 4
    idx = lax.axis_index("seq")
    listed = jnp.concatenate(
        [
            jnp.stack([idx, (idx - 1) % n, (idx + 1) % n]).astype(jnp.int32),
            global_blocks.astype(jnp.int32),
            random_blocks[idx].astype(jnp.int32),
        ]
    )
    listed = jnp.clip(listed, 0, n - 1)
    core = idx % 2
    ypos = (idx // 2) % 2
    pos = (((listed % 2) ^ core) * 2 + (((listed // 2) % 2) ^ ypos)) * line_len + listed // 4
    cut = width // STREAMS
    outs = []
    after = None
    for s in range(STREAMS):
        cols = slice(s * cut, (s + 1) * cut)
        with jax.named_scope(f"stream{s}"):
            out, after = _stream(
                pos, query[:, cols], grad_out[:, cols], keys[:, cols], values[:, cols], after
            )
            outs.append(out)
    return tuple(jnp.concatenate(parts, axis=1) for parts in zip(*outs))


def shards(query, keys, values, grad_out, global_blocks, random_blocks):
    n = lax.axis_size("seq")
    if query.shape[0] == BLK and n % 4 == 0 and n <= 32:
        return shards_gather(query, keys, values, grad_out, global_blocks, random_blocks)
    return shards_exchange(query, keys, values, grad_out, global_blocks, random_blocks)


def solution(mesh):
    placed = (
        P(("groups", "seq"), None),
        P(("groups", "seq"), None),
        P(("groups", "seq"), None),
        P(("groups", "seq"), None),
        P("groups"),
        P("groups", None),
    )
    return jax.shard_map(
        shards,
        mesh=mesh,
        in_specs=placed,
        out_specs=(
            P(("groups", "seq"), None),
            P(("groups", "seq"), None),
            P(("groups", "seq"), None),
            P(("groups", "seq"), None),
        ),
        check_vma=False,
    )
```

```python
import jax
import jax.numpy as jnp
from jax import lax
from jax.experimental import pallas as pl
from jax.experimental.pallas import tpu as pltpu
from jax.sharding import PartitionSpec as P

HD = 128
BLK = 128
G = 2


def attend_block(operands):
    query_blk, grad_blk, key_tiles, value_tiles = operands
    row_count, width = query_blk.shape
    keys_total = key_tiles.shape[0]
    head_size = HD
    head_count = width // head_size
    scaling = HD ** (-0.5)
    last_dims = (((1,), (1,)), ((), ()))
    first_dims = (((0,), (0,)), ((), ()))

    def one_head(head, carry):
        out_attended, out_gquery, out_gkeys, out_gvalues = carry
        start = head * head_size
        query_head = lax.dynamic_slice_in_dim(query_blk, start, head_size, 1)
        grad_head = lax.dynamic_slice_in_dim(grad_blk, start, head_size, 1)
        key_head = lax.dynamic_slice_in_dim(key_tiles, start, head_size, 1)
        value_head = lax.dynamic_slice_in_dim(value_tiles, start, head_size, 1)
        scores = (
            lax.dot_general(query_head, key_head, last_dims, preferred_element_type=jnp.float32)
            * scaling
        )
        probability = jax.nn.softmax(scores, axis=-1)
        weights = probability.astype(jnp.bfloat16)
        attended_head = jnp.dot(weights, value_head, preferred_element_type=jnp.float32).astype(
            jnp.bfloat16
        )
        deltas = jnp.sum(grad_head.astype(jnp.float32) * attended_head.astype(jnp.float32), axis=-1)
        grad_prob = lax.dot_general(
            grad_head, value_head, last_dims, preferred_element_type=jnp.float32
        )
        grad_score = (probability * (grad_prob - deltas[:, None])).astype(jnp.bfloat16)
        gquery_head = (
            jnp.dot(grad_score, key_head, preferred_element_type=jnp.float32) * scaling
        ).astype(jnp.bfloat16)
        gkeys_head = (
            lax.dot_general(grad_score, query_head, first_dims, preferred_element_type=jnp.float32)
            * scaling
        )
        gvalues_head = lax.dot_general(
            weights, grad_head, first_dims, preferred_element_type=jnp.float32
        )
        out_attended = lax.dynamic_update_slice_in_dim(out_attended, attended_head, start, 1)
        out_gquery = lax.dynamic_update_slice_in_dim(out_gquery, gquery_head, start, 1)
        out_gkeys = lax.dynamic_update_slice_in_dim(out_gkeys, gkeys_head, start, 1)
        out_gvalues = lax.dynamic_update_slice_in_dim(out_gvalues, gvalues_head, start, 1)
        return (out_attended, out_gquery, out_gkeys, out_gvalues)

    initial = (
        jnp.zeros((row_count, width), jnp.bfloat16),
        jnp.zeros((row_count, width), jnp.bfloat16),
        jnp.zeros((keys_total, width), jnp.float32),
        jnp.zeros((keys_total, width), jnp.float32),
    )
    return lax.fori_loop(0, head_count, one_head, initial)


def fetch_table(device_ids, block_count, total_blocks, global_blocks, random_blocks):
    owned_blocks = (
        device_ids[:, None] * block_count + jnp.arange(block_count, dtype=jnp.int32)[None, :]
    )
    pieces = []
    pieces.append(((owned_blocks - 1) % total_blocks)[:, :, None])
    pieces.append(((owned_blocks + 1) % total_blocks)[:, :, None])
    pieces.append(
        jnp.broadcast_to(
            global_blocks[None, None, :], owned_blocks.shape + (global_blocks.shape[0],)
        )
    )
    pieces.append(random_blocks[owned_blocks])
    return jnp.concatenate(pieces, axis=2).reshape(device_ids.shape[0], -1)


def shards_exchange(query, keys, values, grad_out, global_blocks, random_blocks):
    devices = lax.axis_size("seq")
    tok_rows, width = query.shape
    per_device = tok_rows // BLK
    total_blocks = per_device * devices
    row_share = BLK // devices
    key_blocks = keys.reshape(per_device, BLK, width)
    value_blocks = values.reshape(per_device, BLK, width)
    row_keys, row_values = (
        lax.all_to_all(
            keys.reshape(per_device, devices, row_share, width),
            "seq",
            split_axis=1,
            concat_axis=0,
            tiled=True,
        ),
        lax.all_to_all(
            values.reshape(per_device, devices, row_share, width),
            "seq",
            split_axis=1,
            concat_axis=0,
            tiled=True,
        ),
    )
    row_keys = row_keys.reshape(total_blocks, row_share, width)
    row_values = row_values.reshape(total_blocks, row_share, width)
    fetch_lists = fetch_table(
        jnp.arange(devices, dtype=jnp.int32), per_device, total_blocks, global_blocks, random_blocks
    )
    fetched = fetch_lists.shape[1]
    got_keys, got_values = (
        lax.all_to_all(row_keys[fetch_lists], "seq", split_axis=0, concat_axis=2, tiled=True),
        lax.all_to_all(row_values[fetch_lists], "seq", split_axis=0, concat_axis=2, tiled=True),
    )
    offset = 0
    window_keys = got_keys[:, 0:2]
    window_values = got_values[:, 0:2]
    offset = 2
    global_keys = got_keys[:, offset : offset + G]
    global_values = got_values[:, offset : offset + G]
    offset = offset + G
    random_keys = got_keys[:, offset:]
    random_values = got_values[:, offset:]
    tile_keys = jnp.concatenate(
        [key_blocks[:, None], window_keys, global_keys, random_keys], axis=1
    ).reshape(per_device, -1, width)
    tile_values = jnp.concatenate(
        [value_blocks[:, None], window_values, global_values, random_values], axis=1
    ).reshape(per_device, -1, width)
    attended, grad_query, tile_gkeys, tile_gvalues = lax.map(
        attend_block,
        (
            query.reshape(per_device, BLK, width),
            grad_out.reshape(per_device, BLK, width),
            tile_keys,
            tile_values,
        ),
    )
    tile_gkeys = tile_gkeys.reshape(per_device, -1, BLK, width)
    tile_gvalues = tile_gvalues.reshape(per_device, -1, BLK, width)
    window_gkeys = tile_gkeys[:, 1:3]
    window_gvalues = tile_gvalues[:, 1:3]
    global_gkeys = tile_gkeys[:, 3 : 3 + G]
    global_gvalues = tile_gvalues[:, 3 : 3 + G]
    back_keys = []
    back_values = []
    back_keys.append(window_gkeys)
    back_values.append(window_gvalues)
    back_keys.append(global_gkeys)
    back_values.append(global_gvalues)
    back_keys.append(tile_gkeys[:, 3 + G :])
    back_values.append(tile_gvalues[:, 3 + G :])
    back_keys = jnp.concatenate(back_keys, axis=1).reshape(1, fetched, devices, row_share, width)
    back_values = jnp.concatenate(back_values, axis=1).reshape(
        1, fetched, devices, row_share, width
    )
    recv_keys, recv_values = (
        lax.all_to_all(back_keys, "seq", split_axis=2, concat_axis=0, tiled=True),
        lax.all_to_all(back_values, "seq", split_axis=2, concat_axis=0, tiled=True),
    )
    flat_index = fetch_lists.reshape(-1)
    table_keys = (
        jnp.zeros((total_blocks, row_share, width), jnp.float32)
        .at[flat_index]
        .add(recv_keys.reshape(devices * fetched, row_share, width))
    )
    table_values = (
        jnp.zeros((total_blocks, row_share, width), jnp.float32)
        .at[flat_index]
        .add(recv_values.reshape(devices * fetched, row_share, width))
    )
    home_keys, home_values = (
        lax.all_to_all(
            table_keys.reshape(total_blocks, 1, row_share, width),
            "seq",
            split_axis=0,
            concat_axis=1,
            tiled=True,
        ),
        lax.all_to_all(
            table_values.reshape(total_blocks, 1, row_share, width),
            "seq",
            split_axis=0,
            concat_axis=1,
            tiled=True,
        ),
    )
    grad_key_blocks = tile_gkeys[:, 0] + home_keys.reshape(per_device, BLK, width)
    grad_value_blocks = tile_gvalues[:, 0] + home_values.reshape(per_device, BLK, width)
    return (
        attended.reshape(tok_rows, width),
        grad_query.reshape(tok_rows, width),
        grad_key_blocks.astype(jnp.bfloat16).reshape(tok_rows, width),
        grad_value_blocks.astype(jnp.bfloat16).reshape(tok_rows, width),
    )

SLOTS = 3 + G + 3


def _send(v, pairs):
    return lax.ppermute(v.astype(jnp.bfloat16), "seq", pairs).astype(v.dtype)


def gather_blocks(x, n):
    line_len = n // 4
    z = lax.axis_index("seq") // 4
    ups, downs = [], []
    up, down = x, x
    for k in range(1, line_len):
        up = _send(
            up, [(4 * z0 + r, 4 * (z0 + 1) + r) for z0 in range(k - 1, line_len - 1) for r in range(4)]
        )
        down = _send(
            down, [(4 * z0 + r, 4 * (z0 - 1) + r) for z0 in range(1, line_len - k + 1) for r in range(4)]
        )
        ups.append(up)
        downs.append(down)
    rel = jnp.stack(ups[::-1] + [x] + downs)
    line = lax.dynamic_slice_in_dim(rel, line_len - 1 - z, line_len, axis=0)
    other = _send(line, [(i, i ^ 2) for i in range(n)])
    pair = jnp.stack([line, other])
    sibling = _send(pair, [(i, i ^ 1) for i in range(n)])
    return jnp.stack([pair, sibling]), line


HEADS_PER_STEP = 2


def _attend_kernel(pos_ref, q_ref, g_ref, *refs):
    k_refs = refs[:SLOTS]
    v_refs = refs[SLOTS : 2 * SLOTS]
    att_ref, gq_ref, dk_ref, dv_ref, dk_acc, dv_acc = refs[2 * SLOTS :]
    scale = HD ** (-0.5)
    nt = (((1,), (1,)), ((), ()))
    tn = (((0,), (0,)), ((), ()))
    rows = q_ref.shape[0]
    empty = jnp.zeros((rows, dk_acc.shape[-1]), jnp.float32)
    for j in range(SLOTS):
        dk_acc[pos_ref[j]] = empty
        dv_acc[pos_ref[j]] = empty
    for hh in range(q_ref.shape[1] // HD):
        cols = slice(hh * HD, (hh + 1) * HD)
        q = q_ref[:, cols]
        g = g_ref[:, cols]
        k_all = jnp.concatenate([r[:, cols] for r in k_refs], axis=0)
        v_all = jnp.concatenate([r[:, cols] for r in v_refs], axis=0)
        s = lax.dot_general(q, k_all, nt, preferred_element_type=jnp.float32) * scale
        e = jnp.exp(s - jnp.max(s, axis=-1, keepdims=True))
        p = e / jnp.sum(e, axis=-1, keepdims=True)
        w = p.astype(jnp.bfloat16)
        att = jnp.dot(w, v_all, preferred_element_type=jnp.float32).astype(jnp.bfloat16)
        att_ref[:, cols] = att
        delta = jnp.sum(g.astype(jnp.float32) * att.astype(jnp.float32), axis=-1, keepdims=True)
        gp = lax.dot_general(g, v_all, nt, preferred_element_type=jnp.float32)
        gs = (p * (gp - delta)).astype(jnp.bfloat16)
        gq_ref[:, cols] = (jnp.dot(gs, k_all, preferred_element_type=jnp.float32) * scale).astype(
            jnp.bfloat16
        )
        gk = lax.dot_general(gs, q, tn, preferred_element_type=jnp.float32) * scale
        gv = lax.dot_general(w, g, tn, preferred_element_type=jnp.float32)
        for j in range(SLOTS):
            at = pos_ref[j]
            dk_acc[at, :, cols] = dk_acc[at, :, cols] + gk[j * rows : (j + 1) * rows]
            dv_acc[at, :, cols] = dv_acc[at, :, cols] + gv[j * rows : (j + 1) * rows]
    dk_ref[...] = jnp.zeros(dk_ref.shape, dk_ref.dtype)
    dv_ref[...] = jnp.zeros(dv_ref.shape, dv_ref.dtype)
    for j in range(SLOTS):
        at = pos_ref[j]
        dk_ref[at] = dk_acc[at].astype(dk_ref.dtype)
        dv_ref[at] = dv_acc[at].astype(dv_ref.dtype)


def attend_local(pos, query, grad_out, keys_local, values_local):
    rows, width = query.shape
    held = keys_local.shape[0]
    step = HEADS_PER_STEP * HD if (width // HD) % HEADS_PER_STEP == 0 else HD
    heads = width // HD
    head_spec = pl.BlockSpec((rows, step), lambda h, pos: (0, h))
    slot_specs = [
        pl.BlockSpec((None, rows, step), lambda h, pos, j=j: (pos[j], 0, h)) for j in range(SLOTS)
    ]
    part_spec = pl.BlockSpec((held, rows, step), lambda h, pos: (0, 0, h))
    flops = 12 * rows * SLOTS * rows * HD * heads
    moved = 2 * SLOTS * rows * width * 2 + 4 * rows * width * 2 + 2 * held * rows * width * 2
    call = pl.pallas_call(
        _attend_kernel,
        out_shape=(
            jax.ShapeDtypeStruct((rows, width), jnp.bfloat16),
            jax.ShapeDtypeStruct((rows, width), jnp.bfloat16),
            jax.ShapeDtypeStruct((held, rows, width), jnp.bfloat16),
            jax.ShapeDtypeStruct((held, rows, width), jnp.bfloat16),
        ),
        grid_spec=pltpu.PrefetchScalarGridSpec(
            num_scalar_prefetch=1,
            grid=(width // step,),
            in_specs=[head_spec, head_spec] + slot_specs + slot_specs,
            out_specs=(head_spec, head_spec, part_spec, part_spec),
            scratch_shapes=[pltpu.VMEM((held, rows, step), jnp.float32)] * 2,
        ),
        compiler_params=pltpu.CompilerParams(dimension_semantics=("arbitrary",)),
        cost_estimate=pl.CostEstimate(
            flops=flops, transcendentals=rows * SLOTS * rows * heads, bytes_accessed=moved
        ),
    )
    return call(
        pos, query, grad_out, *([keys_local] * SLOTS), *([values_local] * SLOTS)
    )


STREAMS = 2


def _stream(pos, query, grad_out, keys, values, after=None):
    n = lax.axis_size("seq")
    rows, width = query.shape
    line_len = n // 4
    if after is not None:
        keys, values, _ = lax.optimization_barrier((keys, values, after))
    keys_local, keys_line = gather_blocks(keys, n)
    values_local, values_line = gather_blocks(values, n)
    keys_local = keys_local.reshape(n, rows, width)
    values_local = values_local.reshape(n, rows, width)
    attended, grad_query, part_keys, part_values = attend_local(
        pos, query, grad_out, keys_local, values_local
    )
    scatter = jax.linear_transpose(
        lambda t: gather_blocks(t, n)[0], jax.ShapeDtypeStruct((rows, width), jnp.float32)
    )
    (grad_keys,) = scatter(part_keys.astype(jnp.float32).reshape(2, 2, line_len, rows, width))
    (grad_values,) = scatter(part_values.astype(jnp.float32).reshape(2, 2, line_len, rows, width))
    outs = (attended, grad_query, grad_keys.astype(jnp.bfloat16), grad_values.astype(jnp.bfloat16))
    return outs, (keys_line, values_line)


def shards_gather(query, keys, values, grad_out, global_blocks, random_blocks):
    n = lax.axis_size("seq")
    rows, width = query.shape
    line_len = n // 4
    idx = lax.axis_index("seq")
    listed = jnp.concatenate(
        [
            jnp.stack([idx, (idx - 1) % n, (idx + 1) % n]).astype(jnp.int32),
            global_blocks.astype(jnp.int32),
            random_blocks[idx].astype(jnp.int32),
        ]
    )
    listed = jnp.clip(listed, 0, n - 1)
    core = idx % 2
    ypos = (idx // 2) % 2
    pos = (((listed % 2) ^ core) * 2 + (((listed // 2) % 2) ^ ypos)) * line_len + listed // 4
    cut = width // STREAMS
    outs = []
    after = None
    for s in range(STREAMS):
        cols = slice(s * cut, (s + 1) * cut)
        with jax.named_scope(f"stream{s}"):
            out, after = _stream(
                pos, query[:, cols], grad_out[:, cols], keys[:, cols], values[:, cols], after
            )
            outs.append(out)
    return tuple(jnp.concatenate(parts, axis=1) for parts in zip(*outs))


def shards(query, keys, values, grad_out, global_blocks, random_blocks):
    n = lax.axis_size("seq")
    if query.shape[0] == BLK and n % 4 == 0 and n <= 32:
        return shards_gather(query, keys, values, grad_out, global_blocks, random_blocks)
    return shards_exchange(query, keys, values, grad_out, global_blocks, random_blocks)


def solution(mesh):
    placed = (
        P(("groups", "seq"), None),
        P(("groups", "seq"), None),
        P(("groups", "seq"), None),
        P(("groups", "seq"), None),
        P("groups"),
        P("groups", None),
    )
    return jax.shard_map(
        shards,
        mesh=mesh,
        in_specs=placed,
        out_specs=(
            P(("groups", "seq"), None),
            P(("groups", "seq"), None),
            P(("groups", "seq"), None),
            P(("groups", "seq"), None),
        ),
        check_vma=False,
    )
```

```python
import jax
import jax.numpy as jnp
from jax import lax
from jax.experimental import pallas as pl
from jax.experimental.pallas import tpu as pltpu
from jax.sharding import PartitionSpec as P

HD = 128
BLK = 128
G = 2


def attend_block(operands):
    query_blk, grad_blk, key_tiles, value_tiles = operands
    row_count, width = query_blk.shape
    keys_total = key_tiles.shape[0]
    head_size = HD
    head_count = width // head_size
    scaling = HD ** (-0.5)
    last_dims = (((1,), (1,)), ((), ()))
    first_dims = (((0,), (0,)), ((), ()))

    def one_head(head, carry):
        out_attended, out_gquery, out_gkeys, out_gvalues = carry
        start = head * head_size
        query_head = lax.dynamic_slice_in_dim(query_blk, start, head_size, 1)
        grad_head = lax.dynamic_slice_in_dim(grad_blk, start, head_size, 1)
        key_head = lax.dynamic_slice_in_dim(key_tiles, start, head_size, 1)
        value_head = lax.dynamic_slice_in_dim(value_tiles, start, head_size, 1)
        scores = (
            lax.dot_general(query_head, key_head, last_dims, preferred_element_type=jnp.float32)
            * scaling
        )
        probability = jax.nn.softmax(scores, axis=-1)
        weights = probability.astype(jnp.bfloat16)
        attended_head = jnp.dot(weights, value_head, preferred_element_type=jnp.float32).astype(
            jnp.bfloat16
        )
        deltas = jnp.sum(grad_head.astype(jnp.float32) * attended_head.astype(jnp.float32), axis=-1)
        grad_prob = lax.dot_general(
            grad_head, value_head, last_dims, preferred_element_type=jnp.float32
        )
        grad_score = (probability * (grad_prob - deltas[:, None])).astype(jnp.bfloat16)
        gquery_head = (
            jnp.dot(grad_score, key_head, preferred_element_type=jnp.float32) * scaling
        ).astype(jnp.bfloat16)
        gkeys_head = (
            lax.dot_general(grad_score, query_head, first_dims, preferred_element_type=jnp.float32)
            * scaling
        )
        gvalues_head = lax.dot_general(
            weights, grad_head, first_dims, preferred_element_type=jnp.float32
        )
        out_attended = lax.dynamic_update_slice_in_dim(out_attended, attended_head, start, 1)
        out_gquery = lax.dynamic_update_slice_in_dim(out_gquery, gquery_head, start, 1)
        out_gkeys = lax.dynamic_update_slice_in_dim(out_gkeys, gkeys_head, start, 1)
        out_gvalues = lax.dynamic_update_slice_in_dim(out_gvalues, gvalues_head, start, 1)
        return (out_attended, out_gquery, out_gkeys, out_gvalues)

    initial = (
        jnp.zeros((row_count, width), jnp.bfloat16),
        jnp.zeros((row_count, width), jnp.bfloat16),
        jnp.zeros((keys_total, width), jnp.float32),
        jnp.zeros((keys_total, width), jnp.float32),
    )
    return lax.fori_loop(0, head_count, one_head, initial)


def fetch_table(device_ids, block_count, total_blocks, global_blocks, random_blocks):
    owned_blocks = (
        device_ids[:, None] * block_count + jnp.arange(block_count, dtype=jnp.int32)[None, :]
    )
    pieces = []
    pieces.append(((owned_blocks - 1) % total_blocks)[:, :, None])
    pieces.append(((owned_blocks + 1) % total_blocks)[:, :, None])
    pieces.append(
        jnp.broadcast_to(
            global_blocks[None, None, :], owned_blocks.shape + (global_blocks.shape[0],)
        )
    )
    pieces.append(random_blocks[owned_blocks])
    return jnp.concatenate(pieces, axis=2).reshape(device_ids.shape[0], -1)


def shards_exchange(query, keys, values, grad_out, global_blocks, random_blocks):
    devices = lax.axis_size("seq")
    tok_rows, width = query.shape
    per_device = tok_rows // BLK
    total_blocks = per_device * devices
    row_share = BLK // devices
    key_blocks = keys.reshape(per_device, BLK, width)
    value_blocks = values.reshape(per_device, BLK, width)
    row_keys, row_values = (
        lax.all_to_all(
            keys.reshape(per_device, devices, row_share, width),
            "seq",
            split_axis=1,
            concat_axis=0,
            tiled=True,
        ),
        lax.all_to_all(
            values.reshape(per_device, devices, row_share, width),
            "seq",
            split_axis=1,
            concat_axis=0,
            tiled=True,
        ),
    )
    row_keys = row_keys.reshape(total_blocks, row_share, width)
    row_values = row_values.reshape(total_blocks, row_share, width)
    fetch_lists = fetch_table(
        jnp.arange(devices, dtype=jnp.int32), per_device, total_blocks, global_blocks, random_blocks
    )
    fetched = fetch_lists.shape[1]
    got_keys, got_values = (
        lax.all_to_all(row_keys[fetch_lists], "seq", split_axis=0, concat_axis=2, tiled=True),
        lax.all_to_all(row_values[fetch_lists], "seq", split_axis=0, concat_axis=2, tiled=True),
    )
    offset = 0
    window_keys = got_keys[:, 0:2]
    window_values = got_values[:, 0:2]
    offset = 2
    global_keys = got_keys[:, offset : offset + G]
    global_values = got_values[:, offset : offset + G]
    offset = offset + G
    random_keys = got_keys[:, offset:]
    random_values = got_values[:, offset:]
    tile_keys = jnp.concatenate(
        [key_blocks[:, None], window_keys, global_keys, random_keys], axis=1
    ).reshape(per_device, -1, width)
    tile_values = jnp.concatenate(
        [value_blocks[:, None], window_values, global_values, random_values], axis=1
    ).reshape(per_device, -1, width)
    attended, grad_query, tile_gkeys, tile_gvalues = lax.map(
        attend_block,
        (
            query.reshape(per_device, BLK, width),
            grad_out.reshape(per_device, BLK, width),
            tile_keys,
            tile_values,
        ),
    )
    tile_gkeys = tile_gkeys.reshape(per_device, -1, BLK, width)
    tile_gvalues = tile_gvalues.reshape(per_device, -1, BLK, width)
    window_gkeys = tile_gkeys[:, 1:3]
    window_gvalues = tile_gvalues[:, 1:3]
    global_gkeys = tile_gkeys[:, 3 : 3 + G]
    global_gvalues = tile_gvalues[:, 3 : 3 + G]
    back_keys = []
    back_values = []
    back_keys.append(window_gkeys)
    back_values.append(window_gvalues)
    back_keys.append(global_gkeys)
    back_values.append(global_gvalues)
    back_keys.append(tile_gkeys[:, 3 + G :])
    back_values.append(tile_gvalues[:, 3 + G :])
    back_keys = jnp.concatenate(back_keys, axis=1).reshape(1, fetched, devices, row_share, width)
    back_values = jnp.concatenate(back_values, axis=1).reshape(
        1, fetched, devices, row_share, width
    )
    recv_keys, recv_values = (
        lax.all_to_all(back_keys, "seq", split_axis=2, concat_axis=0, tiled=True),
        lax.all_to_all(back_values, "seq", split_axis=2, concat_axis=0, tiled=True),
    )
    flat_index = fetch_lists.reshape(-1)
    table_keys = (
        jnp.zeros((total_blocks, row_share, width), jnp.float32)
        .at[flat_index]
        .add(recv_keys.reshape(devices * fetched, row_share, width))
    )
    table_values = (
        jnp.zeros((total_blocks, row_share, width), jnp.float32)
        .at[flat_index]
        .add(recv_values.reshape(devices * fetched, row_share, width))
    )
    home_keys, home_values = (
        lax.all_to_all(
            table_keys.reshape(total_blocks, 1, row_share, width),
            "seq",
            split_axis=0,
            concat_axis=1,
            tiled=True,
        ),
        lax.all_to_all(
            table_values.reshape(total_blocks, 1, row_share, width),
            "seq",
            split_axis=0,
            concat_axis=1,
            tiled=True,
        ),
    )
    grad_key_blocks = tile_gkeys[:, 0] + home_keys.reshape(per_device, BLK, width)
    grad_value_blocks = tile_gvalues[:, 0] + home_values.reshape(per_device, BLK, width)
    return (
        attended.reshape(tok_rows, width),
        grad_query.reshape(tok_rows, width),
        grad_key_blocks.astype(jnp.bfloat16).reshape(tok_rows, width),
        grad_value_blocks.astype(jnp.bfloat16).reshape(tok_rows, width),
    )

SLOTS = 3 + G + 3


def _send(v, pairs):
    return lax.ppermute(v.astype(jnp.bfloat16), "seq", pairs).astype(v.dtype)


def gather_blocks(x, n):
    line_len = n // 4
    z = lax.axis_index("seq") // 4
    y_swap = [(i, i ^ 2) for i in range(n)]
    other_own = _send(x, y_swap)
    ups, downs = [], []
    up, down = x, x
    for k in range(1, line_len):
        up = _send(
            up, [(4 * z0 + r, 4 * (z0 + 1) + r) for z0 in range(k - 1, line_len - 1) for r in range(4)]
        )
        down = _send(
            down, [(4 * z0 + r, 4 * (z0 - 1) + r) for z0 in range(1, line_len - k + 1) for r in range(4)]
        )
        ups.append(up)
        downs.append(down)
    rest = lax.dynamic_slice_in_dim(
        jnp.stack(ups[::-1] + downs), line_len - 1 - z, line_len - 1, axis=0
    )
    mine = jnp.concatenate([x[None], rest])
    other = jnp.concatenate([other_own[None], _send(rest, y_swap)])
    pair = jnp.stack([mine, other])
    sibling = _send(pair, [(i, i ^ 1) for i in range(n)])
    return jnp.stack([pair, sibling]), mine


HEADS_PER_STEP = 2


def _attend_kernel(pos_ref, q_ref, g_ref, *refs):
    k_refs = refs[:SLOTS]
    v_refs = refs[SLOTS : 2 * SLOTS]
    att_ref, gq_ref, dk_ref, dv_ref, dk_acc, dv_acc = refs[2 * SLOTS :]
    scale = HD ** (-0.5)
    nt = (((1,), (1,)), ((), ()))
    tn = (((0,), (0,)), ((), ()))
    rows = q_ref.shape[0]
    empty = jnp.zeros((rows, dk_acc.shape[-1]), jnp.float32)
    for j in range(SLOTS):
        dk_acc[pos_ref[j]] = empty
        dv_acc[pos_ref[j]] = empty
    for hh in range(q_ref.shape[1] // HD):
        cols = slice(hh * HD, (hh + 1) * HD)
        q = q_ref[:, cols]
        g = g_ref[:, cols]
        k_all = jnp.concatenate([r[:, cols] for r in k_refs], axis=0)
        v_all = jnp.concatenate([r[:, cols] for r in v_refs], axis=0)
        s = lax.dot_general(q, k_all, nt, preferred_element_type=jnp.float32) * scale
        e = jnp.exp(s - jnp.max(s, axis=-1, keepdims=True))
        p = e / jnp.sum(e, axis=-1, keepdims=True)
        w = p.astype(jnp.bfloat16)
        att = jnp.dot(w, v_all, preferred_element_type=jnp.float32).astype(jnp.bfloat16)
        att_ref[:, cols] = att
        delta = jnp.sum(g.astype(jnp.float32) * att.astype(jnp.float32), axis=-1, keepdims=True)
        gp = lax.dot_general(g, v_all, nt, preferred_element_type=jnp.float32)
        gs = (p * (gp - delta)).astype(jnp.bfloat16)
        gq_ref[:, cols] = (jnp.dot(gs, k_all, preferred_element_type=jnp.float32) * scale).astype(
            jnp.bfloat16
        )
        gk = lax.dot_general(gs, q, tn, preferred_element_type=jnp.float32) * scale
        gv = lax.dot_general(w, g, tn, preferred_element_type=jnp.float32)
        for j in range(SLOTS):
            at = pos_ref[j]
            dk_acc[at, :, cols] = dk_acc[at, :, cols] + gk[j * rows : (j + 1) * rows]
            dv_acc[at, :, cols] = dv_acc[at, :, cols] + gv[j * rows : (j + 1) * rows]
    dk_ref[...] = jnp.zeros(dk_ref.shape, dk_ref.dtype)
    dv_ref[...] = jnp.zeros(dv_ref.shape, dv_ref.dtype)
    for j in range(SLOTS):
        at = pos_ref[j]
        dk_ref[at] = dk_acc[at].astype(dk_ref.dtype)
        dv_ref[at] = dv_acc[at].astype(dv_ref.dtype)


def attend_local(pos, query, grad_out, keys_local, values_local):
    rows, width = query.shape
    held = keys_local.shape[0]
    step = HEADS_PER_STEP * HD if (width // HD) % HEADS_PER_STEP == 0 else HD
    heads = width // HD
    head_spec = pl.BlockSpec((rows, step), lambda h, pos: (0, h))
    slot_specs = [
        pl.BlockSpec((None, rows, step), lambda h, pos, j=j: (pos[j], 0, h)) for j in range(SLOTS)
    ]
    part_spec = pl.BlockSpec((held, rows, step), lambda h, pos: (0, 0, h))
    flops = 12 * rows * SLOTS * rows * HD * heads
    moved = 2 * SLOTS * rows * width * 2 + 4 * rows * width * 2 + 2 * held * rows * width * 2
    call = pl.pallas_call(
        _attend_kernel,
        out_shape=(
            jax.ShapeDtypeStruct((rows, width), jnp.bfloat16),
            jax.ShapeDtypeStruct((rows, width), jnp.bfloat16),
            jax.ShapeDtypeStruct((held, rows, width), jnp.bfloat16),
            jax.ShapeDtypeStruct((held, rows, width), jnp.bfloat16),
        ),
        grid_spec=pltpu.PrefetchScalarGridSpec(
            num_scalar_prefetch=1,
            grid=(width // step,),
            in_specs=[head_spec, head_spec] + slot_specs + slot_specs,
            out_specs=(head_spec, head_spec, part_spec, part_spec),
            scratch_shapes=[pltpu.VMEM((held, rows, step), jnp.float32)] * 2,
        ),
        compiler_params=pltpu.CompilerParams(dimension_semantics=("arbitrary",)),
        cost_estimate=pl.CostEstimate(
            flops=flops, transcendentals=rows * SLOTS * rows * heads, bytes_accessed=moved
        ),
    )
    return call(
        pos, query, grad_out, *([keys_local] * SLOTS), *([values_local] * SLOTS)
    )


STREAMS = 2


def _stream(pos, query, grad_out, keys, values, after=None):
    n = lax.axis_size("seq")
    rows, width = query.shape
    line_len = n // 4
    if after is not None:
        keys, values, _ = lax.optimization_barrier((keys, values, after))
    keys_local, keys_line = gather_blocks(keys, n)
    values_local, values_line = gather_blocks(values, n)
    keys_local = keys_local.reshape(n, rows, width)
    values_local = values_local.reshape(n, rows, width)
    attended, grad_query, part_keys, part_values = attend_local(
        pos, query, grad_out, keys_local, values_local
    )
    scatter = jax.linear_transpose(
        lambda t: gather_blocks(t, n)[0], jax.ShapeDtypeStruct((rows, width), jnp.float32)
    )
    (grad_keys,) = scatter(part_keys.astype(jnp.float32).reshape(2, 2, line_len, rows, width))
    (grad_values,) = scatter(part_values.astype(jnp.float32).reshape(2, 2, line_len, rows, width))
    outs = (attended, grad_query, grad_keys.astype(jnp.bfloat16), grad_values.astype(jnp.bfloat16))
    return outs, (keys_line, values_line)


def shards_gather(query, keys, values, grad_out, global_blocks, random_blocks):
    n = lax.axis_size("seq")
    rows, width = query.shape
    line_len = n // 4
    idx = lax.axis_index("seq")
    listed = jnp.concatenate(
        [
            jnp.stack([idx, (idx - 1) % n, (idx + 1) % n]).astype(jnp.int32),
            global_blocks.astype(jnp.int32),
            random_blocks[idx].astype(jnp.int32),
        ]
    )
    listed = jnp.clip(listed, 0, n - 1)
    core = idx % 2
    ypos = (idx // 2) % 2
    zpos = idx // 4
    plane = listed // 4
    in_line = jnp.where(plane == zpos, 0, jnp.where(plane < zpos, plane + 1, plane))
    pos = (((listed % 2) ^ core) * 2 + (((listed // 2) % 2) ^ ypos)) * line_len + in_line
    cut = width // STREAMS
    outs = []
    after = None
    for s in range(STREAMS):
        cols = slice(s * cut, (s + 1) * cut)
        with jax.named_scope(f"stream{s}"):
            out, after = _stream(
                pos, query[:, cols], grad_out[:, cols], keys[:, cols], values[:, cols], after
            )
            outs.append(out)
    return tuple(jnp.concatenate(parts, axis=1) for parts in zip(*outs))


def shards(query, keys, values, grad_out, global_blocks, random_blocks):
    n = lax.axis_size("seq")
    if query.shape[0] == BLK and n % 4 == 0 and n <= 32:
        return shards_gather(query, keys, values, grad_out, global_blocks, random_blocks)
    return shards_exchange(query, keys, values, grad_out, global_blocks, random_blocks)


def solution(mesh):
    placed = (
        P(("groups", "seq"), None),
        P(("groups", "seq"), None),
        P(("groups", "seq"), None),
        P(("groups", "seq"), None),
        P("groups"),
        P("groups", None),
    )
    return jax.shard_map(
        shards,
        mesh=mesh,
        in_specs=placed,
        out_specs=(
            P(("groups", "seq"), None),
            P(("groups", "seq"), None),
            P(("groups", "seq"), None),
            P(("groups", "seq"), None),
        ),
        check_vma=False,
    )
```

```python
import jax
import jax.numpy as jnp
from jax import lax
from jax.experimental import pallas as pl
from jax.experimental.pallas import tpu as pltpu
from jax.sharding import PartitionSpec as P

HD = 128
BLK = 128
G = 2


def attend_block(operands):
    query_blk, grad_blk, key_tiles, value_tiles = operands
    row_count, width = query_blk.shape
    keys_total = key_tiles.shape[0]
    head_size = HD
    head_count = width // head_size
    scaling = HD ** (-0.5)
    last_dims = (((1,), (1,)), ((), ()))
    first_dims = (((0,), (0,)), ((), ()))

    def one_head(head, carry):
        out_attended, out_gquery, out_gkeys, out_gvalues = carry
        start = head * head_size
        query_head = lax.dynamic_slice_in_dim(query_blk, start, head_size, 1)
        grad_head = lax.dynamic_slice_in_dim(grad_blk, start, head_size, 1)
        key_head = lax.dynamic_slice_in_dim(key_tiles, start, head_size, 1)
        value_head = lax.dynamic_slice_in_dim(value_tiles, start, head_size, 1)
        scores = (
            lax.dot_general(query_head, key_head, last_dims, preferred_element_type=jnp.float32)
            * scaling
        )
        probability = jax.nn.softmax(scores, axis=-1)
        weights = probability.astype(jnp.bfloat16)
        attended_head = jnp.dot(weights, value_head, preferred_element_type=jnp.float32).astype(
            jnp.bfloat16
        )
        deltas = jnp.sum(grad_head.astype(jnp.float32) * attended_head.astype(jnp.float32), axis=-1)
        grad_prob = lax.dot_general(
            grad_head, value_head, last_dims, preferred_element_type=jnp.float32
        )
        grad_score = (probability * (grad_prob - deltas[:, None])).astype(jnp.bfloat16)
        gquery_head = (
            jnp.dot(grad_score, key_head, preferred_element_type=jnp.float32) * scaling
        ).astype(jnp.bfloat16)
        gkeys_head = (
            lax.dot_general(grad_score, query_head, first_dims, preferred_element_type=jnp.float32)
            * scaling
        )
        gvalues_head = lax.dot_general(
            weights, grad_head, first_dims, preferred_element_type=jnp.float32
        )
        out_attended = lax.dynamic_update_slice_in_dim(out_attended, attended_head, start, 1)
        out_gquery = lax.dynamic_update_slice_in_dim(out_gquery, gquery_head, start, 1)
        out_gkeys = lax.dynamic_update_slice_in_dim(out_gkeys, gkeys_head, start, 1)
        out_gvalues = lax.dynamic_update_slice_in_dim(out_gvalues, gvalues_head, start, 1)
        return (out_attended, out_gquery, out_gkeys, out_gvalues)

    initial = (
        jnp.zeros((row_count, width), jnp.bfloat16),
        jnp.zeros((row_count, width), jnp.bfloat16),
        jnp.zeros((keys_total, width), jnp.float32),
        jnp.zeros((keys_total, width), jnp.float32),
    )
    return lax.fori_loop(0, head_count, one_head, initial)


def fetch_table(device_ids, block_count, total_blocks, global_blocks, random_blocks):
    owned_blocks = (
        device_ids[:, None] * block_count + jnp.arange(block_count, dtype=jnp.int32)[None, :]
    )
    pieces = []
    pieces.append(((owned_blocks - 1) % total_blocks)[:, :, None])
    pieces.append(((owned_blocks + 1) % total_blocks)[:, :, None])
    pieces.append(
        jnp.broadcast_to(
            global_blocks[None, None, :], owned_blocks.shape + (global_blocks.shape[0],)
        )
    )
    pieces.append(random_blocks[owned_blocks])
    return jnp.concatenate(pieces, axis=2).reshape(device_ids.shape[0], -1)


def shards_exchange(query, keys, values, grad_out, global_blocks, random_blocks):
    devices = lax.axis_size("seq")
    tok_rows, width = query.shape
    per_device = tok_rows // BLK
    total_blocks = per_device * devices
    row_share = BLK // devices
    key_blocks = keys.reshape(per_device, BLK, width)
    value_blocks = values.reshape(per_device, BLK, width)
    row_keys, row_values = (
        lax.all_to_all(
            keys.reshape(per_device, devices, row_share, width),
            "seq",
            split_axis=1,
            concat_axis=0,
            tiled=True,
        ),
        lax.all_to_all(
            values.reshape(per_device, devices, row_share, width),
            "seq",
            split_axis=1,
            concat_axis=0,
            tiled=True,
        ),
    )
    row_keys = row_keys.reshape(total_blocks, row_share, width)
    row_values = row_values.reshape(total_blocks, row_share, width)
    fetch_lists = fetch_table(
        jnp.arange(devices, dtype=jnp.int32), per_device, total_blocks, global_blocks, random_blocks
    )
    fetched = fetch_lists.shape[1]
    got_keys, got_values = (
        lax.all_to_all(row_keys[fetch_lists], "seq", split_axis=0, concat_axis=2, tiled=True),
        lax.all_to_all(row_values[fetch_lists], "seq", split_axis=0, concat_axis=2, tiled=True),
    )
    offset = 0
    window_keys = got_keys[:, 0:2]
    window_values = got_values[:, 0:2]
    offset = 2
    global_keys = got_keys[:, offset : offset + G]
    global_values = got_values[:, offset : offset + G]
    offset = offset + G
    random_keys = got_keys[:, offset:]
    random_values = got_values[:, offset:]
    tile_keys = jnp.concatenate(
        [key_blocks[:, None], window_keys, global_keys, random_keys], axis=1
    ).reshape(per_device, -1, width)
    tile_values = jnp.concatenate(
        [value_blocks[:, None], window_values, global_values, random_values], axis=1
    ).reshape(per_device, -1, width)
    attended, grad_query, tile_gkeys, tile_gvalues = lax.map(
        attend_block,
        (
            query.reshape(per_device, BLK, width),
            grad_out.reshape(per_device, BLK, width),
            tile_keys,
            tile_values,
        ),
    )
    tile_gkeys = tile_gkeys.reshape(per_device, -1, BLK, width)
    tile_gvalues = tile_gvalues.reshape(per_device, -1, BLK, width)
    window_gkeys = tile_gkeys[:, 1:3]
    window_gvalues = tile_gvalues[:, 1:3]
    global_gkeys = tile_gkeys[:, 3 : 3 + G]
    global_gvalues = tile_gvalues[:, 3 : 3 + G]
    back_keys = []
    back_values = []
    back_keys.append(window_gkeys)
    back_values.append(window_gvalues)
    back_keys.append(global_gkeys)
    back_values.append(global_gvalues)
    back_keys.append(tile_gkeys[:, 3 + G :])
    back_values.append(tile_gvalues[:, 3 + G :])
    back_keys = jnp.concatenate(back_keys, axis=1).reshape(1, fetched, devices, row_share, width)
    back_values = jnp.concatenate(back_values, axis=1).reshape(
        1, fetched, devices, row_share, width
    )
    recv_keys, recv_values = (
        lax.all_to_all(back_keys, "seq", split_axis=2, concat_axis=0, tiled=True),
        lax.all_to_all(back_values, "seq", split_axis=2, concat_axis=0, tiled=True),
    )
    flat_index = fetch_lists.reshape(-1)
    table_keys = (
        jnp.zeros((total_blocks, row_share, width), jnp.float32)
        .at[flat_index]
        .add(recv_keys.reshape(devices * fetched, row_share, width))
    )
    table_values = (
        jnp.zeros((total_blocks, row_share, width), jnp.float32)
        .at[flat_index]
        .add(recv_values.reshape(devices * fetched, row_share, width))
    )
    home_keys, home_values = (
        lax.all_to_all(
            table_keys.reshape(total_blocks, 1, row_share, width),
            "seq",
            split_axis=0,
            concat_axis=1,
            tiled=True,
        ),
        lax.all_to_all(
            table_values.reshape(total_blocks, 1, row_share, width),
            "seq",
            split_axis=0,
            concat_axis=1,
            tiled=True,
        ),
    )
    grad_key_blocks = tile_gkeys[:, 0] + home_keys.reshape(per_device, BLK, width)
    grad_value_blocks = tile_gvalues[:, 0] + home_values.reshape(per_device, BLK, width)
    return (
        attended.reshape(tok_rows, width),
        grad_query.reshape(tok_rows, width),
        grad_key_blocks.astype(jnp.bfloat16).reshape(tok_rows, width),
        grad_value_blocks.astype(jnp.bfloat16).reshape(tok_rows, width),
    )

SLOTS = 3 + G + 3


def _send(v, pairs):
    return lax.ppermute(v.astype(jnp.bfloat16), "seq", pairs).astype(v.dtype)


def gather_blocks(x, n):
    line_len = n // 4
    z = lax.axis_index("seq") // 4
    ups, downs = [], []
    up, down = x, x
    for k in range(1, line_len):
        up = _send(
            up, [(4 * z0 + r, 4 * (z0 + 1) + r) for z0 in range(k - 1, line_len - 1) for r in range(4)]
        )
        down = _send(
            down, [(4 * z0 + r, 4 * (z0 - 1) + r) for z0 in range(1, line_len - k + 1) for r in range(4)]
        )
        ups.append(up)
        downs.append(down)
    rel = jnp.stack(ups[::-1] + [x] + downs)
    line = lax.dynamic_slice_in_dim(rel, line_len - 1 - z, line_len, axis=0)
    other = _send(line, [(i, i ^ 2) for i in range(n)])
    pair = jnp.stack([line, other])
    sibling = _send(pair, [(i, i ^ 1) for i in range(n)])
    return jnp.stack([pair, sibling]), line


HEADS_PER_STEP = 4


def _attend_kernel(pos_ref, q_ref, g_ref, *refs):
    k_refs = refs[:SLOTS]
    v_refs = refs[SLOTS : 2 * SLOTS]
    att_ref, gq_ref, dk_ref, dv_ref, dk_acc, dv_acc = refs[2 * SLOTS :]
    scale = HD ** (-0.5)
    nt = (((1,), (1,)), ((), ()))
    tn = (((0,), (0,)), ((), ()))
    rows = q_ref.shape[0]
    empty = jnp.zeros((rows, dk_acc.shape[-1]), jnp.float32)
    for j in range(SLOTS):
        dk_acc[pos_ref[j]] = empty
        dv_acc[pos_ref[j]] = empty
    for hh in range(q_ref.shape[1] // HD):
        cols = slice(hh * HD, (hh + 1) * HD)
        q = q_ref[:, cols]
        g = g_ref[:, cols]
        k_all = jnp.concatenate([r[:, cols] for r in k_refs], axis=0)
        v_all = jnp.concatenate([r[:, cols] for r in v_refs], axis=0)
        s = lax.dot_general(q, k_all, nt, preferred_element_type=jnp.float32) * scale
        e = jnp.exp(s - jnp.max(s, axis=-1, keepdims=True))
        p = e / jnp.sum(e, axis=-1, keepdims=True)
        w = p.astype(jnp.bfloat16)
        att = jnp.dot(w, v_all, preferred_element_type=jnp.float32).astype(jnp.bfloat16)
        att_ref[:, cols] = att
        delta = jnp.sum(g.astype(jnp.float32) * att.astype(jnp.float32), axis=-1, keepdims=True)
        gp = lax.dot_general(g, v_all, nt, preferred_element_type=jnp.float32)
        gs = (p * (gp - delta)).astype(jnp.bfloat16)
        gq_ref[:, cols] = (jnp.dot(gs, k_all, preferred_element_type=jnp.float32) * scale).astype(
            jnp.bfloat16
        )
        gk = lax.dot_general(gs, q, tn, preferred_element_type=jnp.float32) * scale
        gv = lax.dot_general(w, g, tn, preferred_element_type=jnp.float32)
        for j in range(SLOTS):
            at = pos_ref[j]
            dk_acc[at, :, cols] = dk_acc[at, :, cols] + gk[j * rows : (j + 1) * rows]
            dv_acc[at, :, cols] = dv_acc[at, :, cols] + gv[j * rows : (j + 1) * rows]
    dk_ref[...] = jnp.zeros(dk_ref.shape, dk_ref.dtype)
    dv_ref[...] = jnp.zeros(dv_ref.shape, dv_ref.dtype)
    for j in range(SLOTS):
        at = pos_ref[j]
        dk_ref[at] = dk_acc[at].astype(dk_ref.dtype)
        dv_ref[at] = dv_acc[at].astype(dv_ref.dtype)


def attend_local(pos, query, grad_out, keys_local, values_local):
    rows, width = query.shape
    held = keys_local.shape[0]
    step = HEADS_PER_STEP * HD if (width // HD) % HEADS_PER_STEP == 0 else HD
    heads = width // HD
    head_spec = pl.BlockSpec((rows, step), lambda h, pos: (0, h))
    slot_specs = [
        pl.BlockSpec((None, rows, step), lambda h, pos, j=j: (pos[j], 0, h)) for j in range(SLOTS)
    ]
    part_spec = pl.BlockSpec((held, rows, step), lambda h, pos: (0, 0, h))
    flops = 12 * rows * SLOTS * rows * HD * heads
    moved = 2 * SLOTS * rows * width * 2 + 4 * rows * width * 2 + 2 * held * rows * width * 2
    call = pl.pallas_call(
        _attend_kernel,
        out_shape=(
            jax.ShapeDtypeStruct((rows, width), jnp.bfloat16),
            jax.ShapeDtypeStruct((rows, width), jnp.bfloat16),
            jax.ShapeDtypeStruct((held, rows, width), jnp.bfloat16),
            jax.ShapeDtypeStruct((held, rows, width), jnp.bfloat16),
        ),
        grid_spec=pltpu.PrefetchScalarGridSpec(
            num_scalar_prefetch=1,
            grid=(width // step,),
            in_specs=[head_spec, head_spec] + slot_specs + slot_specs,
            out_specs=(head_spec, head_spec, part_spec, part_spec),
            scratch_shapes=[pltpu.VMEM((held, rows, step), jnp.float32)] * 2,
        ),
        compiler_params=pltpu.CompilerParams(dimension_semantics=("arbitrary",)),
        cost_estimate=pl.CostEstimate(
            flops=flops, transcendentals=rows * SLOTS * rows * heads, bytes_accessed=moved
        ),
    )
    return call(
        pos, query, grad_out, *([keys_local] * SLOTS), *([values_local] * SLOTS)
    )


STREAMS = 2


def _stream(pos, query, grad_out, keys, values, after=None):
    n = lax.axis_size("seq")
    rows, width = query.shape
    line_len = n // 4
    if after is not None:
        keys, values, _ = lax.optimization_barrier((keys, values, after))
    keys_local, keys_line = gather_blocks(keys, n)
    values_local, values_line = gather_blocks(values, n)
    keys_local = keys_local.reshape(n, rows, width)
    values_local = values_local.reshape(n, rows, width)
    attended, grad_query, part_keys, part_values = attend_local(
        pos, query, grad_out, keys_local, values_local
    )
    scatter = jax.linear_transpose(
        lambda t: gather_blocks(t, n)[0], jax.ShapeDtypeStruct((rows, width), jnp.float32)
    )
    (grad_keys,) = scatter(part_keys.astype(jnp.float32).reshape(2, 2, line_len, rows, width))
    (grad_values,) = scatter(part_values.astype(jnp.float32).reshape(2, 2, line_len, rows, width))
    outs = (attended, grad_query, grad_keys.astype(jnp.bfloat16), grad_values.astype(jnp.bfloat16))
    return outs, (keys_line, values_line)


def shards_gather(query, keys, values, grad_out, global_blocks, random_blocks):
    n = lax.axis_size("seq")
    rows, width = query.shape
    line_len = n // 4
    idx = lax.axis_index("seq")
    listed = jnp.concatenate(
        [
            jnp.stack([idx, (idx - 1) % n, (idx + 1) % n]).astype(jnp.int32),
            global_blocks.astype(jnp.int32),
            random_blocks[idx].astype(jnp.int32),
        ]
    )
    listed = jnp.clip(listed, 0, n - 1)
    core = idx % 2
    ypos = (idx // 2) % 2
    pos = (((listed % 2) ^ core) * 2 + (((listed // 2) % 2) ^ ypos)) * line_len + listed // 4
    cut = width // STREAMS
    outs = []
    after = None
    for s in range(STREAMS):
        cols = slice(s * cut, (s + 1) * cut)
        with jax.named_scope(f"stream{s}"):
            out, after = _stream(
                pos, query[:, cols], grad_out[:, cols], keys[:, cols], values[:, cols], after
            )
            outs.append(out)
    return tuple(jnp.concatenate(parts, axis=1) for parts in zip(*outs))


def shards(query, keys, values, grad_out, global_blocks, random_blocks):
    n = lax.axis_size("seq")
    if query.shape[0] == BLK and n % 4 == 0 and n <= 32:
        return shards_gather(query, keys, values, grad_out, global_blocks, random_blocks)
    return shards_exchange(query, keys, values, grad_out, global_blocks, random_blocks)


def solution(mesh):
    placed = (
        P(("groups", "seq"), None),
        P(("groups", "seq"), None),
        P(("groups", "seq"), None),
        P(("groups", "seq"), None),
        P("groups"),
        P("groups", None),
    )
    return jax.shard_map(
        shards,
        mesh=mesh,
        in_specs=placed,
        out_specs=(
            P(("groups", "seq"), None),
            P(("groups", "seq"), None),
            P(("groups", "seq"), None),
            P(("groups", "seq"), None),
        ),
        check_vma=False,
    )
```

```python
import jax
import jax.numpy as jnp
from jax import lax
from jax.experimental import pallas as pl
from jax.experimental.pallas import tpu as pltpu
from jax.sharding import PartitionSpec as P

HD = 128
BLK = 128
G = 2


def attend_block(operands):
    query_blk, grad_blk, key_tiles, value_tiles = operands
    row_count, width = query_blk.shape
    keys_total = key_tiles.shape[0]
    head_size = HD
    head_count = width // head_size
    scaling = HD ** (-0.5)
    last_dims = (((1,), (1,)), ((), ()))
    first_dims = (((0,), (0,)), ((), ()))

    def one_head(head, carry):
        out_attended, out_gquery, out_gkeys, out_gvalues = carry
        start = head * head_size
        query_head = lax.dynamic_slice_in_dim(query_blk, start, head_size, 1)
        grad_head = lax.dynamic_slice_in_dim(grad_blk, start, head_size, 1)
        key_head = lax.dynamic_slice_in_dim(key_tiles, start, head_size, 1)
        value_head = lax.dynamic_slice_in_dim(value_tiles, start, head_size, 1)
        scores = (
            lax.dot_general(query_head, key_head, last_dims, preferred_element_type=jnp.float32)
            * scaling
        )
        probability = jax.nn.softmax(scores, axis=-1)
        weights = probability.astype(jnp.bfloat16)
        attended_head = jnp.dot(weights, value_head, preferred_element_type=jnp.float32).astype(
            jnp.bfloat16
        )
        deltas = jnp.sum(grad_head.astype(jnp.float32) * attended_head.astype(jnp.float32), axis=-1)
        grad_prob = lax.dot_general(
            grad_head, value_head, last_dims, preferred_element_type=jnp.float32
        )
        grad_score = (probability * (grad_prob - deltas[:, None])).astype(jnp.bfloat16)
        gquery_head = (
            jnp.dot(grad_score, key_head, preferred_element_type=jnp.float32) * scaling
        ).astype(jnp.bfloat16)
        gkeys_head = (
            lax.dot_general(grad_score, query_head, first_dims, preferred_element_type=jnp.float32)
            * scaling
        )
        gvalues_head = lax.dot_general(
            weights, grad_head, first_dims, preferred_element_type=jnp.float32
        )
        out_attended = lax.dynamic_update_slice_in_dim(out_attended, attended_head, start, 1)
        out_gquery = lax.dynamic_update_slice_in_dim(out_gquery, gquery_head, start, 1)
        out_gkeys = lax.dynamic_update_slice_in_dim(out_gkeys, gkeys_head, start, 1)
        out_gvalues = lax.dynamic_update_slice_in_dim(out_gvalues, gvalues_head, start, 1)
        return (out_attended, out_gquery, out_gkeys, out_gvalues)

    initial = (
        jnp.zeros((row_count, width), jnp.bfloat16),
        jnp.zeros((row_count, width), jnp.bfloat16),
        jnp.zeros((keys_total, width), jnp.float32),
        jnp.zeros((keys_total, width), jnp.float32),
    )
    return lax.fori_loop(0, head_count, one_head, initial)


def fetch_table(device_ids, block_count, total_blocks, global_blocks, random_blocks):
    owned_blocks = (
        device_ids[:, None] * block_count + jnp.arange(block_count, dtype=jnp.int32)[None, :]
    )
    pieces = []
    pieces.append(((owned_blocks - 1) % total_blocks)[:, :, None])
    pieces.append(((owned_blocks + 1) % total_blocks)[:, :, None])
    pieces.append(
        jnp.broadcast_to(
            global_blocks[None, None, :], owned_blocks.shape + (global_blocks.shape[0],)
        )
    )
    pieces.append(random_blocks[owned_blocks])
    return jnp.concatenate(pieces, axis=2).reshape(device_ids.shape[0], -1)


def shards_exchange(query, keys, values, grad_out, global_blocks, random_blocks):
    devices = lax.axis_size("seq")
    tok_rows, width = query.shape
    per_device = tok_rows // BLK
    total_blocks = per_device * devices
    row_share = BLK // devices
    key_blocks = keys.reshape(per_device, BLK, width)
    value_blocks = values.reshape(per_device, BLK, width)
    row_keys, row_values = (
        lax.all_to_all(
            keys.reshape(per_device, devices, row_share, width),
            "seq",
            split_axis=1,
            concat_axis=0,
            tiled=True,
        ),
        lax.all_to_all(
            values.reshape(per_device, devices, row_share, width),
            "seq",
            split_axis=1,
            concat_axis=0,
            tiled=True,
        ),
    )
    row_keys = row_keys.reshape(total_blocks, row_share, width)
    row_values = row_values.reshape(total_blocks, row_share, width)
    fetch_lists = fetch_table(
        jnp.arange(devices, dtype=jnp.int32), per_device, total_blocks, global_blocks, random_blocks
    )
    fetched = fetch_lists.shape[1]
    got_keys, got_values = (
        lax.all_to_all(row_keys[fetch_lists], "seq", split_axis=0, concat_axis=2, tiled=True),
        lax.all_to_all(row_values[fetch_lists], "seq", split_axis=0, concat_axis=2, tiled=True),
    )
    offset = 0
    window_keys = got_keys[:, 0:2]
    window_values = got_values[:, 0:2]
    offset = 2
    global_keys = got_keys[:, offset : offset + G]
    global_values = got_values[:, offset : offset + G]
    offset = offset + G
    random_keys = got_keys[:, offset:]
    random_values = got_values[:, offset:]
    tile_keys = jnp.concatenate(
        [key_blocks[:, None], window_keys, global_keys, random_keys], axis=1
    ).reshape(per_device, -1, width)
    tile_values = jnp.concatenate(
        [value_blocks[:, None], window_values, global_values, random_values], axis=1
    ).reshape(per_device, -1, width)
    attended, grad_query, tile_gkeys, tile_gvalues = lax.map(
        attend_block,
        (
            query.reshape(per_device, BLK, width),
            grad_out.reshape(per_device, BLK, width),
            tile_keys,
            tile_values,
        ),
    )
    tile_gkeys = tile_gkeys.reshape(per_device, -1, BLK, width)
    tile_gvalues = tile_gvalues.reshape(per_device, -1, BLK, width)
    window_gkeys = tile_gkeys[:, 1:3]
    window_gvalues = tile_gvalues[:, 1:3]
    global_gkeys = tile_gkeys[:, 3 : 3 + G]
    global_gvalues = tile_gvalues[:, 3 : 3 + G]
    back_keys = []
    back_values = []
    back_keys.append(window_gkeys)
    back_values.append(window_gvalues)
    back_keys.append(global_gkeys)
    back_values.append(global_gvalues)
    back_keys.append(tile_gkeys[:, 3 + G :])
    back_values.append(tile_gvalues[:, 3 + G :])
    back_keys = jnp.concatenate(back_keys, axis=1).reshape(1, fetched, devices, row_share, width)
    back_values = jnp.concatenate(back_values, axis=1).reshape(
        1, fetched, devices, row_share, width
    )
    recv_keys, recv_values = (
        lax.all_to_all(back_keys, "seq", split_axis=2, concat_axis=0, tiled=True),
        lax.all_to_all(back_values, "seq", split_axis=2, concat_axis=0, tiled=True),
    )
    flat_index = fetch_lists.reshape(-1)
    table_keys = (
        jnp.zeros((total_blocks, row_share, width), jnp.float32)
        .at[flat_index]
        .add(recv_keys.reshape(devices * fetched, row_share, width))
    )
    table_values = (
        jnp.zeros((total_blocks, row_share, width), jnp.float32)
        .at[flat_index]
        .add(recv_values.reshape(devices * fetched, row_share, width))
    )
    home_keys, home_values = (
        lax.all_to_all(
            table_keys.reshape(total_blocks, 1, row_share, width),
            "seq",
            split_axis=0,
            concat_axis=1,
            tiled=True,
        ),
        lax.all_to_all(
            table_values.reshape(total_blocks, 1, row_share, width),
            "seq",
            split_axis=0,
            concat_axis=1,
            tiled=True,
        ),
    )
    grad_key_blocks = tile_gkeys[:, 0] + home_keys.reshape(per_device, BLK, width)
    grad_value_blocks = tile_gvalues[:, 0] + home_values.reshape(per_device, BLK, width)
    return (
        attended.reshape(tok_rows, width),
        grad_query.reshape(tok_rows, width),
        grad_key_blocks.astype(jnp.bfloat16).reshape(tok_rows, width),
        grad_value_blocks.astype(jnp.bfloat16).reshape(tok_rows, width),
    )

SLOTS = 3 + G + 3


def _send(v, pairs):
    return lax.ppermute(v.astype(jnp.bfloat16), "seq", pairs).astype(v.dtype)


def gather_blocks(x, n):
    line_len = n // 4
    z = lax.axis_index("seq") // 4
    ups, downs = [], []
    up, down = x, x
    for k in range(1, line_len):
        up = _send(
            up, [(4 * z0 + r, 4 * (z0 + 1) + r) for z0 in range(k - 1, line_len - 1) for r in range(4)]
        )
        down = _send(
            down, [(4 * z0 + r, 4 * (z0 - 1) + r) for z0 in range(1, line_len - k + 1) for r in range(4)]
        )
        ups.append(up)
        downs.append(down)
    rel = jnp.stack(ups[::-1] + [x] + downs)
    line = lax.dynamic_slice_in_dim(rel, line_len - 1 - z, line_len, axis=0)
    other = _send(line, [(i, i ^ 2) for i in range(n)])
    pair = jnp.stack([line, other])
    sibling = _send(pair, [(i, i ^ 1) for i in range(n)])
    return jnp.stack([pair, sibling]), line


HEADS_PER_STEP = 2


def _attend_kernel(pos_ref, q_ref, g_ref, *refs):
    k_refs = refs[:SLOTS]
    v_refs = refs[SLOTS : 2 * SLOTS]
    att_ref, gq_ref, dk_ref, dv_ref, dk_acc, dv_acc = refs[2 * SLOTS :]
    scale = HD ** (-0.5)
    nt = (((1,), (1,)), ((), ()))
    tn = (((0,), (0,)), ((), ()))
    rows = q_ref.shape[0]
    empty = jnp.zeros((rows, dk_acc.shape[-1]), jnp.float32)
    for j in range(SLOTS):
        dk_acc[pos_ref[j]] = empty
        dv_acc[pos_ref[j]] = empty
    for hh in range(q_ref.shape[1] // HD):
        cols = slice(hh * HD, (hh + 1) * HD)
        q = q_ref[:, cols]
        g = g_ref[:, cols]
        k_all = jnp.concatenate([r[:, cols] for r in k_refs], axis=0)
        v_all = jnp.concatenate([r[:, cols] for r in v_refs], axis=0)
        s = lax.dot_general(q, k_all, nt, preferred_element_type=jnp.float32) * scale
        e = jnp.exp(s - jnp.max(s, axis=-1, keepdims=True))
        p = e / jnp.sum(e, axis=-1, keepdims=True)
        w = p.astype(jnp.bfloat16)
        att = jnp.dot(w, v_all, preferred_element_type=jnp.float32).astype(jnp.bfloat16)
        att_ref[:, cols] = att
        delta = jnp.sum(g.astype(jnp.float32) * att.astype(jnp.float32), axis=-1, keepdims=True)
        gp = lax.dot_general(g, v_all, nt, preferred_element_type=jnp.float32)
        gs = (p * (gp - delta)).astype(jnp.bfloat16)
        gq_ref[:, cols] = (jnp.dot(gs, k_all, preferred_element_type=jnp.float32) * scale).astype(
            jnp.bfloat16
        )
        gk = lax.dot_general(gs, q, tn, preferred_element_type=jnp.float32) * scale
        gv = lax.dot_general(w, g, tn, preferred_element_type=jnp.float32)
        for j in range(SLOTS):
            at = pos_ref[j]
            dk_acc[at, :, cols] = dk_acc[at, :, cols] + gk[j * rows : (j + 1) * rows]
            dv_acc[at, :, cols] = dv_acc[at, :, cols] + gv[j * rows : (j + 1) * rows]
    dk_ref[...] = jnp.zeros(dk_ref.shape, dk_ref.dtype)
    dv_ref[...] = jnp.zeros(dv_ref.shape, dv_ref.dtype)
    for j in range(SLOTS):
        at = pos_ref[j]
        dk_ref[at] = dk_acc[at].astype(dk_ref.dtype)
        dv_ref[at] = dv_acc[at].astype(dv_ref.dtype)


def attend_local(pos, query, grad_out, keys_local, values_local):
    rows, width = query.shape
    held = keys_local.shape[0]
    step = HEADS_PER_STEP * HD if (width // HD) % HEADS_PER_STEP == 0 else HD
    heads = width // HD
    head_spec = pl.BlockSpec((rows, step), lambda h, pos: (0, h))
    slot_specs = [
        pl.BlockSpec((None, rows, step), lambda h, pos, j=j: (pos[j], 0, h)) for j in range(SLOTS)
    ]
    part_spec = pl.BlockSpec((held, rows, step), lambda h, pos: (0, 0, h))
    flops = 12 * rows * SLOTS * rows * HD * heads
    moved = 2 * SLOTS * rows * width * 2 + 4 * rows * width * 2 + 2 * held * rows * width * 2
    call = pl.pallas_call(
        _attend_kernel,
        out_shape=(
            jax.ShapeDtypeStruct((rows, width), jnp.bfloat16),
            jax.ShapeDtypeStruct((rows, width), jnp.bfloat16),
            jax.ShapeDtypeStruct((held, rows, width), jnp.bfloat16),
            jax.ShapeDtypeStruct((held, rows, width), jnp.bfloat16),
        ),
        grid_spec=pltpu.PrefetchScalarGridSpec(
            num_scalar_prefetch=1,
            grid=(width // step,),
            in_specs=[head_spec, head_spec] + slot_specs + slot_specs,
            out_specs=(head_spec, head_spec, part_spec, part_spec),
            scratch_shapes=[pltpu.VMEM((held, rows, step), jnp.float32)] * 2,
        ),
        compiler_params=pltpu.CompilerParams(dimension_semantics=("arbitrary",)),
        cost_estimate=pl.CostEstimate(
            flops=flops, transcendentals=rows * SLOTS * rows * heads, bytes_accessed=moved
        ),
    )
    return call(
        pos, query, grad_out, *([keys_local] * SLOTS), *([values_local] * SLOTS)
    )


STREAMS = 3


def _stream(pos, query, grad_out, keys, values, after=None):
    n = lax.axis_size("seq")
    rows, width = query.shape
    line_len = n // 4
    if after is not None:
        keys, values, _ = lax.optimization_barrier((keys, values, after))
    keys_local, keys_line = gather_blocks(keys, n)
    values_local, values_line = gather_blocks(values, n)
    keys_local = keys_local.reshape(n, rows, width)
    values_local = values_local.reshape(n, rows, width)
    attended, grad_query, part_keys, part_values = attend_local(
        pos, query, grad_out, keys_local, values_local
    )
    scatter = jax.linear_transpose(
        lambda t: gather_blocks(t, n)[0], jax.ShapeDtypeStruct((rows, width), jnp.float32)
    )
    (grad_keys,) = scatter(part_keys.astype(jnp.float32).reshape(2, 2, line_len, rows, width))
    (grad_values,) = scatter(part_values.astype(jnp.float32).reshape(2, 2, line_len, rows, width))
    outs = (attended, grad_query, grad_keys.astype(jnp.bfloat16), grad_values.astype(jnp.bfloat16))
    return outs, (keys_line, values_line)


def shards_gather(query, keys, values, grad_out, global_blocks, random_blocks):
    n = lax.axis_size("seq")
    rows, width = query.shape
    line_len = n // 4
    idx = lax.axis_index("seq")
    listed = jnp.concatenate(
        [
            jnp.stack([idx, (idx - 1) % n, (idx + 1) % n]).astype(jnp.int32),
            global_blocks.astype(jnp.int32),
            random_blocks[idx].astype(jnp.int32),
        ]
    )
    listed = jnp.clip(listed, 0, n - 1)
    core = idx % 2
    ypos = (idx // 2) % 2
    pos = (((listed % 2) ^ core) * 2 + (((listed // 2) % 2) ^ ypos)) * line_len + listed // 4
    heads = width // HD
    shares = [heads // STREAMS + (1 if s < heads % STREAMS else 0) for s in range(STREAMS)]
    edges = [sum(shares[:s]) * HD for s in range(STREAMS + 1)]
    outs = []
    after = None
    for s in range(STREAMS):
        cols = slice(edges[s], edges[s + 1])
        with jax.named_scope(f"stream{s}"):
            out, after = _stream(
                pos, query[:, cols], grad_out[:, cols], keys[:, cols], values[:, cols], after
            )
            outs.append(out)
    return tuple(jnp.concatenate(parts, axis=1) for parts in zip(*outs))


def shards(query, keys, values, grad_out, global_blocks, random_blocks):
    n = lax.axis_size("seq")
    if query.shape[0] == BLK and n % 4 == 0 and n <= 32:
        return shards_gather(query, keys, values, grad_out, global_blocks, random_blocks)
    return shards_exchange(query, keys, values, grad_out, global_blocks, random_blocks)


def solution(mesh):
    placed = (
        P(("groups", "seq"), None),
        P(("groups", "seq"), None),
        P(("groups", "seq"), None),
        P(("groups", "seq"), None),
        P("groups"),
        P("groups", None),
    )
    return jax.shard_map(
        shards,
        mesh=mesh,
        in_specs=placed,
        out_specs=(
            P(("groups", "seq"), None),
            P(("groups", "seq"), None),
            P(("groups", "seq"), None),
            P(("groups", "seq"), None),
        ),
        check_vma=False,
    )
```
